32 devices in a mesh: group: 2 (over y), seq: 16 (over z, x, core).
Axes of the slice: x: 2, y: 2, z: 4, core: 2. Of those that a mesh axis runs over, the one named last changes fastest.
Arguments:
- queries: bfloat16 [4096, 1536], P(('group', 'seq')), parts along dimension 0, may hold values from -160 to 160
- keys: bfloat16 [4096, 1536], P(('group', 'seq')), parts along dimension 0, may hold values from -4 to 4
- values: bfloat16 [4096, 1536], P(('group', 'seq')), parts along dimension 0, may hold values from -6 to 6
- out_grad: bfloat16 [4096, 1536], P(('group', 'seq')), parts along dimension 0, may hold values from -24 to 24
- query_feats: bfloat16 [4096, 1536], P(('group', 'seq')), parts along dimension 0, may hold values from 0.0019989014 to 0.029907227
- key_feats: bfloat16 [4096, 1536], P(('group', 'seq')), parts along dimension 0, may hold values from 0.0019989014 to 0.029907227
- segment_ids: int32 [4096], P(('group', 'seq')), parts along dimension 0, may hold values from 0 to 3, never falling along the last dimension, each value on 1 to 1024 neighbouring positions
- windows: int32 [24], P('group'), parts along dimension 0, may hold values from 32 to 64, as said below
Outputs:
- query_grad: bfloat16 [4096, 1536], P(('group', 'seq')), parts along dimension 0
- key_grad: bfloat16 [4096, 1536], P(('group', 'seq')), parts along dimension 0
- value_grad: bfloat16 [4096, 1536], P(('group', 'seq')), parts along dimension 0
- query_feat_grad: bfloat16 [4096, 1536], P(('group', 'seq')), parts along dimension 0
- key_feat_grad: bfloat16 [4096, 1536], P(('group', 'seq')), parts along dimension 0
The draws below stay inside these ranges and needn't reach their ends.
There are 2 independent parts, one for each index of `group`. The reference program is written for one: setup_inputs(seed, part) draws one part's arguments, and reference() takes and returns one part's arrays. A program takes and returns all parts, laid end to end along the dimension named above; each array names one. Nothing has to cross between parts.
Inputs may be any that keep to these rules, and one draw needn't show every extreme that they name: `windows`: one head's window is exactly 64.
All inputs are finite; a program needn't handle non-finite values.
Results may differ from the reference program's by a relative error of at most 0.012.
Values may be sent and summed in bfloat16 or wider, within the bound.
No kernel may reach another device: no remote copies, remote signals or barrier semaphores. Data moves between devices by JAX's collectives and lax.ppermute only.
A program may use at most 384 MiB of HBM per device.

```python
import math
import jax
import jax.numpy as jnp
import numpy as np
from jax import lax

HEADS = 12
HEAD_DIM = 128
FEAT = 128
WMAX = 64
SEGS = 4
TOK_DEV = 128
TOKENS = 2048


def shared_pairs(key):
    base = jax.random.fold_in(key, 17)
    key_q, key_k = jax.random.split(base, 2)
    width = HEADS * HEAD_DIM
    query_vals = jnp.clip(jax.random.normal(key_q, (TOKENS, width), jnp.float32), -4.0, 4.0)
    key_vals = jnp.clip(jax.random.normal(key_k, (TOKENS, width), jnp.float32), -4.0, 4.0)
    return (query_vals, key_vals)


def draw_queries(key, part):
    return shared_pairs(key)[0].astype(jnp.bfloat16)


def draw_keys(key, part):
    return shared_pairs(key)[1].astype(jnp.bfloat16)


def draw_windows(key, part):
    key_w, key_p = jax.random.split(jax.random.fold_in(key, 5))
    widths = jax.random.randint(key_w, (HEADS,), WMAX // 2, WMAX + 1, dtype=jnp.int32)
    longest = jax.random.randint(key_p, (), 0, HEADS, dtype=jnp.int32)
    return jnp.where(jnp.arange(HEADS, dtype=jnp.int32) == longest, WMAX, widths).astype(jnp.int32)


def level_of(key, dims, cuts, least, top_value):
    def one(axis_at, parts):
        heights = jax.random.uniform(jax.random.fold_in(jax.random.fold_in(key, 6), axis_at), (parts,), jnp.float32, least / len(cuts), top_value / len(cuts))
        return jnp.repeat(jnp.exp(heights), dims[axis_at] // parts).reshape((-1,) + (1,) * (len(dims) - axis_at - 1))

    gain = one(*cuts[0])
    for cut in cuts[1:]:
        gain = gain * one(*cut)
    return gain


def split_up(amount, total, most, slope):
    portions = [(1 << 20) // math.isqrt(rank ** slope) + 1 for rank in range(2, amount + 1)]
    surplus, given = total - most - (amount - 1), [1] * (amount - 1)
    while surplus > 0:
        free = [i for i in range(amount - 1) if given[i] < most]
        whole, remaining = sum([portions[i] for i in free]), surplus
        for i in free:
            addition = min(most - given[i], max(1, remaining * portions[i] // whole), surplus)
            given[i] = given[i] + addition
            surplus = surplus - addition
    return np.array([most] + given)


def uneven_parts(key, count, total, reach, skew):
    if count == 2:
        one = jax.random.randint(key, (), max(1, total - reach), min(reach, total - 1) + 1)
        return jnp.stack([one, total - one])
    sizes = jnp.asarray(split_up(count, total, reach, skew), jnp.int32)
    couples = (count - 1) // 2
    donor, receiver = sizes[1:1 + 2 * couples:2], sizes[2:2 + 2 * couples:2]
    room = jnp.minimum(donor - 1, reach - receiver)
    moved = jax.random.randint(jax.random.fold_in(key, 1), (couples,), 0, 1 << 20) % (room + 1)
    sizes = sizes.at[1:1 + 2 * couples:2].set(donor - moved).at[2:2 + 2 * couples:2].set(receiver + moved)
    return sizes[jax.random.permutation(jax.random.fold_in(key, 2), count)]


def bell_draw(rng, dims, scale, limit, cuts=(), kind=jnp.bfloat16):
    result = scale * jax.random.normal(rng, dims, jnp.float32)
    if cuts:
        result = result * level_of(rng, dims, cuts, -0.22, 0.18)
    return jnp.clip(result, -limit, limit).astype(kind)


def setup_inputs(seed: int = 0, part: int = 0) -> dict:
    key_of = jax.random.split(jax.random.key(seed), 9)
    own_keys = jax.random.split(jax.random.fold_in(key_of[8], part), 9)
    queries = draw_queries(jax.random.fold_in(jax.random.fold_in(key_of[8], part), 71), part)
    keys = draw_keys(jax.random.fold_in(jax.random.fold_in(key_of[8], part), 71), part)
    values = bell_draw(own_keys[2], (TOKENS, HEADS * HEAD_DIM), 1.0, 6.0, ((0, 16),))
    out_grad = bell_draw(own_keys[3], (TOKENS, HEADS * HEAD_DIM), 4.0, 24.0, ((0, 16),))
    query_feats = jnp.clip(jnp.exp(math.log(0.029907227) - 2.7055024 * jax.random.uniform(own_keys[4], (TOKENS, HEADS * FEAT), jnp.float32) ** level_of(own_keys[4], (TOKENS, HEADS * FEAT), ((0, 16),), -0.2, 0.2)), 0.0019989014, 0.029907227).astype(jnp.bfloat16)
    key_feats = jnp.clip(jnp.exp(math.log(0.029907227) - 2.7055024 * jax.random.uniform(own_keys[5], (TOKENS, HEADS * FEAT), jnp.float32) ** level_of(own_keys[5], (TOKENS, HEADS * FEAT), ((0, 16),), -0.2, 0.2)), 0.0019989014, 0.029907227).astype(jnp.bfloat16)
    segment_ids = jnp.searchsorted(jnp.cumsum(uneven_parts(own_keys[6], SEGS, TOKENS, TOKENS // 2, 0)), jnp.arange(TOKENS), side="right").astype(jnp.int32)
    windows = draw_windows(jax.random.fold_in(jax.random.fold_in(key_of[8], part), 71), part)
    return dict(queries=queries, keys=keys, values=values, out_grad=out_grad, query_feats=query_feats, key_feats=key_feats, segment_ids=segment_ids, windows=windows)


def quick_product(form, left, right):
    return jnp.einsum(form, left.astype(jnp.float32), right.astype(jnp.float32))

def exact_product(form, left, right):
    return jnp.einsum(form, left.astype(jnp.float32), right.astype(jnp.float32), precision=lax.Precision.HIGHEST)

def pair_masks(labels_q, labels_k, windows, offset):
    distance = jnp.arange(labels_q.shape[0], dtype=jnp.int32)[:, None] + offset - jnp.arange(labels_k.shape[0], dtype=jnp.int32)[None, :]
    matched = (labels_q[:, None] == labels_k[None, :]) & (labels_q[:, None] > 0) & (distance >= 0)
    inside = matched[None] & (distance[None] < windows[:, None, None])
    is_local = (jnp.arange(labels_k.shape[0], dtype=jnp.int32) >= offset)[None, None, :]
    far_sign = jnp.where(is_local, (matched[None] & ~inside).astype(jnp.float32), -inside.astype(jnp.float32))
    return (inside, far_sign)

def pair_scores(query_rows, query_feat, key_ext, feat_ext, labels_q, labels_k, windows, offset):
    inside, far_sign = pair_masks(labels_q, labels_k, windows, offset)
    scale = 1.0 / math.sqrt(query_rows.shape[2])
    score = quick_product('thd,ehd->hte', query_rows, key_ext) * scale
    kernel = quick_product('thf,ehf->hte', query_feat, feat_ext) * far_sign
    return (inside, far_sign, score, kernel)

def pair_grads(probability, kernel, far_sign, ratios, deltas, grad_rows, value_ext):
    weight_grad = quick_product('thd,ehd->hte', grad_rows, value_ext) - deltas[:, :, None]
    score_grad = (probability * weight_grad).astype(jnp.bfloat16)
    kernel_grad = weight_grad * ratios[:, :, None] * far_sign
    return (score_grad, kernel_grad, kernel * ratios[:, :, None])

def key_side(query_rows, query_feat, grad_rows, weight_low, score_grad, kernel_grad, kernel_scaled):
    scale = 1.0 / math.sqrt(query_rows.shape[2])
    key_grad = quick_product('hte,thd->ehd', score_grad, query_rows) * scale
    value_grad = quick_product('hte,thd->ehd', weight_low, grad_rows) + exact_product('hte,thd->ehd', kernel_scaled, grad_rows)
    kfeat_grad = exact_product('hte,thf->ehf', kernel_grad, query_feat)
    return (key_grad, value_grad, kfeat_grad)

def forward_block(query_rows, query_feat, grad_rows, key_ext, value_ext, feat_ext, labels_q, labels_k, windows, carry):
    carry_state, carry_sum, carry_mark = carry
    offset = key_ext.shape[0] - query_rows.shape[0]
    scale = 1.0 / math.sqrt(query_rows.shape[2])
    inside, far_sign, score, kernel = pair_scores(query_rows, query_feat, key_ext, feat_ext, labels_q, labels_k, windows, offset)
    maxima = lax.optimization_barrier(jnp.max(jnp.where(inside, score, -jnp.inf), axis=2))
    shrink = jnp.exp(-maxima)
    carry_on = (labels_q == carry_mark).astype(jnp.float32)
    carry_den = exact_product('thf,hf->ht', query_feat, carry_sum) * carry_on[None, :]
    carry_num = exact_product('thf,hfd->htd', query_feat, carry_state) * carry_on[None, :, None]
    powered = jnp.where(inside, jnp.exp(score - maxima[:, :, None]), 0.0)
    denominator = lax.optimization_barrier(jnp.sum(powered, axis=2)) + shrink * (lax.optimization_barrier(jnp.sum(kernel, axis=2)) + carry_den)
    ratios = shrink / denominator
    probability = powered / denominator[:, :, None]
    weight_low = probability.astype(jnp.bfloat16)
    attended = quick_product('hte,ehd->htd', weight_low, value_ext) + ratios[:, :, None] * (exact_product('hte,ehd->htd', kernel, value_ext) + carry_num)
    grad_wide = grad_rows.astype(jnp.float32)
    deltas = lax.optimization_barrier(jnp.sum(jnp.transpose(grad_wide, (1, 0, 2)) * attended, axis=2))
    score_grad, kernel_grad, kernel_scaled = pair_grads(probability, kernel, far_sign, ratios, deltas, grad_rows, value_ext)
    query_grad = quick_product('hte,ehd->thd', score_grad, key_ext) * scale
    carry_term = exact_product('hfd,thd->thf', carry_state, grad_rows) - deltas.T[:, :, None] * carry_sum[None]
    feat_grad = exact_product('hte,ehf->thf', kernel_grad, feat_ext) + (carry_on[:, None] * ratios.T)[:, :, None] * carry_term
    return (query_grad, feat_grad, maxima, denominator, deltas, ratios, (weight_low, score_grad, kernel_grad, kernel_scaled))

def recompute_terms(query_rows, query_feat, grad_rows, key_ext, value_ext, feat_ext, labels_q, labels_k, windows, offset, maxima, denominator, deltas):
    inside, far_sign, score, kernel = pair_scores(query_rows, query_feat, key_ext, feat_ext, labels_q, labels_k, windows, offset)
    powered = jnp.where(inside, jnp.exp(score - maxima[:, :, None]), 0.0)
    probability = powered / denominator[:, :, None]
    ratios = jnp.exp(-maxima) / denominator
    score_grad, kernel_grad, kernel_scaled = pair_grads(probability, kernel, far_sign, ratios, deltas, grad_rows, value_ext)
    return (key_side(query_rows, query_feat, grad_rows, probability.astype(jnp.bfloat16), score_grad, kernel_grad, kernel_scaled), ratios)

def key_summary(key_feat, value_rows, labels):
    keep = labels == labels[-1]
    state = quick_product('thf,thd->hfd', key_feat * keep.astype(jnp.bfloat16)[:, None, None], value_rows)
    total = lax.optimization_barrier(jnp.sum(key_feat.astype(jnp.float32) * keep.astype(jnp.float32)[:, None, None], axis=0))
    return (state, total, labels[-1])

def query_summary(query_feat, grad_rows, labels, ratios, deltas):
    use = (labels == labels[0]).astype(jnp.float32)[:, None] * ratios.T
    weighted = query_feat.astype(jnp.float32) * use[:, :, None]
    state = exact_product('thf,thd->hfd', weighted, grad_rows)
    total = lax.optimization_barrier(jnp.sum(weighted * deltas.T[:, :, None], axis=0))
    return (state, total, labels[0])

def combine_pair(earlier, later):
    keep = ((earlier[2] == later[2]) | (later[2] == 0)).astype(jnp.float32)
    state = later[0] + keep.reshape(keep.shape + (1, 1, 1)) * earlier[0]
    total = later[1] + keep.reshape(keep.shape + (1, 1)) * earlier[1]
    mark = jnp.where(later[2] == 0, earlier[2], later[2])
    return (state, total, mark)

def apply_reverse(value_grad, kfeat_grad, key_feat, value_rows, labels, summary):
    state, total, mark = summary
    use = (labels == mark).astype(jnp.float32)[:, None, None]
    value_grad = value_grad + use * exact_product('hfd,thf->thd', state, key_feat)
    kfeat_grad = kfeat_grad + use * (exact_product('hfd,thd->thf', state, value_rows) - total[None])
    return (value_grad, kfeat_grad)

def reference(queries, keys, values, out_grad, query_feats, key_feats, segment_ids, windows):
    heads = windows.shape[0]
    length = queries.shape[0]
    head_dim = queries.shape[1] // heads
    feat = query_feats.shape[1] // heads
    blocks = length // TOK_DEV
    span = TOK_DEV + WMAX
    tail = TOK_DEV - WMAX

    def padded(array, width):
        return jnp.concatenate([jnp.zeros((WMAX, heads, width), array.dtype), array.reshape(length, heads, width)], axis=0)
    labels = (segment_ids + 1).astype(jnp.int32)
    label_pad = jnp.concatenate([jnp.zeros((WMAX,), jnp.int32), labels]).astype(jnp.int32)
    key_pad = padded(keys, head_dim)
    value_pad = padded(values, head_dim)
    feat_pad = padded(key_feats, feat)
    query_blocks = queries.reshape(blocks, TOK_DEV, heads, head_dim)
    grad_blocks = out_grad.reshape(blocks, TOK_DEV, heads, head_dim)
    qfeature_blocks = query_feats.reshape(blocks, TOK_DEV, heads, feat)
    label_blocks = labels.reshape(blocks, TOK_DEV)
    index = jnp.arange(blocks, dtype=jnp.int32)

    def extend(block):
        start = (block * TOK_DEV).astype(jnp.int32)
        return (lax.dynamic_slice_in_dim(key_pad, start, span, 0), lax.dynamic_slice_in_dim(value_pad, start, span, 0), lax.dynamic_slice_in_dim(feat_pad, start, span, 0), lax.dynamic_slice_in_dim(label_pad, start, span, 0))
    zero_state = (jnp.zeros((heads, feat, head_dim), jnp.float32), jnp.zeros((heads, feat), jnp.float32), jnp.int32(0))

    def forward_step(carry, inputs):
        block, query_rows, grad_rows, query_feat, labels_q = inputs
        key_ext, value_ext, feat_ext, label_ext = extend(block)
        query_grad, feat_grad, maxima, denominator, deltas, ratios, unused = forward_block(query_rows, query_feat, grad_rows, key_ext, value_ext, feat_ext, labels_q, label_ext, windows, carry)
        own = key_summary(feat_ext[WMAX:], value_ext[WMAX:], label_ext[WMAX:])
        return (combine_pair(carry, own), (query_grad.astype(jnp.bfloat16), feat_grad.astype(jnp.bfloat16), maxima, denominator, deltas))
    unused_carry, results = lax.scan(forward_step, zero_state, (index, query_blocks, grad_blocks, qfeature_blocks, label_blocks))
    query_grads, qfeat_grads, maxima_all, denominator_all, deltas_all = results
    zero_rim = (jnp.zeros((WMAX, heads, head_dim), jnp.float32), jnp.zeros((WMAX, heads, head_dim), jnp.float32), jnp.zeros((WMAX, heads, feat), jnp.float32))

    def reverse_step(carry, inputs):
        summary, rim = carry
        block, query_rows, grad_rows, query_feat, labels_q, maxima, denominator, deltas = inputs
        key_ext, value_ext, feat_ext, label_ext = extend(block)
        grads, ratios = recompute_terms(query_rows, query_feat, grad_rows, key_ext, value_ext, feat_ext, labels_q, label_ext, windows, WMAX, maxima, denominator, deltas)
        key_full, value_full, kfeat_full = grads
        key_grad = jnp.concatenate([key_full[WMAX:WMAX + tail], key_full[WMAX + tail:] + rim[0]], axis=0)
        value_grad = jnp.concatenate([value_full[WMAX:WMAX + tail], value_full[WMAX + tail:] + rim[1]], axis=0)
        kfeat_grad = jnp.concatenate([kfeat_full[WMAX:WMAX + tail], kfeat_full[WMAX + tail:] + rim[2]], axis=0)
        value_grad, kfeat_grad = apply_reverse(value_grad, kfeat_grad, feat_ext[WMAX:], value_ext[WMAX:], labels_q, summary)
        own = query_summary(query_feat, grad_rows, labels_q, ratios, deltas)
        new_summary = combine_pair(summary, own)
        new_rim = (key_full[:WMAX], value_full[:WMAX], kfeat_full[:WMAX])
        return ((new_summary, new_rim), (key_grad.astype(jnp.bfloat16), value_grad.astype(jnp.bfloat16), kfeat_grad.astype(jnp.bfloat16)))
    unused_back, back = lax.scan(reverse_step, (zero_state, zero_rim), (index, query_blocks, grad_blocks, qfeature_blocks, label_blocks, maxima_all, denominator_all, deltas_all), reverse=True)
    key_grads, value_grads, kfeat_grads = back
    return (query_grads.reshape(length, heads * head_dim), key_grads.reshape(length, heads * head_dim), value_grads.reshape(length, heads * head_dim), qfeat_grads.reshape(length, heads * feat), kfeat_grads.reshape(length, heads * feat))
```

```python
import math

import jax
import jax.numpy as jnp
from jax import lax
from jax.sharding import PartitionSpec as P

WMAX = 64


def passed_along(value, axis, steps):
    count = lax.axis_size(axis)
    leading, last = (max(0, -steps), min(count, count - steps))
    return lax.ppermute(value, axis, [(source, source + steps) for source in range(leading, last)])


def carried_in(value, axis, join, reach, backward):
    step = -1 if backward else 1
    nearest = passed_along(value, axis, step)
    if reach < 2:
        return nearest
    total = join(passed_along(value, axis, 2 * step), nearest)
    length = 2
    while length < reach:
        total = join(passed_along(total, axis, length * step), total)
        length *= 2
    return total


def quick_product(form, left, right):
    return jnp.einsum(form, left, right, preferred_element_type=jnp.float32)


def exact_product(form, left, right):
    return jnp.einsum(
        form,
        left.astype(jnp.float32),
        right.astype(jnp.float32),
        precision=lax.Precision.HIGHEST,
        preferred_element_type=jnp.float32,
    )


def pair_masks(labels_q, labels_k, windows, offset):
    distance = (
        jnp.arange(labels_q.shape[0], dtype=jnp.int32)[:, None]
        + offset
        - jnp.arange(labels_k.shape[0], dtype=jnp.int32)[None, :]
    )
    matched = (labels_q[:, None] == labels_k[None, :]) & (labels_q[:, None] > 0) & (distance >= 0)
    inside = matched[None] & (distance[None] < windows[:, None, None])
    is_local = (jnp.arange(labels_k.shape[0], dtype=jnp.int32) >= offset)[None, None, :]
    far_sign = jnp.where(
        is_local, (matched[None] & ~inside).astype(jnp.float32), -inside.astype(jnp.float32)
    )
    return (inside, far_sign)


def pair_scores(query_rows, query_feat, key_ext, feat_ext, labels_q, labels_k, windows, offset):
    inside, far_sign = pair_masks(labels_q, labels_k, windows, offset)
    scale = 1.0 / math.sqrt(query_rows.shape[2])
    score = quick_product("thd,ehd->hte", query_rows, key_ext) * scale
    kernel = quick_product("thf,ehf->hte", query_feat, feat_ext) * far_sign
    return (inside, far_sign, score, kernel)


def pair_grads(probability, kernel, far_sign, ratios, deltas, grad_rows, value_ext):
    weight_grad = quick_product("thd,ehd->hte", grad_rows, value_ext) - deltas[:, :, None]
    score_grad = (probability * weight_grad).astype(jnp.bfloat16)
    kernel_grad = weight_grad * ratios[:, :, None] * far_sign
    return (score_grad, kernel_grad, kernel * ratios[:, :, None])


def key_side(query_rows, query_feat, grad_rows, weight_low, score_grad, kernel_grad, kernel_scaled):
    scale = 1.0 / math.sqrt(query_rows.shape[2])
    key_grad = quick_product("hte,thd->ehd", score_grad, query_rows) * scale
    value_grad = quick_product("hte,thd->ehd", weight_low, grad_rows) + exact_product(
        "hte,thd->ehd", kernel_scaled, grad_rows
    )
    kfeat_grad = exact_product("hte,thf->ehf", kernel_grad, query_feat)
    return (key_grad, value_grad, kfeat_grad)


def forward_block(
    query_rows,
    query_feat,
    grad_rows,
    key_ext,
    value_ext,
    feat_ext,
    labels_q,
    labels_k,
    windows,
    carry,
):
    carry_state, carry_sum, carry_mark = carry
    offset = key_ext.shape[0] - query_rows.shape[0]
    scale = 1.0 / math.sqrt(query_rows.shape[2])
    inside, far_sign, score, kernel = pair_scores(
        query_rows, query_feat, key_ext, feat_ext, labels_q, labels_k, windows, offset
    )
    maxima = jnp.max(jnp.where(inside, score, -jnp.inf), axis=2)
    shrink = jnp.exp(-maxima)
    carry_on = (labels_q == carry_mark).astype(jnp.float32)
    carry_den = exact_product("thf,hf->ht", query_feat, carry_sum) * carry_on[None, :]
    carry_num = exact_product("thf,hfd->htd", query_feat, carry_state) * carry_on[None, :, None]
    powered = jnp.where(inside, jnp.exp(score - maxima[:, :, None]), 0.0)
    denominator = jnp.sum(powered, axis=2) + shrink * (jnp.sum(kernel, axis=2) + carry_den)
    ratios = shrink / denominator
    probability = powered / denominator[:, :, None]
    weight_low = probability.astype(jnp.bfloat16)
    attended = quick_product("hte,ehd->htd", weight_low, value_ext) + ratios[:, :, None] * (
        exact_product("hte,ehd->htd", kernel, value_ext) + carry_num
    )
    grad_wide = grad_rows.astype(jnp.float32)
    deltas = jnp.sum(jnp.transpose(grad_wide, (1, 0, 2)) * attended, axis=2)
    score_grad, kernel_grad, kernel_scaled = pair_grads(
        probability, kernel, far_sign, ratios, deltas, grad_rows, value_ext
    )
    query_grad = quick_product("hte,ehd->thd", score_grad, key_ext) * scale
    carry_term = (
        exact_product("hfd,thd->thf", carry_state, grad_rows)
        - deltas.T[:, :, None] * carry_sum[None]
    )
    feat_grad = (
        exact_product("hte,ehf->thf", kernel_grad, feat_ext)
        + (carry_on[:, None] * ratios.T)[:, :, None] * carry_term
    )
    return (
        query_grad,
        feat_grad,
        maxima,
        denominator,
        deltas,
        ratios,
        (weight_low, score_grad, kernel_grad, kernel_scaled),
    )


def key_summary(key_feat, value_rows, labels):
    keep = labels == labels[-1]
    state = quick_product(
        "thf,thd->hfd", key_feat * keep.astype(jnp.bfloat16)[:, None, None], value_rows
    )
    total = jnp.sum(key_feat.astype(jnp.float32) * keep.astype(jnp.float32)[:, None, None], axis=0)
    return (state, total, labels[-1])


def query_summary(query_feat, grad_rows, labels, ratios, deltas):
    use = (labels == labels[0]).astype(jnp.float32)[:, None] * ratios.T
    weighted = query_feat.astype(jnp.float32) * use[:, :, None]
    state = exact_product("thf,thd->hfd", weighted, grad_rows)
    total = jnp.sum(weighted * deltas.T[:, :, None], axis=0)
    return (state, total, labels[0])


def combine_pair(earlier, later):
    keep = ((earlier[2] == later[2]) | (later[2] == 0)).astype(jnp.float32)
    state = later[0] + keep.reshape(keep.shape + (1, 1, 1)) * earlier[0]
    total = later[1] + keep.reshape(keep.shape + (1, 1)) * earlier[1]
    mark = jnp.where(later[2] == 0, earlier[2], later[2])
    return (state, total, mark)


def apply_reverse(value_grad, kfeat_grad, key_feat, value_rows, labels, summary):
    state, total, mark = summary
    use = (labels == mark).astype(jnp.float32)[:, None, None]
    value_grad = value_grad + use * exact_product("hfd,thf->thd", state, key_feat)
    kfeat_grad = kfeat_grad + use * (exact_product("hfd,thd->thf", state, value_rows) - total[None])
    return (value_grad, kfeat_grad)


def per_device(queries, keys, values, out_grad, query_feats, key_feats, segment_ids, windows):
    rows = queries.shape[0]
    heads = windows.shape[0]
    head_dim = queries.shape[1] // heads
    feat = query_feats.shape[1] // heads
    tail = rows - WMAX
    query_rows = queries.reshape(rows, heads, head_dim)
    key_rows = keys.reshape(rows, heads, head_dim)
    value_rows = values.reshape(rows, heads, head_dim)
    grad_rows = out_grad.reshape(rows, heads, head_dim)
    query_feat = query_feats.reshape(rows, heads, feat)
    key_feat = key_feats.reshape(rows, heads, feat)
    labels = segment_ids + 1
    halo_key, halo_value, halo_feat, halo_label = passed_along(
        (key_rows[tail:], value_rows[tail:], key_feat[tail:], labels[tail:]), "seq", 1
    )
    zero_state = (
        jnp.zeros((heads, feat, head_dim), jnp.float32),
        jnp.zeros((heads, feat), jnp.float32),
        jnp.int32(0),
    )
    count = lax.axis_size("seq")
    longest = count * rows // 2
    reach = min(count - 1, (longest + rows - 2) // rows)
    carry = carried_in(
        key_summary(key_feat, value_rows, labels), "seq", combine_pair, reach, False
    )
    key_ext = jnp.concatenate([halo_key, key_rows], axis=0)
    value_ext = jnp.concatenate([halo_value, value_rows], axis=0)
    feat_ext = jnp.concatenate([halo_feat, key_feat], axis=0)
    label_ext = jnp.concatenate([halo_label, labels], axis=0)
    query_grad, feat_grad, maxima, denominator, deltas, ratios, pieces = forward_block(
        query_rows,
        query_feat,
        grad_rows,
        key_ext,
        value_ext,
        feat_ext,
        labels,
        label_ext,
        windows,
        carry,
    )
    summary = carried_in(
        query_summary(query_feat, grad_rows, labels, ratios, deltas),
        "seq",
        combine_pair,
        reach,
        True,
    )
    weight_low, score_grad, kernel_grad, kernel_scaled = pieces
    key_full, value_full, kfeat_full = key_side(
        query_rows, query_feat, grad_rows, weight_low, score_grad, kernel_grad, kernel_scaled
    )
    back_key, back_value, back_feat = (
        passed_along(key_full[:WMAX].astype(jnp.bfloat16), "seq", -1).astype(jnp.float32),
        passed_along(value_full[:WMAX].astype(jnp.bfloat16), "seq", -1).astype(jnp.float32),
        passed_along(kfeat_full[:WMAX].astype(jnp.bfloat16), "seq", -1).astype(jnp.float32),
    )
    key_grad = key_full[WMAX:]
    value_grad = value_full[WMAX:]
    kfeat_grad = kfeat_full[WMAX:]
    key_grad = jnp.concatenate([key_grad[:tail], key_grad[tail:] + back_key], axis=0)
    value_grad = jnp.concatenate([value_grad[:tail], value_grad[tail:] + back_value], axis=0)
    kfeat_grad = jnp.concatenate([kfeat_grad[:tail], kfeat_grad[tail:] + back_feat], axis=0)
    value_grad, kfeat_grad = apply_reverse(
        value_grad, kfeat_grad, key_feat, value_rows, labels, summary
    )
    return (
        query_grad.reshape(rows, heads * head_dim).astype(jnp.bfloat16),
        key_grad.reshape(rows, heads * head_dim).astype(jnp.bfloat16),
        value_grad.reshape(rows, heads * head_dim).astype(jnp.bfloat16),
        feat_grad.reshape(rows, heads * feat).astype(jnp.bfloat16),
        kfeat_grad.reshape(rows, heads * feat).astype(jnp.bfloat16),
    )


def solution(mesh):
    in_specs = (
        P(("group", "seq"), None),
        P(("group", "seq"), None),
        P(("group", "seq"), None),
        P(("group", "seq"), None),
        P(("group", "seq"), None),
        P(("group", "seq"), None),
        P(("group", "seq")),
        P("group"),
    )
    out_specs = (
        P(("group", "seq"), None),
        P(("group", "seq"), None),
        P(("group", "seq"), None),
        P(("group", "seq"), None),
        P(("group", "seq"), None),
    )
    return jax.shard_map(
        per_device, mesh=mesh, in_specs=in_specs, out_specs=out_specs, check_vma=False
    )
```

```python
import math

import jax
import jax.numpy as jnp
from jax import lax
from jax.sharding import PartitionSpec as P

WMAX = 64


def passed_along(value, axis, steps):
    count = lax.axis_size(axis)
    leading, last = (max(0, -steps), min(count, count - steps))
    return lax.ppermute(value, axis, [(source, source + steps) for source in range(leading, last)])


def packed(summary):
    state, total, mark = summary
    heads, feat, width = state.shape
    rows = [state.reshape(heads * feat, width), total, jnp.full((1, width), mark, jnp.float32)]
    return jnp.concatenate(rows, axis=0)


def unpacked(payload, heads, feat):
    width = payload.shape[1]
    state = payload[: heads * feat].reshape(heads, feat, width)
    total = payload[heads * feat : heads * feat + heads]
    mark = payload[heads * feat + heads, 0].astype(jnp.int32)
    return (state, total, mark)


def join_packed(earlier, later):
    at = later.shape[0] - 1
    mark_e, mark_l = (earlier[at, 0], later[at, 0])
    keep = ((mark_e == mark_l) | (mark_l == 0)).astype(jnp.float32)
    mark = jnp.where(mark_l == 0, mark_e, mark_l)
    row = lax.broadcasted_iota(jnp.int32, later.shape, 0)
    return jnp.where(row == at, mark, later + keep * earlier)


def carried_in(value, axis, reach, backward):
    step = -1 if backward else 1
    nearest = passed_along(value, axis, step)
    if reach < 2:
        return nearest
    total = join_packed(passed_along(value, axis, 2 * step), nearest)
    length = 2
    while length < reach:
        total = join_packed(passed_along(total, axis, length * step), total)
        length *= 2
    return total


def quick_product(form, left, right):
    return jnp.einsum(form, left, right, preferred_element_type=jnp.float32)


def exact_product(form, left, right):
    return jnp.einsum(
        form,
        left.astype(jnp.float32),
        right.astype(jnp.float32),
        precision=lax.Precision.HIGHEST,
        preferred_element_type=jnp.float32,
    )


def pair_masks(labels_q, labels_k, windows, offset):
    distance = (
        jnp.arange(labels_q.shape[0], dtype=jnp.int32)[:, None]
        + offset
        - jnp.arange(labels_k.shape[0], dtype=jnp.int32)[None, :]
    )
    matched = (labels_q[:, None] == labels_k[None, :]) & (labels_q[:, None] > 0) & (distance >= 0)
    inside = matched[None] & (distance[None] < windows[:, None, None])
    is_local = (jnp.arange(labels_k.shape[0], dtype=jnp.int32) >= offset)[None, None, :]
    far_sign = jnp.where(
        is_local, (matched[None] & ~inside).astype(jnp.float32), -inside.astype(jnp.float32)
    )
    return (inside, far_sign)


def pair_scores(query_rows, query_feat, key_ext, feat_ext, labels_q, labels_k, windows, offset):
    inside, far_sign = pair_masks(labels_q, labels_k, windows, offset)
    scale = 1.0 / math.sqrt(query_rows.shape[2])
    score = quick_product("thd,ehd->hte", query_rows, key_ext) * scale
    kernel = quick_product("thf,ehf->hte", query_feat, feat_ext) * far_sign
    return (inside, far_sign, score, kernel)


def pair_grads(probability, kernel, far_sign, ratios, deltas, grad_rows, value_ext):
    weight_grad = quick_product("thd,ehd->hte", grad_rows, value_ext) - deltas[:, :, None]
    score_grad = (probability * weight_grad).astype(jnp.bfloat16)
    kernel_grad = weight_grad * ratios[:, :, None] * far_sign
    return (score_grad, kernel_grad, kernel * ratios[:, :, None])


def key_side(query_rows, query_feat, grad_rows, weight_low, score_grad, kernel_grad, kernel_scaled):
    scale = 1.0 / math.sqrt(query_rows.shape[2])
    key_grad = quick_product("hte,thd->ehd", score_grad, query_rows) * scale
    value_grad = quick_product("hte,thd->ehd", weight_low, grad_rows) + exact_product(
        "hte,thd->ehd", kernel_scaled, grad_rows
    )
    kfeat_grad = exact_product("hte,thf->ehf", kernel_grad, query_feat)
    return (key_grad, value_grad, kfeat_grad)


def forward_block(
    query_rows,
    query_feat,
    grad_rows,
    key_ext,
    value_ext,
    feat_ext,
    labels_q,
    labels_k,
    windows,
    carry,
):
    carry_state, carry_sum, carry_mark = carry
    offset = key_ext.shape[0] - query_rows.shape[0]
    scale = 1.0 / math.sqrt(query_rows.shape[2])
    inside, far_sign, score, kernel = pair_scores(
        query_rows, query_feat, key_ext, feat_ext, labels_q, labels_k, windows, offset
    )
    maxima = jnp.max(jnp.where(inside, score, -jnp.inf), axis=2)
    shrink = jnp.exp(-maxima)
    carry_on = (labels_q == carry_mark).astype(jnp.float32)
    carry_den = exact_product("thf,hf->ht", query_feat, carry_sum) * carry_on[None, :]
    carry_num = exact_product("thf,hfd->htd", query_feat, carry_state) * carry_on[None, :, None]
    powered = jnp.where(inside, jnp.exp(score - maxima[:, :, None]), 0.0)
    denominator = jnp.sum(powered, axis=2) + shrink * (jnp.sum(kernel, axis=2) + carry_den)
    ratios = shrink / denominator
    probability = powered / denominator[:, :, None]
    weight_low = probability.astype(jnp.bfloat16)
    attended = quick_product("hte,ehd->htd", weight_low, value_ext) + ratios[:, :, None] * (
        exact_product("hte,ehd->htd", kernel, value_ext) + carry_num
    )
    grad_wide = grad_rows.astype(jnp.float32)
    deltas = jnp.sum(jnp.transpose(grad_wide, (1, 0, 2)) * attended, axis=2)
    score_grad, kernel_grad, kernel_scaled = pair_grads(
        probability, kernel, far_sign, ratios, deltas, grad_rows, value_ext
    )
    query_grad = quick_product("hte,ehd->thd", score_grad, key_ext) * scale
    carry_term = (
        exact_product("hfd,thd->thf", carry_state, grad_rows)
        - deltas.T[:, :, None] * carry_sum[None]
    )
    feat_grad = (
        exact_product("hte,ehf->thf", kernel_grad, feat_ext)
        + (carry_on[:, None] * ratios.T)[:, :, None] * carry_term
    )
    return (
        query_grad,
        feat_grad,
        maxima,
        denominator,
        deltas,
        ratios,
        (weight_low, score_grad, kernel_grad, kernel_scaled),
    )


def key_summary(key_feat, value_rows, labels):
    keep = labels == labels[-1]
    state = quick_product(
        "thf,thd->hfd", key_feat * keep.astype(jnp.bfloat16)[:, None, None], value_rows
    )
    total = jnp.sum(key_feat.astype(jnp.float32) * keep.astype(jnp.float32)[:, None, None], axis=0)
    return (state, total, labels[-1])


def query_summary(query_feat, grad_rows, labels, ratios, deltas):
    use = (labels == labels[0]).astype(jnp.float32)[:, None] * ratios.T
    weighted = query_feat.astype(jnp.float32) * use[:, :, None]
    state = exact_product("thf,thd->hfd", weighted, grad_rows)
    total = jnp.sum(weighted * deltas.T[:, :, None], axis=0)
    return (state, total, labels[0])


def combine_pair(earlier, later):
    keep = ((earlier[2] == later[2]) | (later[2] == 0)).astype(jnp.float32)
    state = later[0] + keep.reshape(keep.shape + (1, 1, 1)) * earlier[0]
    total = later[1] + keep.reshape(keep.shape + (1, 1)) * earlier[1]
    mark = jnp.where(later[2] == 0, earlier[2], later[2])
    return (state, total, mark)


def apply_reverse(value_grad, kfeat_grad, key_feat, value_rows, labels, summary):
    state, total, mark = summary
    use = (labels == mark).astype(jnp.float32)[:, None, None]
    value_grad = value_grad + use * exact_product("hfd,thf->thd", state, key_feat)
    kfeat_grad = kfeat_grad + use * (exact_product("hfd,thd->thf", state, value_rows) - total[None])
    return (value_grad, kfeat_grad)


def per_device(queries, keys, values, out_grad, query_feats, key_feats, segment_ids, windows):
    rows = queries.shape[0]
    heads = windows.shape[0]
    head_dim = queries.shape[1] // heads
    feat = query_feats.shape[1] // heads
    tail = rows - WMAX
    query_rows = queries.reshape(rows, heads, head_dim)
    key_rows = keys.reshape(rows, heads, head_dim)
    value_rows = values.reshape(rows, heads, head_dim)
    grad_rows = out_grad.reshape(rows, heads, head_dim)
    query_feat = query_feats.reshape(rows, heads, feat)
    key_feat = key_feats.reshape(rows, heads, feat)
    labels = segment_ids + 1
    edge = jnp.concatenate(
        [
            keys[tail:],
            values[tail:],
            key_feats[tail:],
            jnp.broadcast_to(labels[tail:, None], (WMAX, 128)).astype(keys.dtype),
        ],
        axis=1,
    )
    halo = passed_along(edge, "seq", 1)
    halo_key = halo[:, : heads * head_dim].reshape(WMAX, heads, head_dim)
    halo_value = halo[:, heads * head_dim : 2 * heads * head_dim].reshape(WMAX, heads, head_dim)
    halo_feat = halo[:, 2 * heads * head_dim : 2 * heads * head_dim + heads * feat].reshape(
        WMAX, heads, feat
    )
    halo_label = halo[:, -1].astype(jnp.int32)
    count = lax.axis_size("seq")
    longest = count * rows // 2
    reach = min(count - 1, (longest + rows - 2) // rows)
    carry = unpacked(
        carried_in(packed(key_summary(key_feat, value_rows, labels)), "seq", reach, False),
        heads,
        feat,
    )
    key_ext = jnp.concatenate([halo_key, key_rows], axis=0)
    value_ext = jnp.concatenate([halo_value, value_rows], axis=0)
    feat_ext = jnp.concatenate([halo_feat, key_feat], axis=0)
    label_ext = jnp.concatenate([halo_label, labels], axis=0)
    query_grad, feat_grad, maxima, denominator, deltas, ratios, pieces = forward_block(
        query_rows,
        query_feat,
        grad_rows,
        key_ext,
        value_ext,
        feat_ext,
        labels,
        label_ext,
        windows,
        carry,
    )
    summary = unpacked(
        carried_in(
            packed(query_summary(query_feat, grad_rows, labels, ratios, deltas)), "seq", reach, True
        ),
        heads,
        feat,
    )
    weight_low, score_grad, kernel_grad, kernel_scaled = pieces
    key_full, value_full, kfeat_full = key_side(
        query_rows, query_feat, grad_rows, weight_low, score_grad, kernel_grad, kernel_scaled
    )
    rim = jnp.concatenate([key_full[:WMAX], value_full[:WMAX], kfeat_full[:WMAX]], axis=1)
    rim = passed_along(rim.astype(jnp.bfloat16), "seq", -1).astype(jnp.float32)
    back_key, back_value, back_feat = (
        rim[:, :heads],
        rim[:, heads : 2 * heads],
        rim[:, 2 * heads :],
    )
    key_grad = key_full[WMAX:]
    value_grad = value_full[WMAX:]
    kfeat_grad = kfeat_full[WMAX:]
    key_grad = jnp.concatenate([key_grad[:tail], key_grad[tail:] + back_key], axis=0)
    value_grad = jnp.concatenate([value_grad[:tail], value_grad[tail:] + back_value], axis=0)
    kfeat_grad = jnp.concatenate([kfeat_grad[:tail], kfeat_grad[tail:] + back_feat], axis=0)
    value_grad, kfeat_grad = apply_reverse(
        value_grad, kfeat_grad, key_feat, value_rows, labels, summary
    )
    return (
        query_grad.reshape(rows, heads * head_dim).astype(jnp.bfloat16),
        key_grad.reshape(rows, heads * head_dim).astype(jnp.bfloat16),
        value_grad.reshape(rows, heads * head_dim).astype(jnp.bfloat16),
        feat_grad.reshape(rows, heads * feat).astype(jnp.bfloat16),
        kfeat_grad.reshape(rows, heads * feat).astype(jnp.bfloat16),
    )


def solution(mesh):
    in_specs = (
        P(("group", "seq"), None),
        P(("group", "seq"), None),
        P(("group", "seq"), None),
        P(("group", "seq"), None),
        P(("group", "seq"), None),
        P(("group", "seq"), None),
        P(("group", "seq")),
        P("group"),
    )
    out_specs = (
        P(("group", "seq"), None),
        P(("group", "seq"), None),
        P(("group", "seq"), None),
        P(("group", "seq"), None),
        P(("group", "seq"), None),
    )
    return jax.shard_map(
        per_device, mesh=mesh, in_specs=in_specs, out_specs=out_specs, check_vma=False
    )
```

```python
import math

import jax
import jax.numpy as jnp
from jax import lax
from jax.sharding import PartitionSpec as P

WMAX = 64
RADIX = 4


def passed_along(value, axis, steps):
    count = lax.axis_size(axis)
    leading, last = (max(0, -steps), min(count, count - steps))
    return lax.ppermute(value, axis, [(source, source + steps) for source in range(leading, last)])


def packed(summary):
    state, total, mark = summary
    heads, feat, width = state.shape
    rows = [state.reshape(heads * feat, width), total, jnp.full((1, width), mark, jnp.float32)]
    return jnp.concatenate(rows, axis=0)


def unpacked(payload, heads, feat):
    width = payload.shape[1]
    state = payload[: heads * feat].reshape(heads, feat, width)
    total = payload[heads * feat : heads * feat + heads]
    mark = payload[heads * feat + heads, 0].astype(jnp.int32)
    return (state, total, mark)


def join_packed(earlier, later):
    at = later.shape[0] - 1
    mark_e, mark_l = (earlier[at, 0], later[at, 0])
    keep = ((mark_e == mark_l) | (mark_l == 0)).astype(jnp.float32)
    mark = jnp.where(mark_l == 0, mark_e, mark_l)
    row = lax.broadcasted_iota(jnp.int32, later.shape, 0)
    return jnp.where(row == at, mark, later + keep * earlier)


def carried_in(value, axis, reach, backward, radix):
    step = -1 if backward else 1
    total = passed_along(value, axis, step)
    length = 1
    while length < min(radix, reach):
        length += 1
        total = join_packed(passed_along(value, axis, length * step), total)
    while length < reach:
        total = join_packed(passed_along(total, axis, length * step), total)
        length *= 2
    return total


def quick_product(form, left, right):
    return jnp.einsum(form, left, right, preferred_element_type=jnp.float32)


def exact_product(form, left, right):
    return jnp.einsum(
        form,
        left.astype(jnp.float32),
        right.astype(jnp.float32),
        precision=lax.Precision.HIGHEST,
        preferred_element_type=jnp.float32,
    )


def pair_masks(labels_q, labels_k, windows, offset):
    distance = (
        jnp.arange(labels_q.shape[0], dtype=jnp.int32)[:, None]
        + offset
        - jnp.arange(labels_k.shape[0], dtype=jnp.int32)[None, :]
    )
    matched = (labels_q[:, None] == labels_k[None, :]) & (labels_q[:, None] > 0) & (distance >= 0)
    inside = matched[None] & (distance[None] < windows[:, None, None])
    is_local = (jnp.arange(labels_k.shape[0], dtype=jnp.int32) >= offset)[None, None, :]
    far_sign = jnp.where(
        is_local, (matched[None] & ~inside).astype(jnp.float32), -inside.astype(jnp.float32)
    )
    return (inside, far_sign)


def pair_scores(query_rows, query_feat, key_ext, feat_ext, labels_q, labels_k, windows, offset):
    inside, far_sign = pair_masks(labels_q, labels_k, windows, offset)
    scale = 1.0 / math.sqrt(query_rows.shape[2])
    score = quick_product("thd,ehd->hte", query_rows, key_ext) * scale
    kernel = quick_product("thf,ehf->hte", query_feat, feat_ext) * far_sign
    return (inside, far_sign, score, kernel)


def pair_grads(probability, kernel, far_sign, ratios, deltas, grad_rows, value_ext):
    weight_grad = quick_product("thd,ehd->hte", grad_rows, value_ext) - deltas[:, :, None]
    score_grad = (probability * weight_grad).astype(jnp.bfloat16)
    kernel_grad = weight_grad * ratios[:, :, None] * far_sign
    return (score_grad, kernel_grad, kernel * ratios[:, :, None])


def key_side(query_rows, query_feat, grad_rows, weight_low, score_grad, kernel_grad, kernel_scaled):
    scale = 1.0 / math.sqrt(query_rows.shape[2])
    key_grad = quick_product("hte,thd->ehd", score_grad, query_rows) * scale
    value_grad = quick_product("hte,thd->ehd", weight_low, grad_rows) + exact_product(
        "hte,thd->ehd", kernel_scaled, grad_rows
    )
    kfeat_grad = exact_product("hte,thf->ehf", kernel_grad, query_feat)
    return (key_grad, value_grad, kfeat_grad)


def forward_block(
    query_rows,
    query_feat,
    grad_rows,
    key_ext,
    value_ext,
    feat_ext,
    labels_q,
    labels_k,
    windows,
    carry,
):
    carry_state, carry_sum, carry_mark = carry
    offset = key_ext.shape[0] - query_rows.shape[0]
    scale = 1.0 / math.sqrt(query_rows.shape[2])
    inside, far_sign, score, kernel = pair_scores(
        query_rows, query_feat, key_ext, feat_ext, labels_q, labels_k, windows, offset
    )
    maxima = jnp.max(jnp.where(inside, score, -jnp.inf), axis=2)
    shrink = jnp.exp(-maxima)
    carry_on = (labels_q == carry_mark).astype(jnp.float32)
    carry_den = exact_product("thf,hf->ht", query_feat, carry_sum) * carry_on[None, :]
    carry_num = exact_product("thf,hfd->htd", query_feat, carry_state) * carry_on[None, :, None]
    powered = jnp.where(inside, jnp.exp(score - maxima[:, :, None]), 0.0)
    denominator = jnp.sum(powered, axis=2) + shrink * (jnp.sum(kernel, axis=2) + carry_den)
    ratios = shrink / denominator
    probability = powered / denominator[:, :, None]
    weight_low = probability.astype(jnp.bfloat16)
    attended = quick_product("hte,ehd->htd", weight_low, value_ext) + ratios[:, :, None] * (
        exact_product("hte,ehd->htd", kernel, value_ext) + carry_num
    )
    grad_wide = grad_rows.astype(jnp.float32)
    deltas = jnp.sum(jnp.transpose(grad_wide, (1, 0, 2)) * attended, axis=2)
    score_grad, kernel_grad, kernel_scaled = pair_grads(
        probability, kernel, far_sign, ratios, deltas, grad_rows, value_ext
    )
    query_grad = quick_product("hte,ehd->thd", score_grad, key_ext) * scale
    carry_term = (
        exact_product("hfd,thd->thf", carry_state, grad_rows)
        - deltas.T[:, :, None] * carry_sum[None]
    )
    feat_grad = (
        exact_product("hte,ehf->thf", kernel_grad, feat_ext)
        + (carry_on[:, None] * ratios.T)[:, :, None] * carry_term
    )
    return (
        query_grad,
        feat_grad,
        maxima,
        denominator,
        deltas,
        ratios,
        (weight_low, score_grad, kernel_grad, kernel_scaled),
    )


def key_summary(key_feat, value_rows, labels):
    keep = labels == labels[-1]
    state = quick_product(
        "thf,thd->hfd", key_feat * keep.astype(jnp.bfloat16)[:, None, None], value_rows
    )
    total = jnp.sum(key_feat.astype(jnp.float32) * keep.astype(jnp.float32)[:, None, None], axis=0)
    return (state, total, labels[-1])


def query_summary(query_feat, grad_rows, labels, ratios, deltas):
    use = (labels == labels[0]).astype(jnp.float32)[:, None] * ratios.T
    weighted = query_feat.astype(jnp.float32) * use[:, :, None]
    state = exact_product("thf,thd->hfd", weighted, grad_rows)
    total = jnp.sum(weighted * deltas.T[:, :, None], axis=0)
    return (state, total, labels[0])


def combine_pair(earlier, later):
    keep = ((earlier[2] == later[2]) | (later[2] == 0)).astype(jnp.float32)
    state = later[0] + keep.reshape(keep.shape + (1, 1, 1)) * earlier[0]
    total = later[1] + keep.reshape(keep.shape + (1, 1)) * earlier[1]
    mark = jnp.where(later[2] == 0, earlier[2], later[2])
    return (state, total, mark)


def apply_reverse(value_grad, kfeat_grad, key_feat, value_rows, labels, summary):
    state, total, mark = summary
    use = (labels == mark).astype(jnp.float32)[:, None, None]
    value_grad = value_grad + use * exact_product("hfd,thf->thd", state, key_feat)
    kfeat_grad = kfeat_grad + use * (exact_product("hfd,thd->thf", state, value_rows) - total[None])
    return (value_grad, kfeat_grad)


def per_device(queries, keys, values, out_grad, query_feats, key_feats, segment_ids, windows):
    rows = queries.shape[0]
    heads = windows.shape[0]
    head_dim = queries.shape[1] // heads
    feat = query_feats.shape[1] // heads
    tail = rows - WMAX
    query_rows = queries.reshape(rows, heads, head_dim)
    key_rows = keys.reshape(rows, heads, head_dim)
    value_rows = values.reshape(rows, heads, head_dim)
    grad_rows = out_grad.reshape(rows, heads, head_dim)
    query_feat = query_feats.reshape(rows, heads, feat)
    key_feat = key_feats.reshape(rows, heads, feat)
    labels = segment_ids + 1
    edge = jnp.concatenate(
        [
            keys[tail:],
            values[tail:],
            key_feats[tail:],
            jnp.broadcast_to(labels[tail:, None], (WMAX, 128)).astype(keys.dtype),
        ],
        axis=1,
    )
    halo = passed_along(edge, "seq", 1)
    halo_key = halo[:, : heads * head_dim].reshape(WMAX, heads, head_dim)
    halo_value = halo[:, heads * head_dim : 2 * heads * head_dim].reshape(WMAX, heads, head_dim)
    halo_feat = halo[:, 2 * heads * head_dim : 2 * heads * head_dim + heads * feat].reshape(
        WMAX, heads, feat
    )
    halo_label = halo[:, -1].astype(jnp.int32)
    count = lax.axis_size("seq")
    longest = count * rows // 2
    reach = min(count - 1, (longest + rows - 2) // rows)
    carry = unpacked(
        carried_in(
            packed(key_summary(key_feat, value_rows, labels)), "seq", reach, False, RADIX
        ),
        heads,
        feat,
    )
    key_ext = jnp.concatenate([halo_key, key_rows], axis=0)
    value_ext = jnp.concatenate([halo_value, value_rows], axis=0)
    feat_ext = jnp.concatenate([halo_feat, key_feat], axis=0)
    label_ext = jnp.concatenate([halo_label, labels], axis=0)
    query_grad, feat_grad, maxima, denominator, deltas, ratios, pieces = forward_block(
        query_rows,
        query_feat,
        grad_rows,
        key_ext,
        value_ext,
        feat_ext,
        labels,
        label_ext,
        windows,
        carry,
    )
    summary = unpacked(
        carried_in(
            packed(query_summary(query_feat, grad_rows, labels, ratios, deltas)),
            "seq",
            reach,
            True,
            RADIX,
        ),
        heads,
        feat,
    )
    weight_low, score_grad, kernel_grad, kernel_scaled = pieces
    key_full, value_full, kfeat_full = key_side(
        query_rows, query_feat, grad_rows, weight_low, score_grad, kernel_grad, kernel_scaled
    )
    rim = jnp.concatenate([key_full[:WMAX], value_full[:WMAX], kfeat_full[:WMAX]], axis=1)
    rim = passed_along(rim.astype(jnp.bfloat16), "seq", -1).astype(jnp.float32)
    back_key, back_value, back_feat = (
        rim[:, :heads],
        rim[:, heads : 2 * heads],
        rim[:, 2 * heads :],
    )
    key_grad = key_full[WMAX:]
    value_grad = value_full[WMAX:]
    kfeat_grad = kfeat_full[WMAX:]
    key_grad = jnp.concatenate([key_grad[:tail], key_grad[tail:] + back_key], axis=0)
    value_grad = jnp.concatenate([value_grad[:tail], value_grad[tail:] + back_value], axis=0)
    kfeat_grad = jnp.concatenate([kfeat_grad[:tail], kfeat_grad[tail:] + back_feat], axis=0)
    value_grad, kfeat_grad = apply_reverse(
        value_grad, kfeat_grad, key_feat, value_rows, labels, summary
    )
    return (
        query_grad.reshape(rows, heads * head_dim).astype(jnp.bfloat16),
        key_grad.reshape(rows, heads * head_dim).astype(jnp.bfloat16),
        value_grad.reshape(rows, heads * head_dim).astype(jnp.bfloat16),
        feat_grad.reshape(rows, heads * feat).astype(jnp.bfloat16),
        kfeat_grad.reshape(rows, heads * feat).astype(jnp.bfloat16),
    )


def solution(mesh):
    in_specs = (
        P(("group", "seq"), None),
        P(("group", "seq"), None),
        P(("group", "seq"), None),
        P(("group", "seq"), None),
        P(("group", "seq"), None),
        P(("group", "seq"), None),
        P(("group", "seq")),
        P("group"),
    )
    out_specs = (
        P(("group", "seq"), None),
        P(("group", "seq"), None),
        P(("group", "seq"), None),
        P(("group", "seq"), None),
        P(("group", "seq"), None),
    )
    return jax.shard_map(
        per_device, mesh=mesh, in_specs=in_specs, out_specs=out_specs, check_vma=False
    )
```

```python
import math

import jax
import jax.numpy as jnp
from jax import lax
from jax.sharding import PartitionSpec as P

WMAX = 64


def passed_along(value, axis, steps):
    count = lax.axis_size(axis)
    leading, last = (max(0, -steps), min(count, count - steps))
    return lax.ppermute(value, axis, [(source, source + steps) for source in range(leading, last)])


def packed(summary):
    state, total, mark = summary
    heads, feat, width = state.shape
    half = heads // 2
    marks = jnp.full((2, 1, width), mark, jnp.float32)
    rows = [state.reshape(2, half * feat, width), total.reshape(2, half, width), marks]
    return jnp.concatenate(rows, axis=1)


def unpacked(payload, heads, feat):
    width = payload.shape[2]
    half = heads // 2
    state = payload[:, : half * feat].reshape(heads, feat, width)
    total = payload[:, half * feat : half * feat + half].reshape(heads, width)
    mark = payload[0, half * feat + half, 0].astype(jnp.int32)
    return (state, total, mark)


def join_packed(earlier, later):
    at = later.shape[-2] - 1
    mark_e, mark_l = (earlier[..., at : at + 1, :1], later[..., at : at + 1, :1])
    keep = ((mark_e == mark_l) | (mark_l == 0)).astype(jnp.float32)
    mark = jnp.where(mark_l == 0, mark_e, mark_l)
    row = lax.broadcasted_iota(jnp.int32, later.shape, later.ndim - 2)
    return jnp.where(row == at, mark, later + keep * earlier)


def between_cores(value, axis, source):
    count = lax.axis_size(axis)
    pairs = [(chip + source, chip + 1 - source) for chip in range(0, count, 2)]
    return lax.ppermute(value, axis, pairs)


def swapped(value, axis):
    count = lax.axis_size(axis)
    pairs = [(device, device ^ 1) for device in range(count)]
    return lax.ppermute(value, axis, pairs)


def carried_in(value, axis, reach, backward):
    step = -1 if backward else 1
    parity = lax.axis_index(axis) % 2
    first_core = 1 if backward else 0
    is_first = parity == first_core
    own_half = lax.dynamic_index_in_dim(value, parity, 0, keepdims=False)
    other_half = lax.dynamic_index_in_dim(value, 1 - parity, 0, keepdims=False)
    whole_first = between_cores(value, axis, first_core)
    half_second = between_cores(other_half, axis, 1 - first_core)
    first_half = lax.dynamic_index_in_dim(whole_first, parity, 0, keepdims=False)
    earlier = jnp.where(is_first, own_half, first_half)
    later = jnp.where(is_first, half_second, own_half)
    chip = join_packed(earlier, later)
    chips = (reach + 1) // 2
    total = passed_along(chip, axis, 2 * step)
    length = 1
    if chips >= 2:
        total = join_packed(passed_along(chip, axis, 4 * step), total)
        length = 2
    while length < chips:
        total = join_packed(passed_along(total, axis, 2 * length * step), total)
        length *= 2
    partner = swapped(total, axis)
    whole = jnp.where(parity == 0, jnp.stack([total, partner]), jnp.stack([partner, total]))
    return jnp.where(is_first, whole, join_packed(whole, whole_first))


def quick_product(form, left, right):
    return jnp.einsum(form, left, right, preferred_element_type=jnp.float32)


def exact_product(form, left, right):
    return jnp.einsum(
        form,
        left.astype(jnp.float32),
        right.astype(jnp.float32),
        precision=lax.Precision.HIGHEST,
        preferred_element_type=jnp.float32,
    )


def pair_masks(labels_q, labels_k, windows, offset):
    distance = (
        jnp.arange(labels_q.shape[0], dtype=jnp.int32)[:, None]
        + offset
        - jnp.arange(labels_k.shape[0], dtype=jnp.int32)[None, :]
    )
    matched = (labels_q[:, None] == labels_k[None, :]) & (labels_q[:, None] > 0) & (distance >= 0)
    inside = matched[None] & (distance[None] < windows[:, None, None])
    is_local = (jnp.arange(labels_k.shape[0], dtype=jnp.int32) >= offset)[None, None, :]
    far_sign = jnp.where(
        is_local, (matched[None] & ~inside).astype(jnp.float32), -inside.astype(jnp.float32)
    )
    return (inside, far_sign)


def pair_scores(query_rows, query_feat, key_ext, feat_ext, labels_q, labels_k, windows, offset):
    inside, far_sign = pair_masks(labels_q, labels_k, windows, offset)
    scale = 1.0 / math.sqrt(query_rows.shape[2])
    score = quick_product("thd,ehd->hte", query_rows, key_ext) * scale
    kernel = quick_product("thf,ehf->hte", query_feat, feat_ext) * far_sign
    return (inside, far_sign, score, kernel)


def pair_grads(probability, kernel, far_sign, ratios, deltas, grad_rows, value_ext):
    weight_grad = quick_product("thd,ehd->hte", grad_rows, value_ext) - deltas[:, :, None]
    score_grad = (probability * weight_grad).astype(jnp.bfloat16)
    kernel_grad = weight_grad * ratios[:, :, None] * far_sign
    return (score_grad, kernel_grad, kernel * ratios[:, :, None])


def key_side(query_rows, query_feat, grad_rows, weight_low, score_grad, kernel_grad, kernel_scaled):
    scale = 1.0 / math.sqrt(query_rows.shape[2])
    key_grad = quick_product("hte,thd->ehd", score_grad, query_rows) * scale
    value_grad = quick_product("hte,thd->ehd", weight_low, grad_rows) + exact_product(
        "hte,thd->ehd", kernel_scaled, grad_rows
    )
    kfeat_grad = exact_product("hte,thf->ehf", kernel_grad, query_feat)
    return (key_grad, value_grad, kfeat_grad)


def forward_block(
    query_rows,
    query_feat,
    grad_rows,
    key_ext,
    value_ext,
    feat_ext,
    labels_q,
    labels_k,
    windows,
    carry,
):
    carry_state, carry_sum, carry_mark = carry
    offset = key_ext.shape[0] - query_rows.shape[0]
    scale = 1.0 / math.sqrt(query_rows.shape[2])
    inside, far_sign, score, kernel = pair_scores(
        query_rows, query_feat, key_ext, feat_ext, labels_q, labels_k, windows, offset
    )
    maxima = jnp.max(jnp.where(inside, score, -jnp.inf), axis=2)
    shrink = jnp.exp(-maxima)
    carry_on = (labels_q == carry_mark).astype(jnp.float32)
    carry_den = exact_product("thf,hf->ht", query_feat, carry_sum) * carry_on[None, :]
    carry_num = exact_product("thf,hfd->htd", query_feat, carry_state) * carry_on[None, :, None]
    powered = jnp.where(inside, jnp.exp(score - maxima[:, :, None]), 0.0)
    denominator = jnp.sum(powered, axis=2) + shrink * (jnp.sum(kernel, axis=2) + carry_den)
    ratios = shrink / denominator
    probability = powered / denominator[:, :, None]
    weight_low = probability.astype(jnp.bfloat16)
    attended = quick_product("hte,ehd->htd", weight_low, value_ext) + ratios[:, :, None] * (
        exact_product("hte,ehd->htd", kernel, value_ext) + carry_num
    )
    grad_wide = grad_rows.astype(jnp.float32)
    deltas = jnp.sum(jnp.transpose(grad_wide, (1, 0, 2)) * attended, axis=2)
    score_grad, kernel_grad, kernel_scaled = pair_grads(
        probability, kernel, far_sign, ratios, deltas, grad_rows, value_ext
    )
    query_grad = quick_product("hte,ehd->thd", score_grad, key_ext) * scale
    carry_term = (
        exact_product("hfd,thd->thf", carry_state, grad_rows)
        - deltas.T[:, :, None] * carry_sum[None]
    )
    feat_grad = (
        exact_product("hte,ehf->thf", kernel_grad, feat_ext)
        + (carry_on[:, None] * ratios.T)[:, :, None] * carry_term
    )
    return (
        query_grad,
        feat_grad,
        maxima,
        denominator,
        deltas,
        ratios,
        (weight_low, score_grad, kernel_grad, kernel_scaled),
    )


def key_summary(key_feat, value_rows, labels):
    keep = labels == labels[-1]
    state = quick_product(
        "thf,thd->hfd", key_feat * keep.astype(jnp.bfloat16)[:, None, None], value_rows
    )
    total = jnp.sum(key_feat.astype(jnp.float32) * keep.astype(jnp.float32)[:, None, None], axis=0)
    return (state, total, labels[-1])


def query_summary(query_feat, grad_rows, labels, ratios, deltas):
    use = (labels == labels[0]).astype(jnp.float32)[:, None] * ratios.T
    weighted = query_feat.astype(jnp.float32) * use[:, :, None]
    state = exact_product("thf,thd->hfd", weighted, grad_rows)
    total = jnp.sum(weighted * deltas.T[:, :, None], axis=0)
    return (state, total, labels[0])


def combine_pair(earlier, later):
    keep = ((earlier[2] == later[2]) | (later[2] == 0)).astype(jnp.float32)
    state = later[0] + keep.reshape(keep.shape + (1, 1, 1)) * earlier[0]
    total = later[1] + keep.reshape(keep.shape + (1, 1)) * earlier[1]
    mark = jnp.where(later[2] == 0, earlier[2], later[2])
    return (state, total, mark)


def apply_reverse(value_grad, kfeat_grad, key_feat, value_rows, labels, summary):
    state, total, mark = summary
    use = (labels == mark).astype(jnp.float32)[:, None, None]
    value_grad = value_grad + use * exact_product("hfd,thf->thd", state, key_feat)
    kfeat_grad = kfeat_grad + use * (exact_product("hfd,thd->thf", state, value_rows) - total[None])
    return (value_grad, kfeat_grad)


def per_device(queries, keys, values, out_grad, query_feats, key_feats, segment_ids, windows):
    rows = queries.shape[0]
    heads = windows.shape[0]
    head_dim = queries.shape[1] // heads
    feat = query_feats.shape[1] // heads
    tail = rows - WMAX
    query_rows = queries.reshape(rows, heads, head_dim)
    key_rows = keys.reshape(rows, heads, head_dim)
    value_rows = values.reshape(rows, heads, head_dim)
    grad_rows = out_grad.reshape(rows, heads, head_dim)
    query_feat = query_feats.reshape(rows, heads, feat)
    key_feat = key_feats.reshape(rows, heads, feat)
    labels = segment_ids + 1
    edge = jnp.concatenate(
        [
            keys[tail:],
            values[tail:],
            key_feats[tail:],
            jnp.broadcast_to(labels[tail:, None], (WMAX, 128)).astype(keys.dtype),
        ],
        axis=1,
    )
    halo = passed_along(edge, "seq", 1)
    halo_key = halo[:, : heads * head_dim].reshape(WMAX, heads, head_dim)
    halo_value = halo[:, heads * head_dim : 2 * heads * head_dim].reshape(WMAX, heads, head_dim)
    halo_feat = halo[:, 2 * heads * head_dim : 2 * heads * head_dim + heads * feat].reshape(
        WMAX, heads, feat
    )
    halo_label = halo[:, -1].astype(jnp.int32)
    count = lax.axis_size("seq")
    longest = count * rows // 2
    reach = min(count - 1, (longest + rows - 2) // rows)
    carry = unpacked(
        carried_in(packed(key_summary(key_feat, value_rows, labels)), "seq", reach, False),
        heads,
        feat,
    )
    key_ext = jnp.concatenate([halo_key, key_rows], axis=0)
    value_ext = jnp.concatenate([halo_value, value_rows], axis=0)
    feat_ext = jnp.concatenate([halo_feat, key_feat], axis=0)
    label_ext = jnp.concatenate([halo_label, labels], axis=0)
    query_grad, feat_grad, maxima, denominator, deltas, ratios, pieces = forward_block(
        query_rows,
        query_feat,
        grad_rows,
        key_ext,
        value_ext,
        feat_ext,
        labels,
        label_ext,
        windows,
        carry,
    )
    summary = unpacked(
        carried_in(
            packed(query_summary(query_feat, grad_rows, labels, ratios, deltas)), "seq", reach, True
        ),
        heads,
        feat,
    )
    weight_low, score_grad, kernel_grad, kernel_scaled = pieces
    key_full, value_full, kfeat_full = key_side(
        query_rows, query_feat, grad_rows, weight_low, score_grad, kernel_grad, kernel_scaled
    )
    rim = jnp.concatenate([key_full[:WMAX], value_full[:WMAX], kfeat_full[:WMAX]], axis=1)
    rim = passed_along(rim.astype(jnp.bfloat16), "seq", -1).astype(jnp.float32)
    back_key, back_value, back_feat = (
        rim[:, :heads],
        rim[:, heads : 2 * heads],
        rim[:, 2 * heads :],
    )
    key_grad = key_full[WMAX:]
    value_grad = value_full[WMAX:]
    kfeat_grad = kfeat_full[WMAX:]
    key_grad = jnp.concatenate([key_grad[:tail], key_grad[tail:] + back_key], axis=0)
    value_grad = jnp.concatenate([value_grad[:tail], value_grad[tail:] + back_value], axis=0)
    kfeat_grad = jnp.concatenate([kfeat_grad[:tail], kfeat_grad[tail:] + back_feat], axis=0)
    value_grad, kfeat_grad = apply_reverse(
        value_grad, kfeat_grad, key_feat, value_rows, labels, summary
    )
    return (
        query_grad.reshape(rows, heads * head_dim).astype(jnp.bfloat16),
        key_grad.reshape(rows, heads * head_dim).astype(jnp.bfloat16),
        value_grad.reshape(rows, heads * head_dim).astype(jnp.bfloat16),
        feat_grad.reshape(rows, heads * feat).astype(jnp.bfloat16),
        kfeat_grad.reshape(rows, heads * feat).astype(jnp.bfloat16),
    )


def solution(mesh):
    in_specs = (
        P(("group", "seq"), None),
        P(("group", "seq"), None),
        P(("group", "seq"), None),
        P(("group", "seq"), None),
        P(("group", "seq"), None),
        P(("group", "seq"), None),
        P(("group", "seq")),
        P("group"),
    )
    out_specs = (
        P(("group", "seq"), None),
        P(("group", "seq"), None),
        P(("group", "seq"), None),
        P(("group", "seq"), None),
        P(("group", "seq"), None),
    )
    return jax.shard_map(
        per_device, mesh=mesh, in_specs=in_specs, out_specs=out_specs, check_vma=False
    )
```

```python
import math

import jax
import jax.numpy as jnp
from jax import lax
from jax.sharding import PartitionSpec as P

WMAX = 64


def passed_along(value, axis, steps):
    count = lax.axis_size(axis)
    leading, last = (max(0, -steps), min(count, count - steps))
    return lax.ppermute(value, axis, [(source, source + steps) for source in range(leading, last)])


def packed(summary):
    state, total, mark = summary
    heads, feat, width = state.shape
    half = heads // 2
    marks = jnp.full((2, 1, width), mark, jnp.float32)
    rows = [state.reshape(2, half * feat, width), total.reshape(2, half, width), marks]
    return jnp.concatenate(rows, axis=1)


def unpacked(payload, heads, feat):
    width = payload.shape[2]
    half = heads // 2
    state = payload[:, : half * feat].reshape(heads, feat, width)
    total = payload[:, half * feat : half * feat + half].reshape(heads, width)
    mark = payload[0, half * feat + half, 0].astype(jnp.int32)
    return (state, total, mark)


def join_packed(earlier, later):
    at = later.shape[-2] - 1
    mark_e, mark_l = (earlier[..., at : at + 1, :1], later[..., at : at + 1, :1])
    keep = ((mark_e == mark_l) | (mark_l == 0)).astype(jnp.float32)
    mark = jnp.where(mark_l == 0, mark_e, mark_l)
    row = lax.broadcasted_iota(jnp.int32, later.shape, later.ndim - 2)
    return jnp.where(row == at, mark, later + keep * earlier)


def swapped(value, axis):
    count = lax.axis_size(axis)
    pairs = [(device, device ^ 1) for device in range(count)]
    return lax.ppermute(value, axis, pairs)


def carried_in(value, axis, reach, backward):
    step = -1 if backward else 1
    parity = lax.axis_index(axis) % 2
    is_first = parity == (1 if backward else 0)
    own_half = lax.dynamic_index_in_dim(value, parity, 0, keepdims=False)
    other_half = lax.dynamic_index_in_dim(value, 1 - parity, 0, keepdims=False)
    partner_half = swapped(other_half, axis)
    earlier = jnp.where(is_first, own_half, partner_half)
    later = jnp.where(is_first, partner_half, own_half)
    chip = join_packed(earlier, later)
    chips = (reach + 1) // 2
    total = passed_along(chip, axis, 2 * step)
    length = 1
    if chips >= 2:
        total = join_packed(passed_along(chip, axis, 4 * step), total)
        length = 2
    while length < chips:
        total = join_packed(passed_along(total, axis, 2 * length * step), total)
        length *= 2
    extended = join_packed(total, earlier)
    mine = jnp.where(is_first, total, extended)
    theirs = swapped(jnp.where(is_first, extended, total), axis)
    return jnp.where(parity == 0, jnp.stack([mine, theirs]), jnp.stack([theirs, mine]))


def quick_product(form, left, right):
    return jnp.einsum(form, left, right, preferred_element_type=jnp.float32)


def exact_product(form, left, right):
    return jnp.einsum(
        form,
        left.astype(jnp.float32),
        right.astype(jnp.float32),
        precision=lax.Precision.HIGHEST,
        preferred_element_type=jnp.float32,
    )


def pair_masks(labels_q, labels_k, windows, offset):
    distance = (
        jnp.arange(labels_q.shape[0], dtype=jnp.int32)[:, None]
        + offset
        - jnp.arange(labels_k.shape[0], dtype=jnp.int32)[None, :]
    )
    matched = (labels_q[:, None] == labels_k[None, :]) & (labels_q[:, None] > 0) & (distance >= 0)
    inside = matched[None] & (distance[None] < windows[:, None, None])
    is_local = (jnp.arange(labels_k.shape[0], dtype=jnp.int32) >= offset)[None, None, :]
    far_sign = jnp.where(
        is_local, (matched[None] & ~inside).astype(jnp.float32), -inside.astype(jnp.float32)
    )
    return (inside, far_sign)


def pair_scores(query_rows, query_feat, key_ext, feat_ext, labels_q, labels_k, windows, offset):
    inside, far_sign = pair_masks(labels_q, labels_k, windows, offset)
    scale = 1.0 / math.sqrt(query_rows.shape[2])
    score = quick_product("thd,ehd->hte", query_rows, key_ext) * scale
    kernel = quick_product("thf,ehf->hte", query_feat, feat_ext) * far_sign
    return (inside, far_sign, score, kernel)


def pair_grads(probability, kernel, far_sign, ratios, deltas, grad_rows, value_ext):
    weight_grad = quick_product("thd,ehd->hte", grad_rows, value_ext) - deltas[:, :, None]
    score_grad = (probability * weight_grad).astype(jnp.bfloat16)
    kernel_grad = weight_grad * ratios[:, :, None] * far_sign
    return (score_grad, kernel_grad, kernel * ratios[:, :, None])


def key_side(query_rows, query_feat, grad_rows, weight_low, score_grad, kernel_grad, kernel_scaled):
    scale = 1.0 / math.sqrt(query_rows.shape[2])
    key_grad = quick_product("hte,thd->ehd", score_grad, query_rows) * scale
    value_grad = quick_product("hte,thd->ehd", weight_low, grad_rows) + exact_product(
        "hte,thd->ehd", kernel_scaled, grad_rows
    )
    kfeat_grad = exact_product("hte,thf->ehf", kernel_grad, query_feat)
    return (key_grad, value_grad, kfeat_grad)


def forward_block(
    query_rows,
    query_feat,
    grad_rows,
    key_ext,
    value_ext,
    feat_ext,
    labels_q,
    labels_k,
    windows,
    carry,
):
    carry_state, carry_sum, carry_mark = carry
    offset = key_ext.shape[0] - query_rows.shape[0]
    scale = 1.0 / math.sqrt(query_rows.shape[2])
    inside, far_sign, score, kernel = pair_scores(
        query_rows, query_feat, key_ext, feat_ext, labels_q, labels_k, windows, offset
    )
    maxima = jnp.max(jnp.where(inside, score, -jnp.inf), axis=2)
    shrink = jnp.exp(-maxima)
    carry_on = (labels_q == carry_mark).astype(jnp.float32)
    carry_den = exact_product("thf,hf->ht", query_feat, carry_sum) * carry_on[None, :]
    carry_num = exact_product("thf,hfd->htd", query_feat, carry_state) * carry_on[None, :, None]
    powered = jnp.where(inside, jnp.exp(score - maxima[:, :, None]), 0.0)
    denominator = jnp.sum(powered, axis=2) + shrink * (jnp.sum(kernel, axis=2) + carry_den)
    ratios = shrink / denominator
    probability = powered / denominator[:, :, None]
    weight_low = probability.astype(jnp.bfloat16)
    attended = quick_product("hte,ehd->htd", weight_low, value_ext) + ratios[:, :, None] * (
        exact_product("hte,ehd->htd", kernel, value_ext) + carry_num
    )
    grad_wide = grad_rows.astype(jnp.float32)
    deltas = jnp.sum(jnp.transpose(grad_wide, (1, 0, 2)) * attended, axis=2)
    score_grad, kernel_grad, kernel_scaled = pair_grads(
        probability, kernel, far_sign, ratios, deltas, grad_rows, value_ext
    )
    query_grad = quick_product("hte,ehd->thd", score_grad, key_ext) * scale
    carry_term = (
        exact_product("hfd,thd->thf", carry_state, grad_rows)
        - deltas.T[:, :, None] * carry_sum[None]
    )
    feat_grad = (
        exact_product("hte,ehf->thf", kernel_grad, feat_ext)
        + (carry_on[:, None] * ratios.T)[:, :, None] * carry_term
    )
    return (
        query_grad,
        feat_grad,
        maxima,
        denominator,
        deltas,
        ratios,
        (weight_low, score_grad, kernel_grad, kernel_scaled),
    )


def key_summary(key_feat, value_rows, labels):
    keep = labels == labels[-1]
    state = quick_product(
        "thf,thd->hfd", key_feat * keep.astype(jnp.bfloat16)[:, None, None], value_rows
    )
    total = jnp.sum(key_feat.astype(jnp.float32) * keep.astype(jnp.float32)[:, None, None], axis=0)
    return (state, total, labels[-1])


def query_summary(query_feat, grad_rows, labels, ratios, deltas):
    use = (labels == labels[0]).astype(jnp.float32)[:, None] * ratios.T
    weighted = query_feat.astype(jnp.float32) * use[:, :, None]
    state = exact_product("thf,thd->hfd", weighted, grad_rows)
    total = jnp.sum(weighted * deltas.T[:, :, None], axis=0)
    return (state, total, labels[0])


def combine_pair(earlier, later):
    keep = ((earlier[2] == later[2]) | (later[2] == 0)).astype(jnp.float32)
    state = later[0] + keep.reshape(keep.shape + (1, 1, 1)) * earlier[0]
    total = later[1] + keep.reshape(keep.shape + (1, 1)) * earlier[1]
    mark = jnp.where(later[2] == 0, earlier[2], later[2])
    return (state, total, mark)


def apply_reverse(value_grad, kfeat_grad, key_feat, value_rows, labels, summary):
    state, total, mark = summary
    use = (labels == mark).astype(jnp.float32)[:, None, None]
    value_grad = value_grad + use * exact_product("hfd,thf->thd", state, key_feat)
    kfeat_grad = kfeat_grad + use * (exact_product("hfd,thd->thf", state, value_rows) - total[None])
    return (value_grad, kfeat_grad)


def per_device(queries, keys, values, out_grad, query_feats, key_feats, segment_ids, windows):
    rows = queries.shape[0]
    heads = windows.shape[0]
    head_dim = queries.shape[1] // heads
    feat = query_feats.shape[1] // heads
    tail = rows - WMAX
    query_rows = queries.reshape(rows, heads, head_dim)
    key_rows = keys.reshape(rows, heads, head_dim)
    value_rows = values.reshape(rows, heads, head_dim)
    grad_rows = out_grad.reshape(rows, heads, head_dim)
    query_feat = query_feats.reshape(rows, heads, feat)
    key_feat = key_feats.reshape(rows, heads, feat)
    labels = segment_ids + 1
    edge = jnp.concatenate(
        [
            keys[tail:],
            values[tail:],
            key_feats[tail:],
            jnp.broadcast_to(labels[tail:, None], (WMAX, 128)).astype(keys.dtype),
        ],
        axis=1,
    )
    halo = passed_along(edge, "seq", 1)
    halo_key = halo[:, : heads * head_dim].reshape(WMAX, heads, head_dim)
    halo_value = halo[:, heads * head_dim : 2 * heads * head_dim].reshape(WMAX, heads, head_dim)
    halo_feat = halo[:, 2 * heads * head_dim : 2 * heads * head_dim + heads * feat].reshape(
        WMAX, heads, feat
    )
    halo_label = halo[:, -1].astype(jnp.int32)
    count = lax.axis_size("seq")
    longest = count * rows // 2
    reach = min(count - 1, (longest + rows - 2) // rows)
    carry = unpacked(
        carried_in(packed(key_summary(key_feat, value_rows, labels)), "seq", reach, False),
        heads,
        feat,
    )
    key_ext = jnp.concatenate([halo_key, key_rows], axis=0)
    value_ext = jnp.concatenate([halo_value, value_rows], axis=0)
    feat_ext = jnp.concatenate([halo_feat, key_feat], axis=0)
    label_ext = jnp.concatenate([halo_label, labels], axis=0)
    query_grad, feat_grad, maxima, denominator, deltas, ratios, pieces = forward_block(
        query_rows,
        query_feat,
        grad_rows,
        key_ext,
        value_ext,
        feat_ext,
        labels,
        label_ext,
        windows,
        carry,
    )
    summary = unpacked(
        carried_in(
            packed(query_summary(query_feat, grad_rows, labels, ratios, deltas)), "seq", reach, True
        ),
        heads,
        feat,
    )
    weight_low, score_grad, kernel_grad, kernel_scaled = pieces
    key_full, value_full, kfeat_full = key_side(
        query_rows, query_feat, grad_rows, weight_low, score_grad, kernel_grad, kernel_scaled
    )
    rim = jnp.concatenate([key_full[:WMAX], value_full[:WMAX], kfeat_full[:WMAX]], axis=1)
    rim = passed_along(rim.astype(jnp.bfloat16), "seq", -1).astype(jnp.float32)
    back_key, back_value, back_feat = (
        rim[:, :heads],
        rim[:, heads : 2 * heads],
        rim[:, 2 * heads :],
    )
    key_grad = key_full[WMAX:]
    value_grad = value_full[WMAX:]
    kfeat_grad = kfeat_full[WMAX:]
    key_grad = jnp.concatenate([key_grad[:tail], key_grad[tail:] + back_key], axis=0)
    value_grad = jnp.concatenate([value_grad[:tail], value_grad[tail:] + back_value], axis=0)
    kfeat_grad = jnp.concatenate([kfeat_grad[:tail], kfeat_grad[tail:] + back_feat], axis=0)
    value_grad, kfeat_grad = apply_reverse(
        value_grad, kfeat_grad, key_feat, value_rows, labels, summary
    )
    return (
        query_grad.reshape(rows, heads * head_dim).astype(jnp.bfloat16),
        key_grad.reshape(rows, heads * head_dim).astype(jnp.bfloat16),
        value_grad.reshape(rows, heads * head_dim).astype(jnp.bfloat16),
        feat_grad.reshape(rows, heads * feat).astype(jnp.bfloat16),
        kfeat_grad.reshape(rows, heads * feat).astype(jnp.bfloat16),
    )


def solution(mesh):
    in_specs = (
        P(("group", "seq"), None),
        P(("group", "seq"), None),
        P(("group", "seq"), None),
        P(("group", "seq"), None),
        P(("group", "seq"), None),
        P(("group", "seq"), None),
        P(("group", "seq")),
        P("group"),
    )
    out_specs = (
        P(("group", "seq"), None),
        P(("group", "seq"), None),
        P(("group", "seq"), None),
        P(("group", "seq"), None),
        P(("group", "seq"), None),
    )
    return jax.shard_map(
        per_device, mesh=mesh, in_specs=in_specs, out_specs=out_specs, check_vma=False
    )
```

```python
import math

import jax
import jax.numpy as jnp
from jax import lax
from jax.sharding import PartitionSpec as P

WMAX = 64
STREAMS = 2


def passed_along(value, axis, steps):
    count = lax.axis_size(axis)
    leading, last = (max(0, -steps), min(count, count - steps))
    return lax.ppermute(value, axis, [(source, source + steps) for source in range(leading, last)])


def packed(summary):
    state, total, mark = summary
    heads, feat, width = state.shape
    half = heads // 2
    marks = jnp.full((2, 1, width), mark, jnp.float32)
    rows = [state.reshape(2, half * feat, width), total.reshape(2, half, width), marks]
    return jnp.concatenate(rows, axis=1)


def unpacked(payload, heads, feat):
    width = payload.shape[2]
    half = heads // 2
    state = payload[:, : half * feat].reshape(heads, feat, width)
    total = payload[:, half * feat : half * feat + half].reshape(heads, width)
    mark = payload[0, half * feat + half, 0].astype(jnp.int32)
    return (state, total, mark)


def join_packed(earlier, later):
    at = later.shape[-2] - 1
    mark_e, mark_l = (earlier[..., at : at + 1, :1], later[..., at : at + 1, :1])
    keep = ((mark_e == mark_l) | (mark_l == 0)).astype(jnp.float32)
    mark = jnp.where(mark_l == 0, mark_e, mark_l)
    row = lax.broadcasted_iota(jnp.int32, later.shape, later.ndim - 2)
    return jnp.where(row == at, mark, later + keep * earlier)


def swapped(value, axis):
    count = lax.axis_size(axis)
    pairs = [(device, device ^ 1) for device in range(count)]
    return lax.ppermute(value, axis, pairs)


def carried_in(value, axis, reach, backward):
    step = -1 if backward else 1
    parity = lax.axis_index(axis) % 2
    is_first = parity == (1 if backward else 0)
    own_half = lax.dynamic_index_in_dim(value, parity, 0, keepdims=False)
    other_half = lax.dynamic_index_in_dim(value, 1 - parity, 0, keepdims=False)
    partner_half = swapped(other_half, axis)
    earlier = jnp.where(is_first, own_half, partner_half)
    later = jnp.where(is_first, partner_half, own_half)
    chip = join_packed(earlier, later)
    chips = (reach + 1) // 2
    total = passed_along(chip, axis, 2 * step)
    length = 1
    if chips >= 2:
        total = join_packed(passed_along(chip, axis, 4 * step), total)
        length = 2
    while length < chips:
        total = join_packed(passed_along(total, axis, 2 * length * step), total)
        length *= 2
    extended = join_packed(total, earlier)
    mine = jnp.where(is_first, total, extended)
    theirs = swapped(jnp.where(is_first, extended, total), axis)
    return jnp.where(parity == 0, jnp.stack([mine, theirs]), jnp.stack([theirs, mine]))


def quick_product(form, left, right):
    return jnp.einsum(form, left, right, preferred_element_type=jnp.float32)


def exact_product(form, left, right):
    return jnp.einsum(
        form,
        left.astype(jnp.float32),
        right.astype(jnp.float32),
        precision=lax.Precision.HIGHEST,
        preferred_element_type=jnp.float32,
    )


def pair_masks(labels_q, labels_k, windows, offset):
    distance = (
        jnp.arange(labels_q.shape[0], dtype=jnp.int32)[:, None]
        + offset
        - jnp.arange(labels_k.shape[0], dtype=jnp.int32)[None, :]
    )
    matched = (labels_q[:, None] == labels_k[None, :]) & (labels_q[:, None] > 0) & (distance >= 0)
    inside = matched[None] & (distance[None] < windows[:, None, None])
    is_local = (jnp.arange(labels_k.shape[0], dtype=jnp.int32) >= offset)[None, None, :]
    far_sign = jnp.where(
        is_local, (matched[None] & ~inside).astype(jnp.float32), -inside.astype(jnp.float32)
    )
    return (inside, far_sign)


def pair_scores(query_rows, query_feat, key_ext, feat_ext, labels_q, labels_k, windows, offset):
    inside, far_sign = pair_masks(labels_q, labels_k, windows, offset)
    scale = 1.0 / math.sqrt(query_rows.shape[2])
    score = quick_product("thd,ehd->hte", query_rows, key_ext) * scale
    kernel = quick_product("thf,ehf->hte", query_feat, feat_ext) * far_sign
    return (inside, far_sign, score, kernel)


def pair_grads(probability, kernel, far_sign, ratios, deltas, grad_rows, value_ext):
    weight_grad = quick_product("thd,ehd->hte", grad_rows, value_ext) - deltas[:, :, None]
    score_grad = (probability * weight_grad).astype(jnp.bfloat16)
    kernel_grad = weight_grad * ratios[:, :, None] * far_sign
    return (score_grad, kernel_grad, kernel * ratios[:, :, None])


def key_side(query_rows, query_feat, grad_rows, weight_low, score_grad, kernel_grad, kernel_scaled):
    scale = 1.0 / math.sqrt(query_rows.shape[2])
    key_grad = quick_product("hte,thd->ehd", score_grad, query_rows) * scale
    value_grad = quick_product("hte,thd->ehd", weight_low, grad_rows) + exact_product(
        "hte,thd->ehd", kernel_scaled, grad_rows
    )
    kfeat_grad = exact_product("hte,thf->ehf", kernel_grad, query_feat)
    return (key_grad, value_grad, kfeat_grad)


def forward_block(
    query_rows,
    query_feat,
    grad_rows,
    key_ext,
    value_ext,
    feat_ext,
    labels_q,
    labels_k,
    windows,
    carry,
):
    carry_state, carry_sum, carry_mark = carry
    offset = key_ext.shape[0] - query_rows.shape[0]
    scale = 1.0 / math.sqrt(query_rows.shape[2])
    inside, far_sign, score, kernel = pair_scores(
        query_rows, query_feat, key_ext, feat_ext, labels_q, labels_k, windows, offset
    )
    maxima = jnp.max(jnp.where(inside, score, -jnp.inf), axis=2)
    shrink = jnp.exp(-maxima)
    carry_on = (labels_q == carry_mark).astype(jnp.float32)
    carry_den = exact_product("thf,hf->ht", query_feat, carry_sum) * carry_on[None, :]
    carry_num = exact_product("thf,hfd->htd", query_feat, carry_state) * carry_on[None, :, None]
    powered = jnp.where(inside, jnp.exp(score - maxima[:, :, None]), 0.0)
    denominator = jnp.sum(powered, axis=2) + shrink * (jnp.sum(kernel, axis=2) + carry_den)
    ratios = shrink / denominator
    probability = powered / denominator[:, :, None]
    weight_low = probability.astype(jnp.bfloat16)
    attended = quick_product("hte,ehd->htd", weight_low, value_ext) + ratios[:, :, None] * (
        exact_product("hte,ehd->htd", kernel, value_ext) + carry_num
    )
    grad_wide = grad_rows.astype(jnp.float32)
    deltas = jnp.sum(jnp.transpose(grad_wide, (1, 0, 2)) * attended, axis=2)
    score_grad, kernel_grad, kernel_scaled = pair_grads(
        probability, kernel, far_sign, ratios, deltas, grad_rows, value_ext
    )
    query_grad = quick_product("hte,ehd->thd", score_grad, key_ext) * scale
    carry_term = (
        exact_product("hfd,thd->thf", carry_state, grad_rows)
        - deltas.T[:, :, None] * carry_sum[None]
    )
    feat_grad = (
        exact_product("hte,ehf->thf", kernel_grad, feat_ext)
        + (carry_on[:, None] * ratios.T)[:, :, None] * carry_term
    )
    return (
        query_grad,
        feat_grad,
        maxima,
        denominator,
        deltas,
        ratios,
        (weight_low, score_grad, kernel_grad, kernel_scaled),
    )


def key_summary(key_feat, value_rows, labels):
    keep = labels == labels[-1]
    state = quick_product(
        "thf,thd->hfd", key_feat * keep.astype(jnp.bfloat16)[:, None, None], value_rows
    )
    total = jnp.sum(key_feat.astype(jnp.float32) * keep.astype(jnp.float32)[:, None, None], axis=0)
    return (state, total, labels[-1])


def query_summary(query_feat, grad_rows, labels, ratios, deltas):
    use = (labels == labels[0]).astype(jnp.float32)[:, None] * ratios.T
    weighted = query_feat.astype(jnp.float32) * use[:, :, None]
    state = exact_product("thf,thd->hfd", weighted, grad_rows)
    total = jnp.sum(weighted * deltas.T[:, :, None], axis=0)
    return (state, total, labels[0])


def combine_pair(earlier, later):
    keep = ((earlier[2] == later[2]) | (later[2] == 0)).astype(jnp.float32)
    state = later[0] + keep.reshape(keep.shape + (1, 1, 1)) * earlier[0]
    total = later[1] + keep.reshape(keep.shape + (1, 1)) * earlier[1]
    mark = jnp.where(later[2] == 0, earlier[2], later[2])
    return (state, total, mark)


def apply_reverse(value_grad, kfeat_grad, key_feat, value_rows, labels, summary):
    state, total, mark = summary
    use = (labels == mark).astype(jnp.float32)[:, None, None]
    value_grad = value_grad + use * exact_product("hfd,thf->thd", state, key_feat)
    kfeat_grad = kfeat_grad + use * (exact_product("hfd,thd->thf", state, value_rows) - total[None])
    return (value_grad, kfeat_grad)


def per_device(queries, keys, values, out_grad, query_feats, key_feats, segment_ids, windows):
    rows = queries.shape[0]
    heads = windows.shape[0]
    head_dim = queries.shape[1] // heads
    feat = query_feats.shape[1] // heads
    tail = rows - WMAX
    query_rows = queries.reshape(rows, heads, head_dim)
    key_rows = keys.reshape(rows, heads, head_dim)
    value_rows = values.reshape(rows, heads, head_dim)
    grad_rows = out_grad.reshape(rows, heads, head_dim)
    query_feat = query_feats.reshape(rows, heads, feat)
    key_feat = key_feats.reshape(rows, heads, feat)
    labels = segment_ids + 1
    edge = jnp.concatenate(
        [
            keys[tail:],
            values[tail:],
            key_feats[tail:],
            jnp.broadcast_to(labels[tail:, None], (WMAX, 128)).astype(keys.dtype),
        ],
        axis=1,
    )
    halo = passed_along(edge, "seq", 1)
    halo_key = halo[:, : heads * head_dim].reshape(WMAX, heads, head_dim)
    halo_value = halo[:, heads * head_dim : 2 * heads * head_dim].reshape(WMAX, heads, head_dim)
    halo_feat = halo[:, 2 * heads * head_dim : 2 * heads * head_dim + heads * feat].reshape(
        WMAX, heads, feat
    )
    halo_label = halo[:, -1].astype(jnp.int32)
    count = lax.axis_size("seq")
    longest = count * rows // 2
    reach = min(count - 1, (longest + rows - 2) // rows)
    pieces = [
        head_group(
            slice(group * heads // STREAMS, (group + 1) * heads // STREAMS),
            query_rows,
            key_rows,
            value_rows,
            grad_rows,
            query_feat,
            key_feat,
            labels,
            windows,
            (halo_key, halo_value, halo_feat, halo_label),
            reach,
        )
        for group in range(STREAMS)
    ]
    outputs = [jnp.concatenate(parts, axis=1) for parts in zip(*pieces)]
    return tuple(out.reshape(rows, -1).astype(jnp.bfloat16) for out in outputs)


def head_group(
    heads_at,
    query_rows,
    key_rows,
    value_rows,
    grad_rows,
    query_feat,
    key_feat,
    labels,
    windows,
    halo,
    reach,
):
    query_rows, key_rows, value_rows, grad_rows, query_feat, key_feat = (
        part[:, heads_at]
        for part in (query_rows, key_rows, value_rows, grad_rows, query_feat, key_feat)
    )
    halo_key, halo_value, halo_feat, halo_label = halo
    halo_key, halo_value, halo_feat = (part[:, heads_at] for part in (halo_key, halo_value, halo_feat))
    windows = windows[heads_at]
    rows, heads, feat = key_feat.shape
    tail = rows - WMAX
    carry = unpacked(
        carried_in(packed(key_summary(key_feat, value_rows, labels)), "seq", reach, False),
        heads,
        feat,
    )
    key_ext = jnp.concatenate([halo_key, key_rows], axis=0)
    value_ext = jnp.concatenate([halo_value, value_rows], axis=0)
    feat_ext = jnp.concatenate([halo_feat, key_feat], axis=0)
    label_ext = jnp.concatenate([halo_label, labels], axis=0)
    query_grad, feat_grad, maxima, denominator, deltas, ratios, pieces = forward_block(
        query_rows,
        query_feat,
        grad_rows,
        key_ext,
        value_ext,
        feat_ext,
        labels,
        label_ext,
        windows,
        carry,
    )
    summary = unpacked(
        carried_in(
            packed(query_summary(query_feat, grad_rows, labels, ratios, deltas)), "seq", reach, True
        ),
        heads,
        feat,
    )
    weight_low, score_grad, kernel_grad, kernel_scaled = pieces
    key_full, value_full, kfeat_full = key_side(
        query_rows, query_feat, grad_rows, weight_low, score_grad, kernel_grad, kernel_scaled
    )
    rim = jnp.concatenate([key_full[:WMAX], value_full[:WMAX], kfeat_full[:WMAX]], axis=1)
    rim = passed_along(rim.astype(jnp.bfloat16), "seq", -1).astype(jnp.float32)
    back_key, back_value, back_feat = (
        rim[:, :heads],
        rim[:, heads : 2 * heads],
        rim[:, 2 * heads :],
    )
    key_grad = key_full[WMAX:]
    value_grad = value_full[WMAX:]
    kfeat_grad = kfeat_full[WMAX:]
    key_grad = jnp.concatenate([key_grad[:tail], key_grad[tail:] + back_key], axis=0)
    value_grad = jnp.concatenate([value_grad[:tail], value_grad[tail:] + back_value], axis=0)
    kfeat_grad = jnp.concatenate([kfeat_grad[:tail], kfeat_grad[tail:] + back_feat], axis=0)
    value_grad, kfeat_grad = apply_reverse(
        value_grad, kfeat_grad, key_feat, value_rows, labels, summary
    )
    return (query_grad, key_grad, value_grad, feat_grad, kfeat_grad)


def solution(mesh):
    in_specs = (
        P(("group", "seq"), None),
        P(("group", "seq"), None),
        P(("group", "seq"), None),
        P(("group", "seq"), None),
        P(("group", "seq"), None),
        P(("group", "seq"), None),
        P(("group", "seq")),
        P("group"),
    )
    out_specs = (
        P(("group", "seq"), None),
        P(("group", "seq"), None),
        P(("group", "seq"), None),
        P(("group", "seq"), None),
        P(("group", "seq"), None),
    )
    return jax.shard_map(
        per_device, mesh=mesh, in_specs=in_specs, out_specs=out_specs, check_vma=False
    )
```

```python
import math

import jax
import jax.numpy as jnp
from jax import lax
from jax.sharding import PartitionSpec as P

WMAX = 64


def passed_along(value, axis, steps):
    count = lax.axis_size(axis)
    leading, last = (max(0, -steps), min(count, count - steps))
    return lax.ppermute(value, axis, [(source, source + steps) for source in range(leading, last)])


def packed(summary):
    state, total, mark = summary
    heads, feat, width = state.shape
    half = heads // 2
    marks = jnp.full((2, 1, width), mark, jnp.float32)
    rows = [state.reshape(2, half * feat, width), total.reshape(2, half, width), marks]
    return jnp.concatenate(rows, axis=1)


def unpacked(payload, heads, feat):
    width = payload.shape[2]
    half = heads // 2
    state = payload[:, : half * feat].reshape(heads, feat, width)
    total = payload[:, half * feat : half * feat + half].reshape(heads, width)
    mark = payload[0, half * feat + half, 0].astype(jnp.int32)
    return (state, total, mark)


def join_packed(earlier, later):
    at = later.shape[-2] - 1
    mark_e, mark_l = (earlier[..., at : at + 1, :1], later[..., at : at + 1, :1])
    keep = ((mark_e == mark_l) | (mark_l == 0)).astype(jnp.float32)
    mark = jnp.where(mark_l == 0, mark_e, mark_l)
    row = lax.broadcasted_iota(jnp.int32, later.shape, later.ndim - 2)
    return jnp.where(row == at, mark, later + keep * earlier)


def swapped(value, axis):
    count = lax.axis_size(axis)
    pairs = [(device, device ^ 1) for device in range(count)]
    return lax.ppermute(value, axis, pairs)


def carried_in(value, axis, reach, backward):
    step = -1 if backward else 1
    parity = lax.axis_index(axis) % 2
    is_first = parity == (1 if backward else 0)
    own_half = lax.dynamic_index_in_dim(value, parity, 0, keepdims=False)
    other_half = lax.dynamic_index_in_dim(value, 1 - parity, 0, keepdims=False)
    partner_half = swapped(other_half, axis)
    earlier = jnp.where(is_first, own_half, partner_half)
    later = jnp.where(is_first, partner_half, own_half)
    chip = join_packed(earlier, later)
    chips = (reach + 1) // 2
    total = passed_along(chip, axis, 2 * step)
    length = 1
    if chips >= 2:
        total = join_packed(passed_along(chip, axis, 4 * step), total)
        length = 2
    while length < chips:
        total = join_packed(passed_along(total, axis, 2 * length * step), total)
        length *= 2
    extended = join_packed(total, earlier)
    mine = jnp.where(is_first, total, extended)
    theirs = swapped(jnp.where(is_first, extended, total), axis)
    return jnp.where(parity == 0, jnp.stack([mine, theirs]), jnp.stack([theirs, mine]))


def quick_product(form, left, right):
    return jnp.einsum(form, left, right, preferred_element_type=jnp.float32)


def exact_product(form, left, right):
    if left.dtype == jnp.bfloat16 and right.dtype != jnp.bfloat16:
        return sum(quick_product(form, left, piece) for piece in split_wide(right))
    if right.dtype == jnp.bfloat16 and left.dtype != jnp.bfloat16:
        return sum(quick_product(form, piece, right) for piece in split_wide(left))
    return jnp.einsum(
        form,
        left.astype(jnp.float32),
        right.astype(jnp.float32),
        precision=lax.Precision.HIGHEST,
        preferred_element_type=jnp.float32,
    )


def split_wide(value):
    value = value.astype(jnp.float32)
    high = value.astype(jnp.bfloat16)
    rest = value - high.astype(jnp.float32)
    middle = rest.astype(jnp.bfloat16)
    low = (rest - middle.astype(jnp.float32)).astype(jnp.bfloat16)
    return (high, middle, low)


def pair_masks(labels_q, labels_k, windows, offset):
    distance = (
        jnp.arange(labels_q.shape[0], dtype=jnp.int32)[:, None]
        + offset
        - jnp.arange(labels_k.shape[0], dtype=jnp.int32)[None, :]
    )
    matched = (labels_q[:, None] == labels_k[None, :]) & (labels_q[:, None] > 0) & (distance >= 0)
    inside = matched[None] & (distance[None] < windows[:, None, None])
    is_local = (jnp.arange(labels_k.shape[0], dtype=jnp.int32) >= offset)[None, None, :]
    far_sign = jnp.where(
        is_local, (matched[None] & ~inside).astype(jnp.float32), -inside.astype(jnp.float32)
    )
    return (inside, far_sign)


def pair_scores(query_rows, query_feat, key_ext, feat_ext, labels_q, labels_k, windows, offset):
    inside, far_sign = pair_masks(labels_q, labels_k, windows, offset)
    scale = 1.0 / math.sqrt(query_rows.shape[2])
    score = quick_product("thd,ehd->hte", query_rows, key_ext) * scale
    kernel = quick_product("thf,ehf->hte", query_feat, feat_ext) * far_sign
    return (inside, far_sign, score, kernel)


def pair_grads(probability, kernel, far_sign, ratios, deltas, grad_rows, value_ext):
    weight_grad = quick_product("thd,ehd->hte", grad_rows, value_ext) - deltas[:, :, None]
    score_grad = (probability * weight_grad).astype(jnp.bfloat16)
    kernel_grad = weight_grad * ratios[:, :, None] * far_sign
    return (score_grad, kernel_grad, kernel * ratios[:, :, None])


def key_side(query_rows, query_feat, grad_rows, weight_low, score_grad, kernel_grad, kernel_scaled):
    scale = 1.0 / math.sqrt(query_rows.shape[2])
    key_grad = quick_product("hte,thd->ehd", score_grad, query_rows) * scale
    value_grad = quick_product("hte,thd->ehd", weight_low, grad_rows) + exact_product(
        "hte,thd->ehd", kernel_scaled, grad_rows
    )
    kfeat_grad = exact_product("hte,thf->ehf", kernel_grad, query_feat)
    return (key_grad, value_grad, kfeat_grad)


def forward_block(
    query_rows,
    query_feat,
    grad_rows,
    key_ext,
    value_ext,
    feat_ext,
    labels_q,
    labels_k,
    windows,
    carry,
):
    carry_state, carry_sum, carry_mark = carry
    offset = key_ext.shape[0] - query_rows.shape[0]
    scale = 1.0 / math.sqrt(query_rows.shape[2])
    inside, far_sign, score, kernel = pair_scores(
        query_rows, query_feat, key_ext, feat_ext, labels_q, labels_k, windows, offset
    )
    maxima = jnp.max(jnp.where(inside, score, -jnp.inf), axis=2)
    shrink = jnp.exp(-maxima)
    carry_on = (labels_q == carry_mark).astype(jnp.float32)
    carry_den = exact_product("thf,hf->ht", query_feat, carry_sum) * carry_on[None, :]
    carry_num = exact_product("thf,hfd->htd", query_feat, carry_state) * carry_on[None, :, None]
    powered = jnp.where(inside, jnp.exp(score - maxima[:, :, None]), 0.0)
    denominator = jnp.sum(powered, axis=2) + shrink * (jnp.sum(kernel, axis=2) + carry_den)
    ratios = shrink / denominator
    probability = powered / denominator[:, :, None]
    weight_low = probability.astype(jnp.bfloat16)
    attended = quick_product("hte,ehd->htd", weight_low, value_ext) + ratios[:, :, None] * (
        exact_product("hte,ehd->htd", kernel, value_ext) + carry_num
    )
    grad_wide = grad_rows.astype(jnp.float32)
    deltas = jnp.sum(jnp.transpose(grad_wide, (1, 0, 2)) * attended, axis=2)
    score_grad, kernel_grad, kernel_scaled = pair_grads(
        probability, kernel, far_sign, ratios, deltas, grad_rows, value_ext
    )
    query_grad = quick_product("hte,ehd->thd", score_grad, key_ext) * scale
    carry_term = (
        exact_product("hfd,thd->thf", carry_state, grad_rows)
        - deltas.T[:, :, None] * carry_sum[None]
    )
    feat_grad = (
        exact_product("hte,ehf->thf", kernel_grad, feat_ext)
        + (carry_on[:, None] * ratios.T)[:, :, None] * carry_term
    )
    return (
        query_grad,
        feat_grad,
        maxima,
        denominator,
        deltas,
        ratios,
        (weight_low, score_grad, kernel_grad, kernel_scaled),
    )


def key_summary(key_feat, value_rows, labels):
    keep = labels == labels[-1]
    state = quick_product(
        "thf,thd->hfd", key_feat * keep.astype(jnp.bfloat16)[:, None, None], value_rows
    )
    total = jnp.sum(key_feat.astype(jnp.float32) * keep.astype(jnp.float32)[:, None, None], axis=0)
    return (state, total, labels[-1])


def query_summary(query_feat, grad_rows, labels, ratios, deltas):
    use = (labels == labels[0]).astype(jnp.float32)[:, None] * ratios.T
    weighted = query_feat.astype(jnp.float32) * use[:, :, None]
    state = exact_product("thf,thd->hfd", weighted, grad_rows)
    total = jnp.sum(weighted * deltas.T[:, :, None], axis=0)
    return (state, total, labels[0])


def combine_pair(earlier, later):
    keep = ((earlier[2] == later[2]) | (later[2] == 0)).astype(jnp.float32)
    state = later[0] + keep.reshape(keep.shape + (1, 1, 1)) * earlier[0]
    total = later[1] + keep.reshape(keep.shape + (1, 1)) * earlier[1]
    mark = jnp.where(later[2] == 0, earlier[2], later[2])
    return (state, total, mark)


def apply_reverse(value_grad, kfeat_grad, key_feat, value_rows, labels, summary):
    state, total, mark = summary
    use = (labels == mark).astype(jnp.float32)[:, None, None]
    value_grad = value_grad + use * exact_product("hfd,thf->thd", state, key_feat)
    kfeat_grad = kfeat_grad + use * (exact_product("hfd,thd->thf", state, value_rows) - total[None])
    return (value_grad, kfeat_grad)


def per_device(queries, keys, values, out_grad, query_feats, key_feats, segment_ids, windows):
    rows = queries.shape[0]
    heads = windows.shape[0]
    head_dim = queries.shape[1] // heads
    feat = query_feats.shape[1] // heads
    tail = rows - WMAX
    query_rows = queries.reshape(rows, heads, head_dim)
    key_rows = keys.reshape(rows, heads, head_dim)
    value_rows = values.reshape(rows, heads, head_dim)
    grad_rows = out_grad.reshape(rows, heads, head_dim)
    query_feat = query_feats.reshape(rows, heads, feat)
    key_feat = key_feats.reshape(rows, heads, feat)
    labels = segment_ids + 1
    edge = jnp.concatenate(
        [
            keys[tail:],
            values[tail:],
            key_feats[tail:],
            jnp.broadcast_to(labels[tail:, None], (WMAX, 128)).astype(keys.dtype),
        ],
        axis=1,
    )
    halo = passed_along(edge, "seq", 1)
    halo_key = halo[:, : heads * head_dim].reshape(WMAX, heads, head_dim)
    halo_value = halo[:, heads * head_dim : 2 * heads * head_dim].reshape(WMAX, heads, head_dim)
    halo_feat = halo[:, 2 * heads * head_dim : 2 * heads * head_dim + heads * feat].reshape(
        WMAX, heads, feat
    )
    halo_label = halo[:, -1].astype(jnp.int32)
    count = lax.axis_size("seq")
    longest = count * rows // 2
    reach = min(count - 1, (longest + rows - 2) // rows)
    carry = unpacked(
        carried_in(packed(key_summary(key_feat, value_rows, labels)), "seq", reach, False),
        heads,
        feat,
    )
    key_ext = jnp.concatenate([halo_key, key_rows], axis=0)
    value_ext = jnp.concatenate([halo_value, value_rows], axis=0)
    feat_ext = jnp.concatenate([halo_feat, key_feat], axis=0)
    label_ext = jnp.concatenate([halo_label, labels], axis=0)
    query_grad, feat_grad, maxima, denominator, deltas, ratios, pieces = forward_block(
        query_rows,
        query_feat,
        grad_rows,
        key_ext,
        value_ext,
        feat_ext,
        labels,
        label_ext,
        windows,
        carry,
    )
    summary = unpacked(
        carried_in(
            packed(query_summary(query_feat, grad_rows, labels, ratios, deltas)), "seq", reach, True
        ),
        heads,
        feat,
    )
    weight_low, score_grad, kernel_grad, kernel_scaled = pieces
    key_full, value_full, kfeat_full = key_side(
        query_rows, query_feat, grad_rows, weight_low, score_grad, kernel_grad, kernel_scaled
    )
    rim = jnp.concatenate([key_full[:WMAX], value_full[:WMAX], kfeat_full[:WMAX]], axis=1)
    rim = passed_along(rim.astype(jnp.bfloat16), "seq", -1).astype(jnp.float32)
    back_key, back_value, back_feat = (
        rim[:, :heads],
        rim[:, heads : 2 * heads],
        rim[:, 2 * heads :],
    )
    key_grad = key_full[WMAX:]
    value_grad = value_full[WMAX:]
    kfeat_grad = kfeat_full[WMAX:]
    key_grad = jnp.concatenate([key_grad[:tail], key_grad[tail:] + back_key], axis=0)
    value_grad = jnp.concatenate([value_grad[:tail], value_grad[tail:] + back_value], axis=0)
    kfeat_grad = jnp.concatenate([kfeat_grad[:tail], kfeat_grad[tail:] + back_feat], axis=0)
    value_grad, kfeat_grad = apply_reverse(
        value_grad, kfeat_grad, key_feat, value_rows, labels, summary
    )
    return (
        query_grad.reshape(rows, heads * head_dim).astype(jnp.bfloat16),
        key_grad.reshape(rows, heads * head_dim).astype(jnp.bfloat16),
        value_grad.reshape(rows, heads * head_dim).astype(jnp.bfloat16),
        feat_grad.reshape(rows, heads * feat).astype(jnp.bfloat16),
        kfeat_grad.reshape(rows, heads * feat).astype(jnp.bfloat16),
    )


def solution(mesh):
    in_specs = (
        P(("group", "seq"), None),
        P(("group", "seq"), None),
        P(("group", "seq"), None),
        P(("group", "seq"), None),
        P(("group", "seq"), None),
        P(("group", "seq"), None),
        P(("group", "seq")),
        P("group"),
    )
    out_specs = (
        P(("group", "seq"), None),
        P(("group", "seq"), None),
        P(("group", "seq"), None),
        P(("group", "seq"), None),
        P(("group", "seq"), None),
    )
    return jax.shard_map(
        per_device, mesh=mesh, in_specs=in_specs, out_specs=out_specs, check_vma=False
    )
```

```python
import math

import jax
import jax.numpy as jnp
from jax import lax
from jax.sharding import PartitionSpec as P

WMAX = 64


def passed_along(value, axis, steps):
    count = lax.axis_size(axis)
    leading, last = (max(0, -steps), min(count, count - steps))
    return lax.ppermute(value, axis, [(source, source + steps) for source in range(leading, last)])


def packed(summary):
    state, total, mark = summary
    heads, feat, width = state.shape
    half = heads // 2
    marks = jnp.full((2, 1, width), mark, jnp.float32)
    rows = [state.reshape(2, half * feat, width), total.reshape(2, half, width), marks]
    return jnp.concatenate(rows, axis=1)


def unpacked(payload, heads, feat):
    width = payload.shape[2]
    half = heads // 2
    state = payload[:, : half * feat].reshape(heads, feat, width)
    total = payload[:, half * feat : half * feat + half].reshape(heads, width)
    mark = payload[0, half * feat + half, 0].astype(jnp.int32)
    return (state, total, mark)


def join_packed(earlier, later):
    at = later.shape[-2] - 1
    mark_e, mark_l = (earlier[..., at : at + 1, :1], later[..., at : at + 1, :1])
    keep = ((mark_e == mark_l) | (mark_l == 0)).astype(jnp.float32)
    mark = jnp.where(mark_l == 0, mark_e, mark_l)
    row = lax.broadcasted_iota(jnp.int32, later.shape, later.ndim - 2)
    return jnp.where(row == at, mark, later + keep * earlier)


def swapped(value, axis):
    count = lax.axis_size(axis)
    pairs = [(device, device ^ 1) for device in range(count)]
    return lax.ppermute(value, axis, pairs)


def carried_in(value, axis, reach, backward, rider=None):
    step = -1 if backward else 1
    parity = lax.axis_index(axis) % 2
    is_first = parity == (1 if backward else 0)
    own_half = lax.dynamic_index_in_dim(value, parity, 0, keepdims=False)
    other_half = lax.dynamic_index_in_dim(value, 1 - parity, 0, keepdims=False)
    partner_half = swapped(other_half, axis)
    if rider is not None:
        rider, partner_half = lax.optimization_barrier((rider, partner_half))
        rider = passed_along(rider, axis, step)
    earlier = jnp.where(is_first, own_half, partner_half)
    later = jnp.where(is_first, partner_half, own_half)
    chip = join_packed(earlier, later)
    chips = (reach + 1) // 2
    total = passed_along(chip, axis, 2 * step)
    length = 1
    if chips >= 2:
        total = join_packed(passed_along(chip, axis, 4 * step), total)
        length = 2
    while length < chips:
        total = join_packed(passed_along(total, axis, 2 * length * step), total)
        length *= 2
    extended = join_packed(total, earlier)
    mine = jnp.where(is_first, total, extended)
    theirs = swapped(jnp.where(is_first, extended, total), axis)
    whole = jnp.where(parity == 0, jnp.stack([mine, theirs]), jnp.stack([theirs, mine]))
    return whole if rider is None else (whole, rider)


def quick_product(form, left, right):
    return jnp.einsum(form, left, right, preferred_element_type=jnp.float32)


def exact_product(form, left, right):
    return jnp.einsum(
        form,
        left.astype(jnp.float32),
        right.astype(jnp.float32),
        precision=lax.Precision.HIGHEST,
        preferred_element_type=jnp.float32,
    )


def pair_masks(labels_q, labels_k, windows, offset):
    distance = (
        jnp.arange(labels_q.shape[0], dtype=jnp.int32)[:, None]
        + offset
        - jnp.arange(labels_k.shape[0], dtype=jnp.int32)[None, :]
    )
    matched = (labels_q[:, None] == labels_k[None, :]) & (labels_q[:, None] > 0) & (distance >= 0)
    inside = matched[None] & (distance[None] < windows[:, None, None])
    is_local = (jnp.arange(labels_k.shape[0], dtype=jnp.int32) >= offset)[None, None, :]
    far_sign = jnp.where(
        is_local, (matched[None] & ~inside).astype(jnp.float32), -inside.astype(jnp.float32)
    )
    return (inside, far_sign)


def pair_scores(query_rows, query_feat, key_ext, feat_ext, labels_q, labels_k, windows, offset):
    inside, far_sign = pair_masks(labels_q, labels_k, windows, offset)
    scale = 1.0 / math.sqrt(query_rows.shape[2])
    score = quick_product("thd,ehd->hte", query_rows, key_ext) * scale
    kernel = quick_product("thf,ehf->hte", query_feat, feat_ext) * far_sign
    return (inside, far_sign, score, kernel)


def pair_grads(probability, kernel, far_sign, ratios, deltas, grad_rows, value_ext):
    weight_grad = quick_product("thd,ehd->hte", grad_rows, value_ext) - deltas[:, :, None]
    score_grad = (probability * weight_grad).astype(jnp.bfloat16)
    kernel_grad = weight_grad * ratios[:, :, None] * far_sign
    return (score_grad, kernel_grad, kernel * ratios[:, :, None])


def key_side(query_rows, query_feat, grad_rows, weight_low, score_grad, kernel_grad, kernel_scaled):
    scale = 1.0 / math.sqrt(query_rows.shape[2])
    key_grad = quick_product("hte,thd->ehd", score_grad, query_rows) * scale
    value_grad = quick_product("hte,thd->ehd", weight_low, grad_rows) + exact_product(
        "hte,thd->ehd", kernel_scaled, grad_rows
    )
    kfeat_grad = exact_product("hte,thf->ehf", kernel_grad, query_feat)
    return (key_grad, value_grad, kfeat_grad)


def forward_block(
    query_rows,
    query_feat,
    grad_rows,
    key_ext,
    value_ext,
    feat_ext,
    labels_q,
    labels_k,
    windows,
    carry,
):
    carry_state, carry_sum, carry_mark = carry
    offset = key_ext.shape[0] - query_rows.shape[0]
    scale = 1.0 / math.sqrt(query_rows.shape[2])
    inside, far_sign, score, kernel = pair_scores(
        query_rows, query_feat, key_ext, feat_ext, labels_q, labels_k, windows, offset
    )
    maxima = jnp.max(jnp.where(inside, score, -jnp.inf), axis=2)
    shrink = jnp.exp(-maxima)
    carry_on = (labels_q == carry_mark).astype(jnp.float32)
    carry_den = exact_product("thf,hf->ht", query_feat, carry_sum) * carry_on[None, :]
    carry_num = exact_product("thf,hfd->htd", query_feat, carry_state) * carry_on[None, :, None]
    powered = jnp.where(inside, jnp.exp(score - maxima[:, :, None]), 0.0)
    denominator = jnp.sum(powered, axis=2) + shrink * (jnp.sum(kernel, axis=2) + carry_den)
    ratios = shrink / denominator
    probability = powered / denominator[:, :, None]
    weight_low = probability.astype(jnp.bfloat16)
    attended = quick_product("hte,ehd->htd", weight_low, value_ext) + ratios[:, :, None] * (
        exact_product("hte,ehd->htd", kernel, value_ext) + carry_num
    )
    grad_wide = grad_rows.astype(jnp.float32)
    deltas = jnp.sum(jnp.transpose(grad_wide, (1, 0, 2)) * attended, axis=2)
    score_grad, kernel_grad, kernel_scaled = pair_grads(
        probability, kernel, far_sign, ratios, deltas, grad_rows, value_ext
    )
    query_grad = quick_product("hte,ehd->thd", score_grad, key_ext) * scale
    carry_term = (
        exact_product("hfd,thd->thf", carry_state, grad_rows)
        - deltas.T[:, :, None] * carry_sum[None]
    )
    feat_grad = (
        exact_product("hte,ehf->thf", kernel_grad, feat_ext)
        + (carry_on[:, None] * ratios.T)[:, :, None] * carry_term
    )
    return (
        query_grad,
        feat_grad,
        maxima,
        denominator,
        deltas,
        ratios,
        (weight_low, score_grad, kernel_grad, kernel_scaled),
    )


def key_summary(key_feat, value_rows, labels):
    keep = labels == labels[-1]
    state = quick_product(
        "thf,thd->hfd", key_feat * keep.astype(jnp.bfloat16)[:, None, None], value_rows
    )
    total = jnp.sum(key_feat.astype(jnp.float32) * keep.astype(jnp.float32)[:, None, None], axis=0)
    return (state, total, labels[-1])


def query_summary(query_feat, grad_rows, labels, ratios, deltas):
    use = (labels == labels[0]).astype(jnp.float32)[:, None] * ratios.T
    weighted = query_feat.astype(jnp.float32) * use[:, :, None]
    state = exact_product("thf,thd->hfd", weighted, grad_rows)
    total = jnp.sum(weighted * deltas.T[:, :, None], axis=0)
    return (state, total, labels[0])


def combine_pair(earlier, later):
    keep = ((earlier[2] == later[2]) | (later[2] == 0)).astype(jnp.float32)
    state = later[0] + keep.reshape(keep.shape + (1, 1, 1)) * earlier[0]
    total = later[1] + keep.reshape(keep.shape + (1, 1)) * earlier[1]
    mark = jnp.where(later[2] == 0, earlier[2], later[2])
    return (state, total, mark)


def apply_reverse(value_grad, kfeat_grad, key_feat, value_rows, labels, summary):
    state, total, mark = summary
    use = (labels == mark).astype(jnp.float32)[:, None, None]
    value_grad = value_grad + use * exact_product("hfd,thf->thd", state, key_feat)
    kfeat_grad = kfeat_grad + use * (exact_product("hfd,thd->thf", state, value_rows) - total[None])
    return (value_grad, kfeat_grad)


def per_device(queries, keys, values, out_grad, query_feats, key_feats, segment_ids, windows):
    rows = queries.shape[0]
    heads = windows.shape[0]
    head_dim = queries.shape[1] // heads
    feat = query_feats.shape[1] // heads
    tail = rows - WMAX
    query_rows = queries.reshape(rows, heads, head_dim)
    key_rows = keys.reshape(rows, heads, head_dim)
    value_rows = values.reshape(rows, heads, head_dim)
    grad_rows = out_grad.reshape(rows, heads, head_dim)
    query_feat = query_feats.reshape(rows, heads, feat)
    key_feat = key_feats.reshape(rows, heads, feat)
    labels = segment_ids + 1
    edge = jnp.concatenate(
        [
            keys[tail:],
            values[tail:],
            key_feats[tail:],
            jnp.broadcast_to(labels[tail:, None], (WMAX, 128)).astype(keys.dtype),
        ],
        axis=1,
    )
    count = lax.axis_size("seq")
    longest = count * rows // 2
    reach = min(count - 1, (longest + rows - 2) // rows)
    carried, halo = carried_in(
        packed(key_summary(key_feat, value_rows, labels)), "seq", reach, False, edge
    )
    carry = unpacked(carried, heads, feat)
    halo_key = halo[:, : heads * head_dim].reshape(WMAX, heads, head_dim)
    halo_value = halo[:, heads * head_dim : 2 * heads * head_dim].reshape(WMAX, heads, head_dim)
    halo_feat = halo[:, 2 * heads * head_dim : 2 * heads * head_dim + heads * feat].reshape(
        WMAX, heads, feat
    )
    halo_label = halo[:, -1].astype(jnp.int32)
    key_ext = jnp.concatenate([halo_key, key_rows], axis=0)
    value_ext = jnp.concatenate([halo_value, value_rows], axis=0)
    feat_ext = jnp.concatenate([halo_feat, key_feat], axis=0)
    label_ext = jnp.concatenate([halo_label, labels], axis=0)
    query_grad, feat_grad, maxima, denominator, deltas, ratios, pieces = forward_block(
        query_rows,
        query_feat,
        grad_rows,
        key_ext,
        value_ext,
        feat_ext,
        labels,
        label_ext,
        windows,
        carry,
    )
    summary = unpacked(
        carried_in(
            packed(query_summary(query_feat, grad_rows, labels, ratios, deltas)), "seq", reach, True
        ),
        heads,
        feat,
    )
    weight_low, score_grad, kernel_grad, kernel_scaled = pieces
    key_full, value_full, kfeat_full = key_side(
        query_rows, query_feat, grad_rows, weight_low, score_grad, kernel_grad, kernel_scaled
    )
    rim = jnp.concatenate([key_full[:WMAX], value_full[:WMAX], kfeat_full[:WMAX]], axis=1)
    rim = passed_along(rim.astype(jnp.bfloat16), "seq", -1).astype(jnp.float32)
    back_key, back_value, back_feat = (
        rim[:, :heads],
        rim[:, heads : 2 * heads],
        rim[:, 2 * heads :],
    )
    key_grad = key_full[WMAX:]
    value_grad = value_full[WMAX:]
    kfeat_grad = kfeat_full[WMAX:]
    key_grad = jnp.concatenate([key_grad[:tail], key_grad[tail:] + back_key], axis=0)
    value_grad = jnp.concatenate([value_grad[:tail], value_grad[tail:] + back_value], axis=0)
    kfeat_grad = jnp.concatenate([kfeat_grad[:tail], kfeat_grad[tail:] + back_feat], axis=0)
    value_grad, kfeat_grad = apply_reverse(
        value_grad, kfeat_grad, key_feat, value_rows, labels, summary
    )
    return (
        query_grad.reshape(rows, heads * head_dim).astype(jnp.bfloat16),
        key_grad.reshape(rows, heads * head_dim).astype(jnp.bfloat16),
        value_grad.reshape(rows, heads * head_dim).astype(jnp.bfloat16),
        feat_grad.reshape(rows, heads * feat).astype(jnp.bfloat16),
        kfeat_grad.reshape(rows, heads * feat).astype(jnp.bfloat16),
    )


def solution(mesh):
    in_specs = (
        P(("group", "seq"), None),
        P(("group", "seq"), None),
        P(("group", "seq"), None),
        P(("group", "seq"), None),
        P(("group", "seq"), None),
        P(("group", "seq"), None),
        P(("group", "seq")),
        P("group"),
    )
    out_specs = (
        P(("group", "seq"), None),
        P(("group", "seq"), None),
        P(("group", "seq"), None),
        P(("group", "seq"), None),
        P(("group", "seq"), None),
    )
    return jax.shard_map(
        per_device, mesh=mesh, in_specs=in_specs, out_specs=out_specs, check_vma=False
    )
```

```python
import math

import jax
import jax.numpy as jnp
from jax import lax
from jax.sharding import PartitionSpec as P

WMAX = 64


def passed_along(value, axis, steps):
    count = lax.axis_size(axis)
    leading, last = (max(0, -steps), min(count, count - steps))
    return lax.ppermute(value, axis, [(source, source + steps) for source in range(leading, last)])


def packed(summary):
    state, total = summary[:2]
    heads, feat, width = state.shape
    half = heads // 2
    rows = [state.reshape(2, half * feat, width), total.reshape(2, half, width)]
    return jnp.concatenate(rows, axis=1)


def unpacked(payload, mark, heads, feat):
    width = payload.shape[2]
    half = heads // 2
    state = payload[:, : half * feat].reshape(heads, feat, width)
    total = payload[:, half * feat : half * feat + half].reshape(heads, width)
    return (state, total, mark)


def join_kept(earlier, later, keep):
    return later + keep.astype(jnp.float32) * earlier


def swapped(value, axis):
    count = lax.axis_size(axis)
    pairs = [(device, device ^ 1) for device in range(count)]
    return lax.ppermute(value, axis, pairs)


def carried_in(value, ends, axis, reach, backward, rider=None):
    count = lax.axis_size(axis)
    step = -1 if backward else 1
    device = lax.axis_index(axis)
    parity = device % 2
    spot = count - 1 - device if backward else device
    chip_at = spot // 2

    def mark_at(place):
        inside = (place >= 0) & (place < count)
        real = count - 1 - place if backward else place
        found = ends[jnp.clip(real, 0, count - 1), 0 if backward else 1]
        return jnp.where(inside, found, 0)

    def chip_mark(chip):
        return mark_at(2 * chip + 1)

    def kept(far, near):
        return (far == near) | (near == 0)

    is_first = spot % 2 == 0
    own_half = lax.dynamic_index_in_dim(value, parity, 0, keepdims=False)
    other_half = lax.dynamic_index_in_dim(value, 1 - parity, 0, keepdims=False)
    partner_half = swapped(other_half, axis)
    if rider is not None:
        rider, partner_half = lax.optimization_barrier((rider, partner_half))
        rider = passed_along(rider, axis, step)
    earlier = jnp.where(is_first, own_half, partner_half)
    later = jnp.where(is_first, partner_half, own_half)
    chip = join_kept(earlier, later, kept(mark_at(2 * chip_at), mark_at(2 * chip_at + 1)))
    chips = (reach + 1) // 2
    total = passed_along(chip, axis, 2 * step)
    length = 1
    if chips >= 2:
        keep = kept(chip_mark(chip_at - 2), chip_mark(chip_at - 1))
        total = join_kept(passed_along(chip, axis, 4 * step), total, keep)
        length = 2
    while length < chips:
        keep = kept(chip_mark(chip_at - length - 1), chip_mark(chip_at - 1))
        total = join_kept(passed_along(total, axis, 2 * length * step), total, keep)
        length *= 2
    extended = join_kept(total, earlier, kept(chip_mark(chip_at - 1), mark_at(2 * chip_at)))
    mine = jnp.where(is_first, total, extended)
    theirs = swapped(jnp.where(is_first, extended, total), axis)
    whole = jnp.where(parity == 0, jnp.stack([mine, theirs]), jnp.stack([theirs, mine]))
    return (whole, mark_at(spot - 1), rider)


def quick_product(form, left, right):
    return jnp.einsum(form, left, right, preferred_element_type=jnp.float32)


def exact_product(form, left, right):
    return jnp.einsum(
        form,
        left.astype(jnp.float32),
        right.astype(jnp.float32),
        precision=lax.Precision.HIGHEST,
        preferred_element_type=jnp.float32,
    )


def pair_masks(labels_q, labels_k, windows, offset):
    distance = (
        jnp.arange(labels_q.shape[0], dtype=jnp.int32)[:, None]
        + offset
        - jnp.arange(labels_k.shape[0], dtype=jnp.int32)[None, :]
    )
    matched = (labels_q[:, None] == labels_k[None, :]) & (labels_q[:, None] > 0) & (distance >= 0)
    inside = matched[None] & (distance[None] < windows[:, None, None])
    is_local = (jnp.arange(labels_k.shape[0], dtype=jnp.int32) >= offset)[None, None, :]
    far_sign = jnp.where(
        is_local, (matched[None] & ~inside).astype(jnp.float32), -inside.astype(jnp.float32)
    )
    return (inside, far_sign)


def pair_scores(query_rows, query_feat, key_ext, feat_ext, labels_q, labels_k, windows, offset):
    inside, far_sign = pair_masks(labels_q, labels_k, windows, offset)
    scale = 1.0 / math.sqrt(query_rows.shape[2])
    score = quick_product("thd,ehd->hte", query_rows, key_ext) * scale
    kernel = quick_product("thf,ehf->hte", query_feat, feat_ext) * far_sign
    return (inside, far_sign, score, kernel)


def pair_grads(probability, kernel, far_sign, ratios, deltas, grad_rows, value_ext):
    weight_grad = quick_product("thd,ehd->hte", grad_rows, value_ext) - deltas[:, :, None]
    score_grad = (probability * weight_grad).astype(jnp.bfloat16)
    kernel_grad = weight_grad * ratios[:, :, None] * far_sign
    return (score_grad, kernel_grad, kernel * ratios[:, :, None])


def key_side(query_rows, query_feat, grad_rows, weight_low, score_grad, kernel_grad, kernel_scaled):
    scale = 1.0 / math.sqrt(query_rows.shape[2])
    key_grad = quick_product("hte,thd->ehd", score_grad, query_rows) * scale
    value_grad = quick_product("hte,thd->ehd", weight_low, grad_rows) + exact_product(
        "hte,thd->ehd", kernel_scaled, grad_rows
    )
    kfeat_grad = exact_product("hte,thf->ehf", kernel_grad, query_feat)
    return (key_grad, value_grad, kfeat_grad)


def forward_block(
    query_rows,
    query_feat,
    grad_rows,
    key_ext,
    value_ext,
    feat_ext,
    labels_q,
    labels_k,
    windows,
    carry,
):
    carry_state, carry_sum, carry_mark = carry
    offset = key_ext.shape[0] - query_rows.shape[0]
    scale = 1.0 / math.sqrt(query_rows.shape[2])
    inside, far_sign, score, kernel = pair_scores(
        query_rows, query_feat, key_ext, feat_ext, labels_q, labels_k, windows, offset
    )
    maxima = jnp.max(jnp.where(inside, score, -jnp.inf), axis=2)
    shrink = jnp.exp(-maxima)
    carry_on = (labels_q == carry_mark).astype(jnp.float32)
    carry_den = exact_product("thf,hf->ht", query_feat, carry_sum) * carry_on[None, :]
    carry_num = exact_product("thf,hfd->htd", query_feat, carry_state) * carry_on[None, :, None]
    powered = jnp.where(inside, jnp.exp(score - maxima[:, :, None]), 0.0)
    denominator = jnp.sum(powered, axis=2) + shrink * (jnp.sum(kernel, axis=2) + carry_den)
    ratios = shrink / denominator
    probability = powered / denominator[:, :, None]
    weight_low = probability.astype(jnp.bfloat16)
    attended = quick_product("hte,ehd->htd", weight_low, value_ext) + ratios[:, :, None] * (
        exact_product("hte,ehd->htd", kernel, value_ext) + carry_num
    )
    grad_wide = grad_rows.astype(jnp.float32)
    deltas = jnp.sum(jnp.transpose(grad_wide, (1, 0, 2)) * attended, axis=2)
    score_grad, kernel_grad, kernel_scaled = pair_grads(
        probability, kernel, far_sign, ratios, deltas, grad_rows, value_ext
    )
    query_grad = quick_product("hte,ehd->thd", score_grad, key_ext) * scale
    carry_term = (
        exact_product("hfd,thd->thf", carry_state, grad_rows)
        - deltas.T[:, :, None] * carry_sum[None]
    )
    feat_grad = (
        exact_product("hte,ehf->thf", kernel_grad, feat_ext)
        + (carry_on[:, None] * ratios.T)[:, :, None] * carry_term
    )
    return (
        query_grad,
        feat_grad,
        maxima,
        denominator,
        deltas,
        ratios,
        (weight_low, score_grad, kernel_grad, kernel_scaled),
    )


def key_summary(key_feat, value_rows, labels):
    keep = labels == labels[-1]
    state = quick_product(
        "thf,thd->hfd", key_feat * keep.astype(jnp.bfloat16)[:, None, None], value_rows
    )
    total = jnp.sum(key_feat.astype(jnp.float32) * keep.astype(jnp.float32)[:, None, None], axis=0)
    return (state, total, labels[-1])


def query_summary(query_feat, grad_rows, labels, ratios, deltas):
    use = (labels == labels[0]).astype(jnp.float32)[:, None] * ratios.T
    weighted = query_feat.astype(jnp.float32) * use[:, :, None]
    state = exact_product("thf,thd->hfd", weighted, grad_rows)
    total = jnp.sum(weighted * deltas.T[:, :, None], axis=0)
    return (state, total, labels[0])


def combine_pair(earlier, later):
    keep = ((earlier[2] == later[2]) | (later[2] == 0)).astype(jnp.float32)
    state = later[0] + keep.reshape(keep.shape + (1, 1, 1)) * earlier[0]
    total = later[1] + keep.reshape(keep.shape + (1, 1)) * earlier[1]
    mark = jnp.where(later[2] == 0, earlier[2], later[2])
    return (state, total, mark)


def apply_reverse(value_grad, kfeat_grad, key_feat, value_rows, labels, summary):
    state, total, mark = summary
    use = (labels == mark).astype(jnp.float32)[:, None, None]
    value_grad = value_grad + use * exact_product("hfd,thf->thd", state, key_feat)
    kfeat_grad = kfeat_grad + use * (exact_product("hfd,thd->thf", state, value_rows) - total[None])
    return (value_grad, kfeat_grad)


def per_device(queries, keys, values, out_grad, query_feats, key_feats, segment_ids, windows):
    rows = queries.shape[0]
    heads = windows.shape[0]
    head_dim = queries.shape[1] // heads
    feat = query_feats.shape[1] // heads
    tail = rows - WMAX
    query_rows = queries.reshape(rows, heads, head_dim)
    key_rows = keys.reshape(rows, heads, head_dim)
    value_rows = values.reshape(rows, heads, head_dim)
    grad_rows = out_grad.reshape(rows, heads, head_dim)
    query_feat = query_feats.reshape(rows, heads, feat)
    key_feat = key_feats.reshape(rows, heads, feat)
    labels = segment_ids + 1
    edge = jnp.concatenate(
        [
            keys[tail:],
            values[tail:],
            key_feats[tail:],
            jnp.broadcast_to(labels[tail:, None], (WMAX, 128)).astype(keys.dtype),
        ],
        axis=1,
    )
    count = lax.axis_size("seq")
    longest = count * rows // 2
    reach = min(count - 1, (longest + rows - 2) // rows)
    ends = lax.all_gather(jnp.stack([labels[0], labels[-1]]), "seq")
    carried, mark, halo = carried_in(
        packed(key_summary(key_feat, value_rows, labels)), ends, "seq", reach, False, edge
    )
    carry = unpacked(carried, mark, heads, feat)
    halo_key = halo[:, : heads * head_dim].reshape(WMAX, heads, head_dim)
    halo_value = halo[:, heads * head_dim : 2 * heads * head_dim].reshape(WMAX, heads, head_dim)
    halo_feat = halo[:, 2 * heads * head_dim : 2 * heads * head_dim + heads * feat].reshape(
        WMAX, heads, feat
    )
    halo_label = halo[:, -1].astype(jnp.int32)
    key_ext = jnp.concatenate([halo_key, key_rows], axis=0)
    value_ext = jnp.concatenate([halo_value, value_rows], axis=0)
    feat_ext = jnp.concatenate([halo_feat, key_feat], axis=0)
    label_ext = jnp.concatenate([halo_label, labels], axis=0)
    query_grad, feat_grad, maxima, denominator, deltas, ratios, pieces = forward_block(
        query_rows,
        query_feat,
        grad_rows,
        key_ext,
        value_ext,
        feat_ext,
        labels,
        label_ext,
        windows,
        carry,
    )
    summed, mark, unused = carried_in(
        packed(query_summary(query_feat, grad_rows, labels, ratios, deltas)),
        ends,
        "seq",
        reach,
        True,
    )
    summary = unpacked(summed, mark, heads, feat)
    weight_low, score_grad, kernel_grad, kernel_scaled = pieces
    key_full, value_full, kfeat_full = key_side(
        query_rows, query_feat, grad_rows, weight_low, score_grad, kernel_grad, kernel_scaled
    )
    rim = jnp.concatenate([key_full[:WMAX], value_full[:WMAX], kfeat_full[:WMAX]], axis=1)
    rim = passed_along(rim.astype(jnp.bfloat16), "seq", -1).astype(jnp.float32)
    back_key, back_value, back_feat = (
        rim[:, :heads],
        rim[:, heads : 2 * heads],
        rim[:, 2 * heads :],
    )
    key_grad = key_full[WMAX:]
    value_grad = value_full[WMAX:]
    kfeat_grad = kfeat_full[WMAX:]
    key_grad = jnp.concatenate([key_grad[:tail], key_grad[tail:] + back_key], axis=0)
    value_grad = jnp.concatenate([value_grad[:tail], value_grad[tail:] + back_value], axis=0)
    kfeat_grad = jnp.concatenate([kfeat_grad[:tail], kfeat_grad[tail:] + back_feat], axis=0)
    value_grad, kfeat_grad = apply_reverse(
        value_grad, kfeat_grad, key_feat, value_rows, labels, summary
    )
    return (
        query_grad.reshape(rows, heads * head_dim).astype(jnp.bfloat16),
        key_grad.reshape(rows, heads * head_dim).astype(jnp.bfloat16),
        value_grad.reshape(rows, heads * head_dim).astype(jnp.bfloat16),
        feat_grad.reshape(rows, heads * feat).astype(jnp.bfloat16),
        kfeat_grad.reshape(rows, heads * feat).astype(jnp.bfloat16),
    )


def solution(mesh):
    in_specs = (
        P(("group", "seq"), None),
        P(("group", "seq"), None),
        P(("group", "seq"), None),
        P(("group", "seq"), None),
        P(("group", "seq"), None),
        P(("group", "seq"), None),
        P(("group", "seq")),
        P("group"),
    )
    out_specs = (
        P(("group", "seq"), None),
        P(("group", "seq"), None),
        P(("group", "seq"), None),
        P(("group", "seq"), None),
        P(("group", "seq"), None),
    )
    return jax.shard_map(
        per_device, mesh=mesh, in_specs=in_specs, out_specs=out_specs, check_vma=False
    )
```

```python
import math

import jax
import jax.numpy as jnp
from jax import lax
from jax.sharding import PartitionSpec as P

WMAX = 64


def passed_along(value, axis, steps):
    count = lax.axis_size(axis)
    leading, last = (max(0, -steps), min(count, count - steps))
    return lax.ppermute(value, axis, [(source, source + steps) for source in range(leading, last)])


def packed(summary):
    state, total = summary[:2]
    heads, feat, width = state.shape
    half = heads // 2
    rows = [state.reshape(2, half * feat, width), total.reshape(2, half, width)]
    return jnp.concatenate(rows, axis=1)


def unpacked(payload, mark, heads, feat):
    width = payload.shape[2]
    half = heads // 2
    state = payload[:, : half * feat].reshape(heads, feat, width)
    total = payload[:, half * feat : half * feat + half].reshape(heads, width)
    return (state, total, mark)


def join_kept(earlier, later, keep):
    return later + keep.astype(jnp.float32) * earlier


def swapped(value, axis):
    count = lax.axis_size(axis)
    pairs = [(device, device ^ 1) for device in range(count)]
    return lax.ppermute(value, axis, pairs)


def carried_in(value, ends, axis, reach, backward, rider=None):
    if callable(ends):
        own = ends(None)
        partner = swapped(own, axis)
        first_keep = own[0 if backward else 1] == partner[0 if backward else 1]
    else:
        first_keep = None
    count = lax.axis_size(axis)
    step = -1 if backward else 1
    device = lax.axis_index(axis)
    parity = device % 2
    spot = count - 1 - device if backward else device
    chip_at = spot // 2

    def mark_at(place):
        inside = (place >= 0) & (place < count)
        real = count - 1 - place if backward else place
        found = ends[jnp.clip(real, 0, count - 1), 0 if backward else 1]
        return jnp.where(inside, found, 0)

    def chip_mark(chip):
        return mark_at(2 * chip + 1)

    def kept(far, near):
        return (far == near) | (near == 0)

    is_first = spot % 2 == 0
    own_half = lax.dynamic_index_in_dim(value, parity, 0, keepdims=False)
    other_half = lax.dynamic_index_in_dim(value, 1 - parity, 0, keepdims=False)
    partner_half = swapped(other_half, axis)
    if rider is not None:
        rider, partner_half = lax.optimization_barrier((rider, partner_half))
        rider = passed_along(rider, axis, step)
    earlier = jnp.where(is_first, own_half, partner_half)
    later = jnp.where(is_first, partner_half, own_half)
    if first_keep is None:
        first_keep = kept(mark_at(2 * chip_at), mark_at(2 * chip_at + 1))
    chip = join_kept(earlier, later, first_keep)
    if callable(ends):
        ends = ends(chip)
    chips = (reach + 1) // 2
    total = passed_along(chip, axis, 2 * step)
    length = 1
    if chips >= 2:
        keep = kept(chip_mark(chip_at - 2), chip_mark(chip_at - 1))
        total = join_kept(passed_along(chip, axis, 4 * step), total, keep)
        length = 2
    while length < chips:
        keep = kept(chip_mark(chip_at - length - 1), chip_mark(chip_at - 1))
        total = join_kept(passed_along(total, axis, 2 * length * step), total, keep)
        length *= 2
    extended = join_kept(total, earlier, kept(chip_mark(chip_at - 1), mark_at(2 * chip_at)))
    mine = jnp.where(is_first, total, extended)
    theirs = swapped(jnp.where(is_first, extended, total), axis)
    whole = jnp.where(parity == 0, jnp.stack([mine, theirs]), jnp.stack([theirs, mine]))
    return (whole, mark_at(spot - 1), rider, ends)


def quick_product(form, left, right):
    return jnp.einsum(form, left, right, preferred_element_type=jnp.float32)


def exact_product(form, left, right):
    return jnp.einsum(
        form,
        left.astype(jnp.float32),
        right.astype(jnp.float32),
        precision=lax.Precision.HIGHEST,
        preferred_element_type=jnp.float32,
    )


def pair_masks(labels_q, labels_k, windows, offset):
    distance = (
        jnp.arange(labels_q.shape[0], dtype=jnp.int32)[:, None]
        + offset
        - jnp.arange(labels_k.shape[0], dtype=jnp.int32)[None, :]
    )
    matched = (labels_q[:, None] == labels_k[None, :]) & (labels_q[:, None] > 0) & (distance >= 0)
    inside = matched[None] & (distance[None] < windows[:, None, None])
    is_local = (jnp.arange(labels_k.shape[0], dtype=jnp.int32) >= offset)[None, None, :]
    far_sign = jnp.where(
        is_local, (matched[None] & ~inside).astype(jnp.float32), -inside.astype(jnp.float32)
    )
    return (inside, far_sign)


def pair_scores(query_rows, query_feat, key_ext, feat_ext, labels_q, labels_k, windows, offset):
    inside, far_sign = pair_masks(labels_q, labels_k, windows, offset)
    scale = 1.0 / math.sqrt(query_rows.shape[2])
    score = quick_product("thd,ehd->hte", query_rows, key_ext) * scale
    kernel = quick_product("thf,ehf->hte", query_feat, feat_ext) * far_sign
    return (inside, far_sign, score, kernel)


def pair_grads(probability, kernel, far_sign, ratios, deltas, grad_rows, value_ext):
    weight_grad = quick_product("thd,ehd->hte", grad_rows, value_ext) - deltas[:, :, None]
    score_grad = (probability * weight_grad).astype(jnp.bfloat16)
    kernel_grad = weight_grad * ratios[:, :, None] * far_sign
    return (score_grad, kernel_grad, kernel * ratios[:, :, None])


def key_side(query_rows, query_feat, grad_rows, weight_low, score_grad, kernel_grad, kernel_scaled):
    scale = 1.0 / math.sqrt(query_rows.shape[2])
    key_grad = quick_product("hte,thd->ehd", score_grad, query_rows) * scale
    value_grad = quick_product("hte,thd->ehd", weight_low, grad_rows) + exact_product(
        "hte,thd->ehd", kernel_scaled, grad_rows
    )
    kfeat_grad = exact_product("hte,thf->ehf", kernel_grad, query_feat)
    return (key_grad, value_grad, kfeat_grad)


def forward_block(
    query_rows,
    query_feat,
    grad_rows,
    key_ext,
    value_ext,
    feat_ext,
    labels_q,
    labels_k,
    windows,
    carry,
):
    carry_state, carry_sum, carry_mark = carry
    offset = key_ext.shape[0] - query_rows.shape[0]
    scale = 1.0 / math.sqrt(query_rows.shape[2])
    inside, far_sign, score, kernel = pair_scores(
        query_rows, query_feat, key_ext, feat_ext, labels_q, labels_k, windows, offset
    )
    maxima = jnp.max(jnp.where(inside, score, -jnp.inf), axis=2)
    shrink = jnp.exp(-maxima)
    carry_on = (labels_q == carry_mark).astype(jnp.float32)
    carry_den = exact_product("thf,hf->ht", query_feat, carry_sum) * carry_on[None, :]
    carry_num = exact_product("thf,hfd->htd", query_feat, carry_state) * carry_on[None, :, None]
    powered = jnp.where(inside, jnp.exp(score - maxima[:, :, None]), 0.0)
    denominator = jnp.sum(powered, axis=2) + shrink * (jnp.sum(kernel, axis=2) + carry_den)
    ratios = shrink / denominator
    probability = powered / denominator[:, :, None]
    weight_low = probability.astype(jnp.bfloat16)
    attended = quick_product("hte,ehd->htd", weight_low, value_ext) + ratios[:, :, None] * (
        exact_product("hte,ehd->htd", kernel, value_ext) + carry_num
    )
    grad_wide = grad_rows.astype(jnp.float32)
    deltas = jnp.sum(jnp.transpose(grad_wide, (1, 0, 2)) * attended, axis=2)
    score_grad, kernel_grad, kernel_scaled = pair_grads(
        probability, kernel, far_sign, ratios, deltas, grad_rows, value_ext
    )
    query_grad = quick_product("hte,ehd->thd", score_grad, key_ext) * scale
    carry_term = (
        exact_product("hfd,thd->thf", carry_state, grad_rows)
        - deltas.T[:, :, None] * carry_sum[None]
    )
    feat_grad = (
        exact_product("hte,ehf->thf", kernel_grad, feat_ext)
        + (carry_on[:, None] * ratios.T)[:, :, None] * carry_term
    )
    return (
        query_grad,
        feat_grad,
        maxima,
        denominator,
        deltas,
        ratios,
        (weight_low, score_grad, kernel_grad, kernel_scaled),
    )


def key_summary(key_feat, value_rows, labels):
    keep = labels == labels[-1]
    state = quick_product(
        "thf,thd->hfd", key_feat * keep.astype(jnp.bfloat16)[:, None, None], value_rows
    )
    total = jnp.sum(key_feat.astype(jnp.float32) * keep.astype(jnp.float32)[:, None, None], axis=0)
    return (state, total, labels[-1])


def query_summary(query_feat, grad_rows, labels, ratios, deltas):
    use = (labels == labels[0]).astype(jnp.float32)[:, None] * ratios.T
    weighted = query_feat.astype(jnp.float32) * use[:, :, None]
    state = exact_product("thf,thd->hfd", weighted, grad_rows)
    total = jnp.sum(weighted * deltas.T[:, :, None], axis=0)
    return (state, total, labels[0])


def combine_pair(earlier, later):
    keep = ((earlier[2] == later[2]) | (later[2] == 0)).astype(jnp.float32)
    state = later[0] + keep.reshape(keep.shape + (1, 1, 1)) * earlier[0]
    total = later[1] + keep.reshape(keep.shape + (1, 1)) * earlier[1]
    mark = jnp.where(later[2] == 0, earlier[2], later[2])
    return (state, total, mark)


def apply_reverse(value_grad, kfeat_grad, key_feat, value_rows, labels, summary):
    state, total, mark = summary
    use = (labels == mark).astype(jnp.float32)[:, None, None]
    value_grad = value_grad + use * exact_product("hfd,thf->thd", state, key_feat)
    kfeat_grad = kfeat_grad + use * (exact_product("hfd,thd->thf", state, value_rows) - total[None])
    return (value_grad, kfeat_grad)


def per_device(queries, keys, values, out_grad, query_feats, key_feats, segment_ids, windows):
    rows = queries.shape[0]
    heads = windows.shape[0]
    head_dim = queries.shape[1] // heads
    feat = query_feats.shape[1] // heads
    tail = rows - WMAX
    query_rows = queries.reshape(rows, heads, head_dim)
    key_rows = keys.reshape(rows, heads, head_dim)
    value_rows = values.reshape(rows, heads, head_dim)
    grad_rows = out_grad.reshape(rows, heads, head_dim)
    query_feat = query_feats.reshape(rows, heads, feat)
    key_feat = key_feats.reshape(rows, heads, feat)
    labels = segment_ids + 1
    edge = jnp.concatenate(
        [
            keys[tail:],
            values[tail:],
            key_feats[tail:],
            jnp.broadcast_to(labels[tail:, None], (WMAX, 128)).astype(keys.dtype),
        ],
        axis=1,
    )
    count = lax.axis_size("seq")
    longest = count * rows // 2
    reach = min(count - 1, (longest + rows - 2) // rows)
    own_ends = jnp.stack([labels[0], labels[-1]])

    def gathered(after):
        if after is None:
            return own_ends
        tied, after = lax.optimization_barrier((own_ends, after))
        return lax.all_gather(tied, "seq")

    carried, mark, halo, ends = carried_in(
        packed(key_summary(key_feat, value_rows, labels)), gathered, "seq", reach, False, edge
    )
    carry = unpacked(carried, mark, heads, feat)
    halo_key = halo[:, : heads * head_dim].reshape(WMAX, heads, head_dim)
    halo_value = halo[:, heads * head_dim : 2 * heads * head_dim].reshape(WMAX, heads, head_dim)
    halo_feat = halo[:, 2 * heads * head_dim : 2 * heads * head_dim + heads * feat].reshape(
        WMAX, heads, feat
    )
    halo_label = halo[:, -1].astype(jnp.int32)
    key_ext = jnp.concatenate([halo_key, key_rows], axis=0)
    value_ext = jnp.concatenate([halo_value, value_rows], axis=0)
    feat_ext = jnp.concatenate([halo_feat, key_feat], axis=0)
    label_ext = jnp.concatenate([halo_label, labels], axis=0)
    query_grad, feat_grad, maxima, denominator, deltas, ratios, pieces = forward_block(
        query_rows,
        query_feat,
        grad_rows,
        key_ext,
        value_ext,
        feat_ext,
        labels,
        label_ext,
        windows,
        carry,
    )
    summed, mark, unused, ends = carried_in(
        packed(query_summary(query_feat, grad_rows, labels, ratios, deltas)),
        ends,
        "seq",
        reach,
        True,
    )
    summary = unpacked(summed, mark, heads, feat)
    weight_low, score_grad, kernel_grad, kernel_scaled = pieces
    key_full, value_full, kfeat_full = key_side(
        query_rows, query_feat, grad_rows, weight_low, score_grad, kernel_grad, kernel_scaled
    )
    rim = jnp.concatenate([key_full[:WMAX], value_full[:WMAX], kfeat_full[:WMAX]], axis=1)
    rim = passed_along(rim.astype(jnp.bfloat16), "seq", -1).astype(jnp.float32)
    back_key, back_value, back_feat = (
        rim[:, :heads],
        rim[:, heads : 2 * heads],
        rim[:, 2 * heads :],
    )
    key_grad = key_full[WMAX:]
    value_grad = value_full[WMAX:]
    kfeat_grad = kfeat_full[WMAX:]
    key_grad = jnp.concatenate([key_grad[:tail], key_grad[tail:] + back_key], axis=0)
    value_grad = jnp.concatenate([value_grad[:tail], value_grad[tail:] + back_value], axis=0)
    kfeat_grad = jnp.concatenate([kfeat_grad[:tail], kfeat_grad[tail:] + back_feat], axis=0)
    value_grad, kfeat_grad = apply_reverse(
        value_grad, kfeat_grad, key_feat, value_rows, labels, summary
    )
    return (
        query_grad.reshape(rows, heads * head_dim).astype(jnp.bfloat16),
        key_grad.reshape(rows, heads * head_dim).astype(jnp.bfloat16),
        value_grad.reshape(rows, heads * head_dim).astype(jnp.bfloat16),
        feat_grad.reshape(rows, heads * feat).astype(jnp.bfloat16),
        kfeat_grad.reshape(rows, heads * feat).astype(jnp.bfloat16),
    )


def solution(mesh):
    in_specs = (
        P(("group", "seq"), None),
        P(("group", "seq"), None),
        P(("group", "seq"), None),
        P(("group", "seq"), None),
        P(("group", "seq"), None),
        P(("group", "seq"), None),
        P(("group", "seq")),
        P("group"),
    )
    out_specs = (
        P(("group", "seq"), None),
        P(("group", "seq"), None),
        P(("group", "seq"), None),
        P(("group", "seq"), None),
        P(("group", "seq"), None),
    )
    return jax.shard_map(
        per_device, mesh=mesh, in_specs=in_specs, out_specs=out_specs, check_vma=False
    )
```

```python
import math

import jax
import jax.numpy as jnp
from jax import lax
from jax.sharding import PartitionSpec as P

WMAX = 64


def passed_along(value, axis, steps):
    count = lax.axis_size(axis)
    leading, last = (max(0, -steps), min(count, count - steps))
    return lax.ppermute(value, axis, [(source, source + steps) for source in range(leading, last)])


def packed(summary):
    state, total = summary[:2]
    heads, feat, width = state.shape
    half = heads // 2
    rows = [state.reshape(2, half * feat, width), total.reshape(2, half, width)]
    return jnp.concatenate(rows, axis=1)


def unpacked(payload, mark, heads, feat):
    width = payload.shape[2]
    half = heads // 2
    state = payload[:, : half * feat].reshape(heads, feat, width)
    total = payload[:, half * feat : half * feat + half].reshape(heads, width)
    return (state, total, mark)


def join_kept(earlier, later, keep):
    return later + keep.astype(jnp.float32) * earlier


def swapped(value, axis):
    count = lax.axis_size(axis)
    pairs = [(device, device ^ 1) for device in range(count)]
    return lax.ppermute(value, axis, pairs)


def chip_steps(reach):
    chips = (reach + 1) // 2
    steps = [1]
    if chips >= 2:
        steps.append(2)
    length = len(steps)
    while length < chips:
        steps.append(length + 1)
        length *= 2
    return steps


def chip_marks(own, partner, axis, reach, backward):
    parity = lax.axis_index(axis) % 2
    slot = 0 if backward else 1
    second = jnp.where(parity == (0 if backward else 1), own[slot], partner[slot])
    first = jnp.where(parity == (1 if backward else 0), own[slot], partner[slot])
    step = -1 if backward else 1
    earlier = {k: passed_along(second, axis, 2 * k * step) for k in chip_steps(reach)}
    return (first, second, earlier)


def carried_in(value, marks, axis, reach, backward, rider=None):
    step = -1 if backward else 1
    parity = lax.axis_index(axis) % 2
    first_mark, second_mark, chip_mark = marks

    def kept(far, near):
        return (far == near) | (near == 0)

    is_first = parity == (1 if backward else 0)
    own_half = lax.dynamic_index_in_dim(value, parity, 0, keepdims=False)
    other_half = lax.dynamic_index_in_dim(value, 1 - parity, 0, keepdims=False)
    partner_half = swapped(other_half, axis)
    if rider is not None:
        rider, partner_half = lax.optimization_barrier((rider, partner_half))
        rider = passed_along(rider, axis, step)
    earlier = jnp.where(is_first, own_half, partner_half)
    later = jnp.where(is_first, partner_half, own_half)
    chip = join_kept(earlier, later, first_mark == second_mark)
    chips = (reach + 1) // 2
    total = passed_along(chip, axis, 2 * step)
    length = 1
    if chips >= 2:
        keep = kept(chip_mark[2], chip_mark[1])
        total = join_kept(passed_along(chip, axis, 4 * step), total, keep)
        length = 2
    while length < chips:
        keep = kept(chip_mark[length + 1], chip_mark[1])
        total = join_kept(passed_along(total, axis, 2 * length * step), total, keep)
        length *= 2
    extended = join_kept(total, earlier, kept(chip_mark[1], first_mark))
    mine = jnp.where(is_first, total, extended)
    theirs = swapped(jnp.where(is_first, extended, total), axis)
    whole = jnp.where(parity == 0, jnp.stack([mine, theirs]), jnp.stack([theirs, mine]))
    nearest = jnp.where(is_first, chip_mark[1], first_mark)
    return (whole, nearest, rider)


def quick_product(form, left, right):
    return jnp.einsum(form, left, right, preferred_element_type=jnp.float32)


def exact_product(form, left, right):
    return jnp.einsum(
        form,
        left.astype(jnp.float32),
        right.astype(jnp.float32),
        precision=lax.Precision.HIGHEST,
        preferred_element_type=jnp.float32,
    )


def pair_masks(labels_q, labels_k, windows, offset):
    distance = (
        jnp.arange(labels_q.shape[0], dtype=jnp.int32)[:, None]
        + offset
        - jnp.arange(labels_k.shape[0], dtype=jnp.int32)[None, :]
    )
    matched = (labels_q[:, None] == labels_k[None, :]) & (labels_q[:, None] > 0) & (distance >= 0)
    inside = matched[None] & (distance[None] < windows[:, None, None])
    is_local = (jnp.arange(labels_k.shape[0], dtype=jnp.int32) >= offset)[None, None, :]
    far_sign = jnp.where(
        is_local, (matched[None] & ~inside).astype(jnp.float32), -inside.astype(jnp.float32)
    )
    return (inside, far_sign)


def pair_scores(query_rows, query_feat, key_ext, feat_ext, labels_q, labels_k, windows, offset):
    inside, far_sign = pair_masks(labels_q, labels_k, windows, offset)
    scale = 1.0 / math.sqrt(query_rows.shape[2])
    score = quick_product("thd,ehd->hte", query_rows, key_ext) * scale
    kernel = quick_product("thf,ehf->hte", query_feat, feat_ext) * far_sign
    return (inside, far_sign, score, kernel)


def pair_grads(probability, kernel, far_sign, ratios, deltas, grad_rows, value_ext):
    weight_grad = quick_product("thd,ehd->hte", grad_rows, value_ext) - deltas[:, :, None]
    score_grad = (probability * weight_grad).astype(jnp.bfloat16)
    kernel_grad = weight_grad * ratios[:, :, None] * far_sign
    return (score_grad, kernel_grad, kernel * ratios[:, :, None])


def key_side(query_rows, query_feat, grad_rows, weight_low, score_grad, kernel_grad, kernel_scaled):
    scale = 1.0 / math.sqrt(query_rows.shape[2])
    key_grad = quick_product("hte,thd->ehd", score_grad, query_rows) * scale
    value_grad = quick_product("hte,thd->ehd", weight_low, grad_rows) + exact_product(
        "hte,thd->ehd", kernel_scaled, grad_rows
    )
    kfeat_grad = exact_product("hte,thf->ehf", kernel_grad, query_feat)
    return (key_grad, value_grad, kfeat_grad)


def forward_block(
    query_rows,
    query_feat,
    grad_rows,
    key_ext,
    value_ext,
    feat_ext,
    labels_q,
    labels_k,
    windows,
    carry,
):
    carry_state, carry_sum, carry_mark = carry
    offset = key_ext.shape[0] - query_rows.shape[0]
    scale = 1.0 / math.sqrt(query_rows.shape[2])
    inside, far_sign, score, kernel = pair_scores(
        query_rows, query_feat, key_ext, feat_ext, labels_q, labels_k, windows, offset
    )
    maxima = jnp.max(jnp.where(inside, score, -jnp.inf), axis=2)
    shrink = jnp.exp(-maxima)
    carry_on = (labels_q == carry_mark).astype(jnp.float32)
    carry_den = exact_product("thf,hf->ht", query_feat, carry_sum) * carry_on[None, :]
    carry_num = exact_product("thf,hfd->htd", query_feat, carry_state) * carry_on[None, :, None]
    powered = jnp.where(inside, jnp.exp(score - maxima[:, :, None]), 0.0)
    denominator = jnp.sum(powered, axis=2) + shrink * (jnp.sum(kernel, axis=2) + carry_den)
    ratios = shrink / denominator
    probability = powered / denominator[:, :, None]
    weight_low = probability.astype(jnp.bfloat16)
    attended = quick_product("hte,ehd->htd", weight_low, value_ext) + ratios[:, :, None] * (
        exact_product("hte,ehd->htd", kernel, value_ext) + carry_num
    )
    grad_wide = grad_rows.astype(jnp.float32)
    deltas = jnp.sum(jnp.transpose(grad_wide, (1, 0, 2)) * attended, axis=2)
    score_grad, kernel_grad, kernel_scaled = pair_grads(
        probability, kernel, far_sign, ratios, deltas, grad_rows, value_ext
    )
    query_grad = quick_product("hte,ehd->thd", score_grad, key_ext) * scale
    carry_term = (
        exact_product("hfd,thd->thf", carry_state, grad_rows)
        - deltas.T[:, :, None] * carry_sum[None]
    )
    feat_grad = (
        exact_product("hte,ehf->thf", kernel_grad, feat_ext)
        + (carry_on[:, None] * ratios.T)[:, :, None] * carry_term
    )
    return (
        query_grad,
        feat_grad,
        maxima,
        denominator,
        deltas,
        ratios,
        (weight_low, score_grad, kernel_grad, kernel_scaled),
    )


def key_summary(key_feat, value_rows, labels):
    keep = labels == labels[-1]
    state = quick_product(
        "thf,thd->hfd", key_feat * keep.astype(jnp.bfloat16)[:, None, None], value_rows
    )
    total = jnp.sum(key_feat.astype(jnp.float32) * keep.astype(jnp.float32)[:, None, None], axis=0)
    return (state, total, labels[-1])


def query_summary(query_feat, grad_rows, labels, ratios, deltas):
    use = (labels == labels[0]).astype(jnp.float32)[:, None] * ratios.T
    weighted = query_feat.astype(jnp.float32) * use[:, :, None]
    state = exact_product("thf,thd->hfd", weighted, grad_rows)
    total = jnp.sum(weighted * deltas.T[:, :, None], axis=0)
    return (state, total, labels[0])


def combine_pair(earlier, later):
    keep = ((earlier[2] == later[2]) | (later[2] == 0)).astype(jnp.float32)
    state = later[0] + keep.reshape(keep.shape + (1, 1, 1)) * earlier[0]
    total = later[1] + keep.reshape(keep.shape + (1, 1)) * earlier[1]
    mark = jnp.where(later[2] == 0, earlier[2], later[2])
    return (state, total, mark)


def apply_reverse(value_grad, kfeat_grad, key_feat, value_rows, labels, summary):
    state, total, mark = summary
    use = (labels == mark).astype(jnp.float32)[:, None, None]
    value_grad = value_grad + use * exact_product("hfd,thf->thd", state, key_feat)
    kfeat_grad = kfeat_grad + use * (exact_product("hfd,thd->thf", state, value_rows) - total[None])
    return (value_grad, kfeat_grad)


def per_device(queries, keys, values, out_grad, query_feats, key_feats, segment_ids, windows):
    rows = queries.shape[0]
    heads = windows.shape[0]
    head_dim = queries.shape[1] // heads
    feat = query_feats.shape[1] // heads
    tail = rows - WMAX
    query_rows = queries.reshape(rows, heads, head_dim)
    key_rows = keys.reshape(rows, heads, head_dim)
    value_rows = values.reshape(rows, heads, head_dim)
    grad_rows = out_grad.reshape(rows, heads, head_dim)
    query_feat = query_feats.reshape(rows, heads, feat)
    key_feat = key_feats.reshape(rows, heads, feat)
    labels = segment_ids + 1
    edge = jnp.concatenate(
        [
            keys[tail:],
            values[tail:],
            key_feats[tail:],
            jnp.broadcast_to(labels[tail:, None], (WMAX, 128)).astype(keys.dtype),
        ],
        axis=1,
    )
    count = lax.axis_size("seq")
    longest = count * rows // 2
    reach = min(count - 1, (longest + rows - 2) // rows)
    own_ends = jnp.stack([labels[0], labels[-1]])
    partner_ends = swapped(own_ends, "seq")
    forward_marks = chip_marks(own_ends, partner_ends, "seq", reach, False)
    backward_marks = chip_marks(own_ends, partner_ends, "seq", reach, True)
    carried, mark, halo = carried_in(
        packed(key_summary(key_feat, value_rows, labels)), forward_marks, "seq", reach, False, edge
    )
    carry = unpacked(carried, mark, heads, feat)
    halo_key = halo[:, : heads * head_dim].reshape(WMAX, heads, head_dim)
    halo_value = halo[:, heads * head_dim : 2 * heads * head_dim].reshape(WMAX, heads, head_dim)
    halo_feat = halo[:, 2 * heads * head_dim : 2 * heads * head_dim + heads * feat].reshape(
        WMAX, heads, feat
    )
    halo_label = halo[:, -1].astype(jnp.int32)
    key_ext = jnp.concatenate([halo_key, key_rows], axis=0)
    value_ext = jnp.concatenate([halo_value, value_rows], axis=0)
    feat_ext = jnp.concatenate([halo_feat, key_feat], axis=0)
    label_ext = jnp.concatenate([halo_label, labels], axis=0)
    query_grad, feat_grad, maxima, denominator, deltas, ratios, pieces = forward_block(
        query_rows,
        query_feat,
        grad_rows,
        key_ext,
        value_ext,
        feat_ext,
        labels,
        label_ext,
        windows,
        carry,
    )
    summed, mark, unused = carried_in(
        packed(query_summary(query_feat, grad_rows, labels, ratios, deltas)),
        backward_marks,
        "seq",
        reach,
        True,
    )
    summary = unpacked(summed, mark, heads, feat)
    weight_low, score_grad, kernel_grad, kernel_scaled = pieces
    key_full, value_full, kfeat_full = key_side(
        query_rows, query_feat, grad_rows, weight_low, score_grad, kernel_grad, kernel_scaled
    )
    rim = jnp.concatenate([key_full[:WMAX], value_full[:WMAX], kfeat_full[:WMAX]], axis=1)
    rim = passed_along(rim.astype(jnp.bfloat16), "seq", -1).astype(jnp.float32)
    back_key, back_value, back_feat = (
        rim[:, :heads],
        rim[:, heads : 2 * heads],
        rim[:, 2 * heads :],
    )
    key_grad = key_full[WMAX:]
    value_grad = value_full[WMAX:]
    kfeat_grad = kfeat_full[WMAX:]
    key_grad = jnp.concatenate([key_grad[:tail], key_grad[tail:] + back_key], axis=0)
    value_grad = jnp.concatenate([value_grad[:tail], value_grad[tail:] + back_value], axis=0)
    kfeat_grad = jnp.concatenate([kfeat_grad[:tail], kfeat_grad[tail:] + back_feat], axis=0)
    value_grad, kfeat_grad = apply_reverse(
        value_grad, kfeat_grad, key_feat, value_rows, labels, summary
    )
    return (
        query_grad.reshape(rows, heads * head_dim).astype(jnp.bfloat16),
        key_grad.reshape(rows, heads * head_dim).astype(jnp.bfloat16),
        value_grad.reshape(rows, heads * head_dim).astype(jnp.bfloat16),
        feat_grad.reshape(rows, heads * feat).astype(jnp.bfloat16),
        kfeat_grad.reshape(rows, heads * feat).astype(jnp.bfloat16),
    )


def solution(mesh):
    in_specs = (
        P(("group", "seq"), None),
        P(("group", "seq"), None),
        P(("group", "seq"), None),
        P(("group", "seq"), None),
        P(("group", "seq"), None),
        P(("group", "seq"), None),
        P(("group", "seq")),
        P("group"),
    )
    out_specs = (
        P(("group", "seq"), None),
        P(("group", "seq"), None),
        P(("group", "seq"), None),
        P(("group", "seq"), None),
        P(("group", "seq"), None),
    )
    return jax.shard_map(
        per_device, mesh=mesh, in_specs=in_specs, out_specs=out_specs, check_vma=False
    )
```

```python
import math

import jax
import jax.numpy as jnp
from jax import lax
from jax.sharding import PartitionSpec as P

WMAX = 64


def passed_along(value, axis, steps):
    count = lax.axis_size(axis)
    leading, last = (max(0, -steps), min(count, count - steps))
    return lax.ppermute(value, axis, [(source, source + steps) for source in range(leading, last)])


def packed(summary):
    state, total, mark = summary
    heads, feat, width = state.shape
    half = heads // 2
    marks = jnp.full((2, 1, width), mark, jnp.float32)
    rows = [state.reshape(2, half * feat, width), total.reshape(2, half, width), marks]
    return jnp.concatenate(rows, axis=1)


def unpacked(payload, heads, feat):
    width = payload.shape[2]
    half = heads // 2
    state = payload[:, : half * feat].reshape(heads, feat, width)
    total = payload[:, half * feat : half * feat + half].reshape(heads, width)
    mark = payload[0, half * feat + half, 0].astype(jnp.int32)
    return (state, total, mark)


def join_packed(earlier, later):
    at = later.shape[-2] - 1
    mark_e, mark_l = (earlier[..., at : at + 1, :], later[..., at : at + 1, :])
    keep = ((mark_e == mark_l) | (mark_l == 0)).astype(jnp.float32)
    mark = jnp.where(mark_l == 0, mark_e, mark_l)
    row = lax.broadcasted_iota(jnp.int32, later.shape, later.ndim - 2)
    return jnp.where(row == at, mark, later + keep * earlier)


def swapped(value, axis):
    count = lax.axis_size(axis)
    pairs = [(device, device ^ 1) for device in range(count)]
    return lax.ppermute(value, axis, pairs)


def carried_in(value, axis, reach, backward, rider=None):
    step = -1 if backward else 1
    parity = lax.axis_index(axis) % 2
    is_first = parity == (1 if backward else 0)
    own_half = lax.dynamic_index_in_dim(value, parity, 0, keepdims=False)
    other_half = lax.dynamic_index_in_dim(value, 1 - parity, 0, keepdims=False)
    partner_half = swapped(other_half, axis)
    if rider is not None:
        rider, partner_half = lax.optimization_barrier((rider, partner_half))
        rider = passed_along(rider, axis, step)
    earlier = jnp.where(is_first, own_half, partner_half)
    later = jnp.where(is_first, partner_half, own_half)
    chip = join_packed(earlier, later)
    chips = (reach + 1) // 2
    total = passed_along(chip, axis, 2 * step)
    length = 1
    if chips >= 2:
        total = join_packed(passed_along(chip, axis, 4 * step), total)
        length = 2
    while length < chips:
        total = join_packed(passed_along(total, axis, 2 * length * step), total)
        length *= 2
    extended = join_packed(total, earlier)
    mine = jnp.where(is_first, total, extended)
    theirs = swapped(jnp.where(is_first, extended, total), axis)
    whole = jnp.where(parity == 0, jnp.stack([mine, theirs]), jnp.stack([theirs, mine]))
    return whole if rider is None else (whole, rider)


def quick_product(form, left, right):
    return jnp.einsum(form, left, right, preferred_element_type=jnp.float32)


def exact_product(form, left, right):
    return jnp.einsum(
        form,
        left.astype(jnp.float32),
        right.astype(jnp.float32),
        precision=lax.Precision.HIGHEST,
        preferred_element_type=jnp.float32,
    )


def pair_masks(labels_q, labels_k, windows, offset):
    distance = (
        jnp.arange(labels_q.shape[0], dtype=jnp.int32)[:, None]
        + offset
        - jnp.arange(labels_k.shape[0], dtype=jnp.int32)[None, :]
    )
    matched = (labels_q[:, None] == labels_k[None, :]) & (labels_q[:, None] > 0) & (distance >= 0)
    inside = matched[None] & (distance[None] < windows[:, None, None])
    is_local = (jnp.arange(labels_k.shape[0], dtype=jnp.int32) >= offset)[None, None, :]
    far_sign = jnp.where(
        is_local, (matched[None] & ~inside).astype(jnp.float32), -inside.astype(jnp.float32)
    )
    return (inside, far_sign)


def pair_scores(query_rows, query_feat, key_ext, feat_ext, labels_q, labels_k, windows, offset):
    inside, far_sign = pair_masks(labels_q, labels_k, windows, offset)
    scale = 1.0 / math.sqrt(query_rows.shape[2])
    score = quick_product("thd,ehd->hte", query_rows, key_ext) * scale
    kernel = quick_product("thf,ehf->hte", query_feat, feat_ext) * far_sign
    return (inside, far_sign, score, kernel)


def pair_grads(probability, kernel, far_sign, ratios, deltas, grad_rows, value_ext):
    weight_grad = quick_product("thd,ehd->hte", grad_rows, value_ext) - deltas[:, :, None]
    score_grad = (probability * weight_grad).astype(jnp.bfloat16)
    kernel_grad = weight_grad * ratios[:, :, None] * far_sign
    return (score_grad, kernel_grad, kernel * ratios[:, :, None])


def key_side(query_rows, query_feat, grad_rows, weight_low, score_grad, kernel_grad, kernel_scaled):
    scale = 1.0 / math.sqrt(query_rows.shape[2])
    key_grad = quick_product("hte,thd->ehd", score_grad, query_rows) * scale
    value_grad = quick_product("hte,thd->ehd", weight_low, grad_rows) + exact_product(
        "hte,thd->ehd", kernel_scaled, grad_rows
    )
    kfeat_grad = exact_product("hte,thf->ehf", kernel_grad, query_feat)
    return (key_grad, value_grad, kfeat_grad)


def forward_block(
    query_rows,
    query_feat,
    grad_rows,
    key_ext,
    value_ext,
    feat_ext,
    labels_q,
    labels_k,
    windows,
    carry,
):
    carry_state, carry_sum, carry_mark = carry
    offset = key_ext.shape[0] - query_rows.shape[0]
    scale = 1.0 / math.sqrt(query_rows.shape[2])
    inside, far_sign, score, kernel = pair_scores(
        query_rows, query_feat, key_ext, feat_ext, labels_q, labels_k, windows, offset
    )
    maxima = jnp.max(jnp.where(inside, score, -jnp.inf), axis=2)
    shrink = jnp.exp(-maxima)
    carry_on = (labels_q == carry_mark).astype(jnp.float32)
    carry_den = exact_product("thf,hf->ht", query_feat, carry_sum) * carry_on[None, :]
    carry_num = exact_product("thf,hfd->htd", query_feat, carry_state) * carry_on[None, :, None]
    powered = jnp.where(inside, jnp.exp(score - maxima[:, :, None]), 0.0)
    denominator = jnp.sum(powered, axis=2) + shrink * (jnp.sum(kernel, axis=2) + carry_den)
    ratios = shrink / denominator
    probability = powered / denominator[:, :, None]
    weight_low = probability.astype(jnp.bfloat16)
    attended = quick_product("hte,ehd->htd", weight_low, value_ext) + ratios[:, :, None] * (
        exact_product("hte,ehd->htd", kernel, value_ext) + carry_num
    )
    grad_wide = grad_rows.astype(jnp.float32)
    deltas = jnp.sum(jnp.transpose(grad_wide, (1, 0, 2)) * attended, axis=2)
    score_grad, kernel_grad, kernel_scaled = pair_grads(
        probability, kernel, far_sign, ratios, deltas, grad_rows, value_ext
    )
    query_grad = quick_product("hte,ehd->thd", score_grad, key_ext) * scale
    carry_term = (
        exact_product("hfd,thd->thf", carry_state, grad_rows)
        - deltas.T[:, :, None] * carry_sum[None]
    )
    feat_grad = (
        exact_product("hte,ehf->thf", kernel_grad, feat_ext)
        + (carry_on[:, None] * ratios.T)[:, :, None] * carry_term
    )
    return (
        query_grad,
        feat_grad,
        maxima,
        denominator,
        deltas,
        ratios,
        (weight_low, score_grad, kernel_grad, kernel_scaled),
    )


def key_summary(key_feat, value_rows, labels):
    keep = labels == labels[-1]
    state = quick_product(
        "thf,thd->hfd", key_feat * keep.astype(jnp.bfloat16)[:, None, None], value_rows
    )
    total = jnp.sum(key_feat.astype(jnp.float32) * keep.astype(jnp.float32)[:, None, None], axis=0)
    return (state, total, labels[-1])


def query_summary(query_feat, grad_rows, labels, ratios, deltas):
    use = (labels == labels[0]).astype(jnp.float32)[:, None] * ratios.T
    weighted = query_feat.astype(jnp.float32) * use[:, :, None]
    state = exact_product("thf,thd->hfd", weighted, grad_rows)
    total = jnp.sum(weighted * deltas.T[:, :, None], axis=0)
    return (state, total, labels[0])


def combine_pair(earlier, later):
    keep = ((earlier[2] == later[2]) | (later[2] == 0)).astype(jnp.float32)
    state = later[0] + keep.reshape(keep.shape + (1, 1, 1)) * earlier[0]
    total = later[1] + keep.reshape(keep.shape + (1, 1)) * earlier[1]
    mark = jnp.where(later[2] == 0, earlier[2], later[2])
    return (state, total, mark)


def apply_reverse(value_grad, kfeat_grad, key_feat, value_rows, labels, summary):
    state, total, mark = summary
    use = (labels == mark).astype(jnp.float32)[:, None, None]
    value_grad = value_grad + use * exact_product("hfd,thf->thd", state, key_feat)
    kfeat_grad = kfeat_grad + use * (exact_product("hfd,thd->thf", state, value_rows) - total[None])
    return (value_grad, kfeat_grad)


def per_device(queries, keys, values, out_grad, query_feats, key_feats, segment_ids, windows):
    rows = queries.shape[0]
    heads = windows.shape[0]
    head_dim = queries.shape[1] // heads
    feat = query_feats.shape[1] // heads
    tail = rows - WMAX
    query_rows = queries.reshape(rows, heads, head_dim)
    key_rows = keys.reshape(rows, heads, head_dim)
    value_rows = values.reshape(rows, heads, head_dim)
    grad_rows = out_grad.reshape(rows, heads, head_dim)
    query_feat = query_feats.reshape(rows, heads, feat)
    key_feat = key_feats.reshape(rows, heads, feat)
    labels = segment_ids + 1
    edge = jnp.concatenate(
        [
            keys[tail:],
            values[tail:],
            key_feats[tail:],
            jnp.broadcast_to(labels[tail:, None], (WMAX, 128)).astype(keys.dtype),
        ],
        axis=1,
    )
    count = lax.axis_size("seq")
    longest = count * rows // 2
    reach = min(count - 1, (longest + rows - 2) // rows)
    carried, halo = carried_in(
        packed(key_summary(key_feat, value_rows, labels)), "seq", reach, False, edge
    )
    carry = unpacked(carried, heads, feat)
    halo_key = halo[:, : heads * head_dim].reshape(WMAX, heads, head_dim)
    halo_value = halo[:, heads * head_dim : 2 * heads * head_dim].reshape(WMAX, heads, head_dim)
    halo_feat = halo[:, 2 * heads * head_dim : 2 * heads * head_dim + heads * feat].reshape(
        WMAX, heads, feat
    )
    halo_label = halo[:, -1].astype(jnp.int32)
    key_ext = jnp.concatenate([halo_key, key_rows], axis=0)
    value_ext = jnp.concatenate([halo_value, value_rows], axis=0)
    feat_ext = jnp.concatenate([halo_feat, key_feat], axis=0)
    label_ext = jnp.concatenate([halo_label, labels], axis=0)
    query_grad, feat_grad, maxima, denominator, deltas, ratios, pieces = forward_block(
        query_rows,
        query_feat,
        grad_rows,
        key_ext,
        value_ext,
        feat_ext,
        labels,
        label_ext,
        windows,
        carry,
    )
    summary = unpacked(
        carried_in(
            packed(query_summary(query_feat, grad_rows, labels, ratios, deltas)), "seq", reach, True
        ),
        heads,
        feat,
    )
    weight_low, score_grad, kernel_grad, kernel_scaled = pieces
    key_full, value_full, kfeat_full = key_side(
        query_rows, query_feat, grad_rows, weight_low, score_grad, kernel_grad, kernel_scaled
    )
    rim = jnp.concatenate([key_full[:WMAX], value_full[:WMAX], kfeat_full[:WMAX]], axis=1)
    rim = passed_along(rim.astype(jnp.bfloat16), "seq", -1).astype(jnp.float32)
    back_key, back_value, back_feat = (
        rim[:, :heads],
        rim[:, heads : 2 * heads],
        rim[:, 2 * heads :],
    )
    key_grad = key_full[WMAX:]
    value_grad = value_full[WMAX:]
    kfeat_grad = kfeat_full[WMAX:]
    key_grad = jnp.concatenate([key_grad[:tail], key_grad[tail:] + back_key], axis=0)
    value_grad = jnp.concatenate([value_grad[:tail], value_grad[tail:] + back_value], axis=0)
    kfeat_grad = jnp.concatenate([kfeat_grad[:tail], kfeat_grad[tail:] + back_feat], axis=0)
    value_grad, kfeat_grad = apply_reverse(
        value_grad, kfeat_grad, key_feat, value_rows, labels, summary
    )
    return (
        query_grad.reshape(rows, heads * head_dim).astype(jnp.bfloat16),
        key_grad.reshape(rows, heads * head_dim).astype(jnp.bfloat16),
        value_grad.reshape(rows, heads * head_dim).astype(jnp.bfloat16),
        feat_grad.reshape(rows, heads * feat).astype(jnp.bfloat16),
        kfeat_grad.reshape(rows, heads * feat).astype(jnp.bfloat16),
    )


def solution(mesh):
    in_specs = (
        P(("group", "seq"), None),
        P(("group", "seq"), None),
        P(("group", "seq"), None),
        P(("group", "seq"), None),
        P(("group", "seq"), None),
        P(("group", "seq"), None),
        P(("group", "seq")),
        P("group"),
    )
    out_specs = (
        P(("group", "seq"), None),
        P(("group", "seq"), None),
        P(("group", "seq"), None),
        P(("group", "seq"), None),
        P(("group", "seq"), None),
    )
    return jax.shard_map(
        per_device, mesh=mesh, in_specs=in_specs, out_specs=out_specs, check_vma=False
    )
```

```python
import math

import jax
import jax.numpy as jnp
from jax import lax
from jax.sharding import PartitionSpec as P

WMAX = 64


def passed_along(value, axis, steps):
    count = lax.axis_size(axis)
    leading, last = (max(0, -steps), min(count, count - steps))
    return lax.ppermute(value, axis, [(source, source + steps) for source in range(leading, last)])


def packed(summary):
    state, total, mark = summary
    heads, feat, width = state.shape
    half = heads // 2
    marks = jnp.full((2, 1, width), mark, jnp.float32)
    rows = [state.reshape(2, half * feat, width), total.reshape(2, half, width), marks]
    return jnp.concatenate(rows, axis=1)


def unpacked(payload, heads, feat):
    width = payload.shape[2]
    half = heads // 2
    state = payload[:, : half * feat].reshape(heads, feat, width)
    total = payload[:, half * feat : half * feat + half].reshape(heads, width)
    mark = payload[0, half * feat + half, 0].astype(jnp.int32)
    return (state, total, mark)


def join_packed(earlier, later):
    at = later.shape[-2] - 1
    mark_e, mark_l = (earlier[..., at : at + 1, :], later[..., at : at + 1, :])
    keep = ((mark_e == mark_l) | (mark_l == 0)).astype(jnp.float32)
    mark = jnp.where(mark_l == 0, mark_e, mark_l)
    row = lax.broadcasted_iota(jnp.int32, later.shape, later.ndim - 2)
    return jnp.where(row == at, mark, later + keep * earlier)


def swapped(value, axis):
    count = lax.axis_size(axis)
    pairs = [(device, device ^ 1) for device in range(count)]
    return lax.ppermute(value, axis, pairs)


def carried_in(value, axis, reach, backward, rider=None, cargo=None):
    step = -1 if backward else 1
    parity = lax.axis_index(axis) % 2
    is_first = parity == (1 if backward else 0)
    own_half = lax.dynamic_index_in_dim(value, parity, 0, keepdims=False)
    other_half = lax.dynamic_index_in_dim(value, 1 - parity, 0, keepdims=False)
    partner_half = swapped(other_half, axis)
    if rider is not None:
        rider, partner_half = lax.optimization_barrier((rider, partner_half))
        rider = passed_along(rider, axis, step)
    earlier = jnp.where(is_first, own_half, partner_half)
    later = jnp.where(is_first, partner_half, own_half)
    chip = join_packed(earlier, later)
    if cargo is not None:
        cargo, chip = lax.optimization_barrier((cargo, chip))
    chips = (reach + 1) // 2
    total = passed_along(chip, axis, 2 * step)
    length = 1
    if chips >= 2:
        total = join_packed(passed_along(chip, axis, 4 * step), total)
        length = 2
    while length < chips:
        total = join_packed(passed_along(total, axis, 2 * length * step), total)
        length *= 2
    extended = join_packed(total, earlier)
    mine = jnp.where(is_first, total, extended)
    theirs = swapped(jnp.where(is_first, extended, total), axis)
    whole = jnp.where(parity == 0, jnp.stack([mine, theirs]), jnp.stack([theirs, mine]))
    if cargo is not None:
        return (whole, rider, cargo)
    return whole if rider is None else (whole, rider)


def quick_product(form, left, right):
    return jnp.einsum(form, left, right, preferred_element_type=jnp.float32)


def exact_product(form, left, right):
    return jnp.einsum(
        form,
        left.astype(jnp.float32),
        right.astype(jnp.float32),
        precision=lax.Precision.HIGHEST,
        preferred_element_type=jnp.float32,
    )


def pair_masks(labels_q, labels_k, windows, offset):
    distance = (
        jnp.arange(labels_q.shape[0], dtype=jnp.int32)[:, None]
        + offset
        - jnp.arange(labels_k.shape[0], dtype=jnp.int32)[None, :]
    )
    matched = (labels_q[:, None] == labels_k[None, :]) & (labels_q[:, None] > 0) & (distance >= 0)
    inside = matched[None] & (distance[None] < windows[:, None, None])
    is_local = (jnp.arange(labels_k.shape[0], dtype=jnp.int32) >= offset)[None, None, :]
    far_sign = jnp.where(
        is_local, (matched[None] & ~inside).astype(jnp.float32), -inside.astype(jnp.float32)
    )
    return (inside, far_sign)


def pair_scores(query_rows, query_feat, key_ext, feat_ext, labels_q, labels_k, windows, offset):
    inside, far_sign = pair_masks(labels_q, labels_k, windows, offset)
    scale = 1.0 / math.sqrt(query_rows.shape[2])
    score = quick_product("thd,ehd->hte", query_rows, key_ext) * scale
    kernel = quick_product("thf,ehf->hte", query_feat, feat_ext) * far_sign
    return (inside, far_sign, score, kernel)


def pair_grads(probability, kernel, far_sign, ratios, deltas, grad_rows, value_ext):
    weight_grad = quick_product("thd,ehd->hte", grad_rows, value_ext) - deltas[:, :, None]
    score_grad = (probability * weight_grad).astype(jnp.bfloat16)
    kernel_grad = weight_grad * ratios[:, :, None] * far_sign
    return (score_grad, kernel_grad, kernel * ratios[:, :, None])


def key_side(query_rows, query_feat, grad_rows, weight_low, score_grad, kernel_grad, kernel_scaled):
    scale = 1.0 / math.sqrt(query_rows.shape[2])
    key_grad = quick_product("hte,thd->ehd", score_grad, query_rows) * scale
    value_grad = quick_product("hte,thd->ehd", weight_low, grad_rows) + exact_product(
        "hte,thd->ehd", kernel_scaled, grad_rows
    )
    kfeat_grad = exact_product("hte,thf->ehf", kernel_grad, query_feat)
    return (key_grad, value_grad, kfeat_grad)


def forward_block(
    query_rows,
    query_feat,
    grad_rows,
    key_ext,
    value_ext,
    feat_ext,
    labels_q,
    labels_k,
    windows,
    carry,
):
    carry_state, carry_sum, carry_mark = carry
    offset = key_ext.shape[0] - query_rows.shape[0]
    scale = 1.0 / math.sqrt(query_rows.shape[2])
    inside, far_sign, score, kernel = pair_scores(
        query_rows, query_feat, key_ext, feat_ext, labels_q, labels_k, windows, offset
    )
    maxima = jnp.max(jnp.where(inside, score, -jnp.inf), axis=2)
    shrink = jnp.exp(-maxima)
    carry_on = (labels_q == carry_mark).astype(jnp.float32)
    carry_den = exact_product("thf,hf->ht", query_feat, carry_sum) * carry_on[None, :]
    carry_num = exact_product("thf,hfd->htd", query_feat, carry_state) * carry_on[None, :, None]
    powered = jnp.where(inside, jnp.exp(score - maxima[:, :, None]), 0.0)
    denominator = jnp.sum(powered, axis=2) + shrink * (jnp.sum(kernel, axis=2) + carry_den)
    ratios = shrink / denominator
    probability = powered / denominator[:, :, None]
    weight_low = probability.astype(jnp.bfloat16)
    attended = quick_product("hte,ehd->htd", weight_low, value_ext) + ratios[:, :, None] * (
        exact_product("hte,ehd->htd", kernel, value_ext) + carry_num
    )
    grad_wide = grad_rows.astype(jnp.float32)
    deltas = jnp.sum(jnp.transpose(grad_wide, (1, 0, 2)) * attended, axis=2)
    score_grad, kernel_grad, kernel_scaled = pair_grads(
        probability, kernel, far_sign, ratios, deltas, grad_rows, value_ext
    )
    query_grad = quick_product("hte,ehd->thd", score_grad, key_ext) * scale
    carry_term = (
        exact_product("hfd,thd->thf", carry_state, grad_rows)
        - deltas.T[:, :, None] * carry_sum[None]
    )
    feat_grad = (
        exact_product("hte,ehf->thf", kernel_grad, feat_ext)
        + (carry_on[:, None] * ratios.T)[:, :, None] * carry_term
    )
    return (
        query_grad,
        feat_grad,
        maxima,
        denominator,
        deltas,
        ratios,
        (weight_low, score_grad, kernel_grad, kernel_scaled),
    )


def key_summary(key_feat, value_rows, labels):
    keep = labels == labels[-1]
    state = quick_product(
        "thf,thd->hfd", key_feat * keep.astype(jnp.bfloat16)[:, None, None], value_rows
    )
    total = jnp.sum(key_feat.astype(jnp.float32) * keep.astype(jnp.float32)[:, None, None], axis=0)
    return (state, total, labels[-1])


def query_summary(query_feat, grad_rows, labels, ratios, deltas):
    use = (labels == labels[0]).astype(jnp.float32)[:, None] * ratios.T
    weighted = query_feat.astype(jnp.float32) * use[:, :, None]
    state = exact_product("thf,thd->hfd", weighted, grad_rows)
    total = jnp.sum(weighted * deltas.T[:, :, None], axis=0)
    return (state, total, labels[0])


def combine_pair(earlier, later):
    keep = ((earlier[2] == later[2]) | (later[2] == 0)).astype(jnp.float32)
    state = later[0] + keep.reshape(keep.shape + (1, 1, 1)) * earlier[0]
    total = later[1] + keep.reshape(keep.shape + (1, 1)) * earlier[1]
    mark = jnp.where(later[2] == 0, earlier[2], later[2])
    return (state, total, mark)


def apply_reverse(value_grad, kfeat_grad, key_feat, value_rows, labels, summary):
    state, total, mark = summary
    use = (labels == mark).astype(jnp.float32)[:, None, None]
    value_grad = value_grad + use * exact_product("hfd,thf->thd", state, key_feat)
    kfeat_grad = kfeat_grad + use * (exact_product("hfd,thd->thf", state, value_rows) - total[None])
    return (value_grad, kfeat_grad)


def per_device(queries, keys, values, out_grad, query_feats, key_feats, segment_ids, windows):
    rows = queries.shape[0]
    heads = windows.shape[0]
    head_dim = queries.shape[1] // heads
    feat = query_feats.shape[1] // heads
    tail = rows - WMAX
    query_rows = queries.reshape(rows, heads, head_dim)
    key_rows = keys.reshape(rows, heads, head_dim)
    value_rows = values.reshape(rows, heads, head_dim)
    grad_rows = out_grad.reshape(rows, heads, head_dim)
    query_feat = query_feats.reshape(rows, heads, feat)
    key_feat = key_feats.reshape(rows, heads, feat)
    labels = segment_ids + 1
    edge = jnp.concatenate(
        [
            keys[tail:],
            values[tail:],
            key_feats[tail:],
            jnp.broadcast_to(labels[tail:, None], (WMAX, 128)).astype(keys.dtype),
        ],
        axis=1,
    )
    count = lax.axis_size("seq")
    longest = count * rows // 2
    reach = min(count - 1, (longest + rows - 2) // rows)
    carried, halo, cargo = carried_in(
        packed(key_summary(key_feat, value_rows, labels)),
        "seq",
        reach,
        False,
        edge,
        (query_rows, key_rows, value_rows, grad_rows, query_feat, key_feat),
    )
    query_rows, key_rows, value_rows, grad_rows, query_feat, key_feat = cargo
    carry = unpacked(carried, heads, feat)
    halo_key = halo[:, : heads * head_dim].reshape(WMAX, heads, head_dim)
    halo_value = halo[:, heads * head_dim : 2 * heads * head_dim].reshape(WMAX, heads, head_dim)
    halo_feat = halo[:, 2 * heads * head_dim : 2 * heads * head_dim + heads * feat].reshape(
        WMAX, heads, feat
    )
    halo_label = halo[:, -1].astype(jnp.int32)
    key_ext = jnp.concatenate([halo_key, key_rows], axis=0)
    value_ext = jnp.concatenate([halo_value, value_rows], axis=0)
    feat_ext = jnp.concatenate([halo_feat, key_feat], axis=0)
    label_ext = jnp.concatenate([halo_label, labels], axis=0)
    query_grad, feat_grad, maxima, denominator, deltas, ratios, pieces = forward_block(
        query_rows,
        query_feat,
        grad_rows,
        key_ext,
        value_ext,
        feat_ext,
        labels,
        label_ext,
        windows,
        carry,
    )
    summary = unpacked(
        carried_in(
            packed(query_summary(query_feat, grad_rows, labels, ratios, deltas)), "seq", reach, True
        ),
        heads,
        feat,
    )
    weight_low, score_grad, kernel_grad, kernel_scaled = pieces
    key_full, value_full, kfeat_full = key_side(
        query_rows, query_feat, grad_rows, weight_low, score_grad, kernel_grad, kernel_scaled
    )
    rim = jnp.concatenate([key_full[:WMAX], value_full[:WMAX], kfeat_full[:WMAX]], axis=1)
    rim = passed_along(rim.astype(jnp.bfloat16), "seq", -1).astype(jnp.float32)
    back_key, back_value, back_feat = (
        rim[:, :heads],
        rim[:, heads : 2 * heads],
        rim[:, 2 * heads :],
    )
    key_grad = key_full[WMAX:]
    value_grad = value_full[WMAX:]
    kfeat_grad = kfeat_full[WMAX:]
    key_grad = jnp.concatenate([key_grad[:tail], key_grad[tail:] + back_key], axis=0)
    value_grad = jnp.concatenate([value_grad[:tail], value_grad[tail:] + back_value], axis=0)
    kfeat_grad = jnp.concatenate([kfeat_grad[:tail], kfeat_grad[tail:] + back_feat], axis=0)
    value_grad, kfeat_grad = apply_reverse(
        value_grad, kfeat_grad, key_feat, value_rows, labels, summary
    )
    return (
        query_grad.reshape(rows, heads * head_dim).astype(jnp.bfloat16),
        key_grad.reshape(rows, heads * head_dim).astype(jnp.bfloat16),
        value_grad.reshape(rows, heads * head_dim).astype(jnp.bfloat16),
        feat_grad.reshape(rows, heads * feat).astype(jnp.bfloat16),
        kfeat_grad.reshape(rows, heads * feat).astype(jnp.bfloat16),
    )


def solution(mesh):
    in_specs = (
        P(("group", "seq"), None),
        P(("group", "seq"), None),
        P(("group", "seq"), None),
        P(("group", "seq"), None),
        P(("group", "seq"), None),
        P(("group", "seq"), None),
        P(("group", "seq")),
        P("group"),
    )
    out_specs = (
        P(("group", "seq"), None),
        P(("group", "seq"), None),
        P(("group", "seq"), None),
        P(("group", "seq"), None),
        P(("group", "seq"), None),
    )
    return jax.shard_map(
        per_device, mesh=mesh, in_specs=in_specs, out_specs=out_specs, check_vma=False
    )
```

```python
import math

import jax
import jax.numpy as jnp
from jax import lax
from jax.sharding import PartitionSpec as P

WMAX = 64


def passed_along(value, axis, steps):
    count = lax.axis_size(axis)
    leading, last = (max(0, -steps), min(count, count - steps))
    return lax.ppermute(value, axis, [(source, source + steps) for source in range(leading, last)])


def packed(summary):
    state, total = summary[:2]
    heads, feat, width = state.shape
    half = heads // 2
    rows = [state.reshape(2, half * feat, width), total.reshape(2, half, width)]
    return jnp.concatenate(rows, axis=1)


def unpacked(payload, mark, heads, feat):
    width = payload.shape[2]
    half = heads // 2
    state = payload[:, : half * feat].reshape(heads, feat, width)
    total = payload[:, half * feat : half * feat + half].reshape(heads, width)
    return (state, total, mark)


def join_kept(earlier, later, keep):
    return later + keep.astype(jnp.float32) * earlier


def swapped(value, axis):
    count = lax.axis_size(axis)
    pairs = [(device, device ^ 1) for device in range(count)]
    return lax.ppermute(value, axis, pairs)


def carried_in(value, ends, axis, reach, backward, rider=None):
    if callable(ends):
        own = ends(None)
        partner = swapped(own, axis)
        first_keep = own[0 if backward else 1] == partner[0 if backward else 1]
    else:
        first_keep = None
    count = lax.axis_size(axis)
    step = -1 if backward else 1
    device = lax.axis_index(axis)
    parity = device % 2
    spot = count - 1 - device if backward else device
    chip_at = spot // 2

    def mark_at(place):
        inside = (place >= 0) & (place < count)
        real = count - 1 - place if backward else place
        found = ends[jnp.clip(real, 0, count - 1), 0 if backward else 1]
        return jnp.where(inside, found, 0)

    def chip_mark(chip):
        return mark_at(2 * chip + 1)

    def kept(far, near):
        return (far == near) | (near == 0)

    is_first = spot % 2 == 0
    own_half = lax.dynamic_index_in_dim(value, parity, 0, keepdims=False)
    other_half = lax.dynamic_index_in_dim(value, 1 - parity, 0, keepdims=False)
    partner_half = swapped(other_half, axis)
    earlier = jnp.where(is_first, own_half, partner_half)
    later = jnp.where(is_first, partner_half, own_half)
    if first_keep is None:
        first_keep = kept(mark_at(2 * chip_at), mark_at(2 * chip_at + 1))
    chip = join_kept(earlier, later, first_keep)
    if callable(ends):
        ends = ends(chip)
    chips = (reach + 1) // 2
    total = passed_along(chip, axis, 2 * step)
    length = 1
    if chips >= 2:
        keep = kept(chip_mark(chip_at - 2), chip_mark(chip_at - 1))
        total = join_kept(passed_along(chip, axis, 4 * step), total, keep)
        length = 2
    if rider is not None:
        rider, total = lax.optimization_barrier((rider, total))
        rider = passed_along(rider, axis, step)
    while length < chips:
        keep = kept(chip_mark(chip_at - length - 1), chip_mark(chip_at - 1))
        total = join_kept(passed_along(total, axis, 2 * length * step), total, keep)
        length *= 2
    extended = join_kept(total, earlier, kept(chip_mark(chip_at - 1), mark_at(2 * chip_at)))
    mine = jnp.where(is_first, total, extended)
    theirs = swapped(jnp.where(is_first, extended, total), axis)
    whole = jnp.where(parity == 0, jnp.stack([mine, theirs]), jnp.stack([theirs, mine]))
    return (whole, mark_at(spot - 1), rider, ends)


def quick_product(form, left, right):
    return jnp.einsum(form, left, right, preferred_element_type=jnp.float32)


def exact_product(form, left, right):
    return jnp.einsum(
        form,
        left.astype(jnp.float32),
        right.astype(jnp.float32),
        precision=lax.Precision.HIGHEST,
        preferred_element_type=jnp.float32,
    )


def pair_masks(labels_q, labels_k, windows, offset):
    distance = (
        jnp.arange(labels_q.shape[0], dtype=jnp.int32)[:, None]
        + offset
        - jnp.arange(labels_k.shape[0], dtype=jnp.int32)[None, :]
    )
    matched = (labels_q[:, None] == labels_k[None, :]) & (labels_q[:, None] > 0) & (distance >= 0)
    inside = matched[None] & (distance[None] < windows[:, None, None])
    is_local = (jnp.arange(labels_k.shape[0], dtype=jnp.int32) >= offset)[None, None, :]
    far_sign = jnp.where(
        is_local, (matched[None] & ~inside).astype(jnp.float32), -inside.astype(jnp.float32)
    )
    return (inside, far_sign)


def pair_scores(query_rows, query_feat, key_ext, feat_ext, labels_q, labels_k, windows, offset):
    inside, far_sign = pair_masks(labels_q, labels_k, windows, offset)
    scale = 1.0 / math.sqrt(query_rows.shape[2])
    score = quick_product("thd,ehd->hte", query_rows, key_ext) * scale
    kernel = quick_product("thf,ehf->hte", query_feat, feat_ext) * far_sign
    return (inside, far_sign, score, kernel)


def pair_grads(probability, kernel, far_sign, ratios, deltas, grad_rows, value_ext):
    weight_grad = quick_product("thd,ehd->hte", grad_rows, value_ext) - deltas[:, :, None]
    score_grad = (probability * weight_grad).astype(jnp.bfloat16)
    kernel_grad = weight_grad * ratios[:, :, None] * far_sign
    return (score_grad, kernel_grad, kernel * ratios[:, :, None])


def key_side(query_rows, query_feat, grad_rows, weight_low, score_grad, kernel_grad, kernel_scaled):
    scale = 1.0 / math.sqrt(query_rows.shape[2])
    key_grad = quick_product("hte,thd->ehd", score_grad, query_rows) * scale
    value_grad = quick_product("hte,thd->ehd", weight_low, grad_rows) + exact_product(
        "hte,thd->ehd", kernel_scaled, grad_rows
    )
    kfeat_grad = exact_product("hte,thf->ehf", kernel_grad, query_feat)
    return (key_grad, value_grad, kfeat_grad)


def forward_block(
    query_rows,
    query_feat,
    grad_rows,
    key_ext,
    value_ext,
    feat_ext,
    labels_q,
    labels_k,
    windows,
    carry,
):
    carry_state, carry_sum, carry_mark = carry
    offset = key_ext.shape[0] - query_rows.shape[0]
    scale = 1.0 / math.sqrt(query_rows.shape[2])
    inside, far_sign, score, kernel = pair_scores(
        query_rows, query_feat, key_ext, feat_ext, labels_q, labels_k, windows, offset
    )
    maxima = jnp.max(jnp.where(inside, score, -jnp.inf), axis=2)
    shrink = jnp.exp(-maxima)
    carry_on = (labels_q == carry_mark).astype(jnp.float32)
    carry_den = exact_product("thf,hf->ht", query_feat, carry_sum) * carry_on[None, :]
    carry_num = exact_product("thf,hfd->htd", query_feat, carry_state) * carry_on[None, :, None]
    powered = jnp.where(inside, jnp.exp(score - maxima[:, :, None]), 0.0)
    denominator = jnp.sum(powered, axis=2) + shrink * (jnp.sum(kernel, axis=2) + carry_den)
    ratios = shrink / denominator
    probability = powered / denominator[:, :, None]
    weight_low = probability.astype(jnp.bfloat16)
    attended = quick_product("hte,ehd->htd", weight_low, value_ext) + ratios[:, :, None] * (
        exact_product("hte,ehd->htd", kernel, value_ext) + carry_num
    )
    grad_wide = grad_rows.astype(jnp.float32)
    deltas = jnp.sum(jnp.transpose(grad_wide, (1, 0, 2)) * attended, axis=2)
    score_grad, kernel_grad, kernel_scaled = pair_grads(
        probability, kernel, far_sign, ratios, deltas, grad_rows, value_ext
    )
    query_grad = quick_product("hte,ehd->thd", score_grad, key_ext) * scale
    carry_term = (
        exact_product("hfd,thd->thf", carry_state, grad_rows)
        - deltas.T[:, :, None] * carry_sum[None]
    )
    feat_grad = (
        exact_product("hte,ehf->thf", kernel_grad, feat_ext)
        + (carry_on[:, None] * ratios.T)[:, :, None] * carry_term
    )
    return (
        query_grad,
        feat_grad,
        maxima,
        denominator,
        deltas,
        ratios,
        (weight_low, score_grad, kernel_grad, kernel_scaled),
    )


def key_summary(key_feat, value_rows, labels):
    keep = labels == labels[-1]
    state = quick_product(
        "thf,thd->hfd", key_feat * keep.astype(jnp.bfloat16)[:, None, None], value_rows
    )
    total = jnp.sum(key_feat.astype(jnp.float32) * keep.astype(jnp.float32)[:, None, None], axis=0)
    return (state, total, labels[-1])


def query_summary(query_feat, grad_rows, labels, ratios, deltas):
    use = (labels == labels[0]).astype(jnp.float32)[:, None] * ratios.T
    weighted = query_feat.astype(jnp.float32) * use[:, :, None]
    state = exact_product("thf,thd->hfd", weighted, grad_rows)
    total = jnp.sum(weighted * deltas.T[:, :, None], axis=0)
    return (state, total, labels[0])


def combine_pair(earlier, later):
    keep = ((earlier[2] == later[2]) | (later[2] == 0)).astype(jnp.float32)
    state = later[0] + keep.reshape(keep.shape + (1, 1, 1)) * earlier[0]
    total = later[1] + keep.reshape(keep.shape + (1, 1)) * earlier[1]
    mark = jnp.where(later[2] == 0, earlier[2], later[2])
    return (state, total, mark)


def apply_reverse(value_grad, kfeat_grad, key_feat, value_rows, labels, summary):
    state, total, mark = summary
    use = (labels == mark).astype(jnp.float32)[:, None, None]
    value_grad = value_grad + use * exact_product("hfd,thf->thd", state, key_feat)
    kfeat_grad = kfeat_grad + use * (exact_product("hfd,thd->thf", state, value_rows) - total[None])
    return (value_grad, kfeat_grad)


def per_device(queries, keys, values, out_grad, query_feats, key_feats, segment_ids, windows):
    rows = queries.shape[0]
    heads = windows.shape[0]
    head_dim = queries.shape[1] // heads
    feat = query_feats.shape[1] // heads
    tail = rows - WMAX
    query_rows = queries.reshape(rows, heads, head_dim)
    key_rows = keys.reshape(rows, heads, head_dim)
    value_rows = values.reshape(rows, heads, head_dim)
    grad_rows = out_grad.reshape(rows, heads, head_dim)
    query_feat = query_feats.reshape(rows, heads, feat)
    key_feat = key_feats.reshape(rows, heads, feat)
    labels = segment_ids + 1
    edge = jnp.concatenate(
        [
            keys[tail:],
            values[tail:],
            key_feats[tail:],
            jnp.broadcast_to(labels[tail:, None], (WMAX, 128)).astype(keys.dtype),
        ],
        axis=1,
    )
    count = lax.axis_size("seq")
    longest = count * rows // 2
    reach = min(count - 1, (longest + rows - 2) // rows)
    own_ends = jnp.stack([labels[0], labels[-1]])

    def gathered(after):
        if after is None:
            return own_ends
        tied, after = lax.optimization_barrier((own_ends, after))
        return lax.all_gather(tied, "seq")

    carried, mark, halo, ends = carried_in(
        packed(key_summary(key_feat, value_rows, labels)), gathered, "seq", reach, False, edge
    )
    carry = unpacked(carried, mark, heads, feat)
    halo_key = halo[:, : heads * head_dim].reshape(WMAX, heads, head_dim)
    halo_value = halo[:, heads * head_dim : 2 * heads * head_dim].reshape(WMAX, heads, head_dim)
    halo_feat = halo[:, 2 * heads * head_dim : 2 * heads * head_dim + heads * feat].reshape(
        WMAX, heads, feat
    )
    halo_label = halo[:, -1].astype(jnp.int32)
    key_ext = jnp.concatenate([halo_key, key_rows], axis=0)
    value_ext = jnp.concatenate([halo_value, value_rows], axis=0)
    feat_ext = jnp.concatenate([halo_feat, key_feat], axis=0)
    label_ext = jnp.concatenate([halo_label, labels], axis=0)
    query_grad, feat_grad, maxima, denominator, deltas, ratios, pieces = forward_block(
        query_rows,
        query_feat,
        grad_rows,
        key_ext,
        value_ext,
        feat_ext,
        labels,
        label_ext,
        windows,
        carry,
    )
    summed, mark, unused, ends = carried_in(
        packed(query_summary(query_feat, grad_rows, labels, ratios, deltas)),
        ends,
        "seq",
        reach,
        True,
    )
    summary = unpacked(summed, mark, heads, feat)
    weight_low, score_grad, kernel_grad, kernel_scaled = pieces
    key_full, value_full, kfeat_full = key_side(
        query_rows, query_feat, grad_rows, weight_low, score_grad, kernel_grad, kernel_scaled
    )
    rim = jnp.concatenate([key_full[:WMAX], value_full[:WMAX], kfeat_full[:WMAX]], axis=1)
    rim = passed_along(rim.astype(jnp.bfloat16), "seq", -1).astype(jnp.float32)
    back_key, back_value, back_feat = (
        rim[:, :heads],
        rim[:, heads : 2 * heads],
        rim[:, 2 * heads :],
    )
    key_grad = key_full[WMAX:]
    value_grad = value_full[WMAX:]
    kfeat_grad = kfeat_full[WMAX:]
    key_grad = jnp.concatenate([key_grad[:tail], key_grad[tail:] + back_key], axis=0)
    value_grad = jnp.concatenate([value_grad[:tail], value_grad[tail:] + back_value], axis=0)
    kfeat_grad = jnp.concatenate([kfeat_grad[:tail], kfeat_grad[tail:] + back_feat], axis=0)
    value_grad, kfeat_grad = apply_reverse(
        value_grad, kfeat_grad, key_feat, value_rows, labels, summary
    )
    return (
        query_grad.reshape(rows, heads * head_dim).astype(jnp.bfloat16),
        key_grad.reshape(rows, heads * head_dim).astype(jnp.bfloat16),
        value_grad.reshape(rows, heads * head_dim).astype(jnp.bfloat16),
        feat_grad.reshape(rows, heads * feat).astype(jnp.bfloat16),
        kfeat_grad.reshape(rows, heads * feat).astype(jnp.bfloat16),
    )


def solution(mesh):
    in_specs = (
        P(("group", "seq"), None),
        P(("group", "seq"), None),
        P(("group", "seq"), None),
        P(("group", "seq"), None),
        P(("group", "seq"), None),
        P(("group", "seq"), None),
        P(("group", "seq")),
        P("group"),
    )
    out_specs = (
        P(("group", "seq"), None),
        P(("group", "seq"), None),
        P(("group", "seq"), None),
        P(("group", "seq"), None),
        P(("group", "seq"), None),
    )
    return jax.shard_map(
        per_device, mesh=mesh, in_specs=in_specs, out_specs=out_specs, check_vma=False
    )
```

```python
import math

import jax
import jax.numpy as jnp
from jax import lax
from jax.sharding import PartitionSpec as P

WMAX = 64


def passed_along(value, axis, steps):
    count = lax.axis_size(axis)
    leading, last = (max(0, -steps), min(count, count - steps))
    return lax.ppermute(value, axis, [(source, source + steps) for source in range(leading, last)])


def packed(summary):
    state, total = summary[:2]
    heads, feat, width = state.shape
    half = heads // 2
    rows = [state.reshape(2, half * feat, width), total.reshape(2, half, width)]
    return jnp.concatenate(rows, axis=1)


def unpacked(payload, mark, heads, feat):
    width = payload.shape[2]
    half = heads // 2
    state = payload[:, : half * feat].reshape(heads, feat, width)
    total = payload[:, half * feat : half * feat + half].reshape(heads, width)
    return (state, total, mark)


def join_kept(earlier, later, keep):
    return later + keep.astype(jnp.float32) * earlier


def swapped(value, axis):
    count = lax.axis_size(axis)
    pairs = [(device, device ^ 1) for device in range(count)]
    return lax.ppermute(value, axis, pairs)


def carried_in(value, ends, axis, reach, backward, rider=None):
    first_keep = None
    count = lax.axis_size(axis)
    step = -1 if backward else 1
    device = lax.axis_index(axis)
    parity = device % 2
    spot = count - 1 - device if backward else device
    chip_at = spot // 2

    def mark_at(place):
        inside = (place >= 0) & (place < count)
        real = count - 1 - place if backward else place
        found = ends[jnp.clip(real, 0, count - 1), 0 if backward else 1]
        return jnp.where(inside, found, 0)

    def chip_mark(chip):
        return mark_at(2 * chip + 1)

    def kept(far, near):
        return (far == near) | (near == 0)

    is_first = spot % 2 == 0
    own_half = lax.dynamic_index_in_dim(value, parity, 0, keepdims=False)
    other_half = lax.dynamic_index_in_dim(value, 1 - parity, 0, keepdims=False)
    if callable(ends):
        ends = ends(other_half)
    partner_half = swapped(other_half, axis)
    if rider is not None:
        rider, partner_half = lax.optimization_barrier((rider, partner_half))
        rider = passed_along(rider, axis, step)
    earlier = jnp.where(is_first, own_half, partner_half)
    later = jnp.where(is_first, partner_half, own_half)
    if first_keep is None:
        first_keep = kept(mark_at(2 * chip_at), mark_at(2 * chip_at + 1))
    chip = join_kept(earlier, later, first_keep)
    chips = (reach + 1) // 2
    total = passed_along(chip, axis, 2 * step)
    length = 1
    if chips >= 2:
        keep = kept(chip_mark(chip_at - 2), chip_mark(chip_at - 1))
        total = join_kept(passed_along(chip, axis, 4 * step), total, keep)
        length = 2
    while length < chips:
        keep = kept(chip_mark(chip_at - length - 1), chip_mark(chip_at - 1))
        total = join_kept(passed_along(total, axis, 2 * length * step), total, keep)
        length *= 2
    extended = join_kept(total, earlier, kept(chip_mark(chip_at - 1), mark_at(2 * chip_at)))
    mine = jnp.where(is_first, total, extended)
    theirs = swapped(jnp.where(is_first, extended, total), axis)
    whole = jnp.where(parity == 0, jnp.stack([mine, theirs]), jnp.stack([theirs, mine]))
    return (whole, mark_at(spot - 1), rider, ends)


def quick_product(form, left, right):
    return jnp.einsum(form, left, right, preferred_element_type=jnp.float32)


def exact_product(form, left, right):
    return jnp.einsum(
        form,
        left.astype(jnp.float32),
        right.astype(jnp.float32),
        precision=lax.Precision.HIGHEST,
        preferred_element_type=jnp.float32,
    )


def pair_masks(labels_q, labels_k, windows, offset):
    distance = (
        jnp.arange(labels_q.shape[0], dtype=jnp.int32)[:, None]
        + offset
        - jnp.arange(labels_k.shape[0], dtype=jnp.int32)[None, :]
    )
    matched = (labels_q[:, None] == labels_k[None, :]) & (labels_q[:, None] > 0) & (distance >= 0)
    inside = matched[None] & (distance[None] < windows[:, None, None])
    is_local = (jnp.arange(labels_k.shape[0], dtype=jnp.int32) >= offset)[None, None, :]
    far_sign = jnp.where(
        is_local, (matched[None] & ~inside).astype(jnp.float32), -inside.astype(jnp.float32)
    )
    return (inside, far_sign)


def pair_scores(query_rows, query_feat, key_ext, feat_ext, labels_q, labels_k, windows, offset):
    inside, far_sign = pair_masks(labels_q, labels_k, windows, offset)
    scale = 1.0 / math.sqrt(query_rows.shape[2])
    score = quick_product("thd,ehd->hte", query_rows, key_ext) * scale
    kernel = quick_product("thf,ehf->hte", query_feat, feat_ext) * far_sign
    return (inside, far_sign, score, kernel)


def pair_grads(probability, kernel, far_sign, ratios, deltas, grad_rows, value_ext):
    weight_grad = quick_product("thd,ehd->hte", grad_rows, value_ext) - deltas[:, :, None]
    score_grad = (probability * weight_grad).astype(jnp.bfloat16)
    kernel_grad = weight_grad * ratios[:, :, None] * far_sign
    return (score_grad, kernel_grad, kernel * ratios[:, :, None])


def key_side(query_rows, query_feat, grad_rows, weight_low, score_grad, kernel_grad, kernel_scaled):
    scale = 1.0 / math.sqrt(query_rows.shape[2])
    key_grad = quick_product("hte,thd->ehd", score_grad, query_rows) * scale
    value_grad = quick_product("hte,thd->ehd", weight_low, grad_rows) + exact_product(
        "hte,thd->ehd", kernel_scaled, grad_rows
    )
    kfeat_grad = exact_product("hte,thf->ehf", kernel_grad, query_feat)
    return (key_grad, value_grad, kfeat_grad)


def forward_block(
    query_rows,
    query_feat,
    grad_rows,
    key_ext,
    value_ext,
    feat_ext,
    labels_q,
    labels_k,
    windows,
    carry,
):
    carry_state, carry_sum, carry_mark = carry
    offset = key_ext.shape[0] - query_rows.shape[0]
    scale = 1.0 / math.sqrt(query_rows.shape[2])
    inside, far_sign, score, kernel = pair_scores(
        query_rows, query_feat, key_ext, feat_ext, labels_q, labels_k, windows, offset
    )
    maxima = jnp.max(jnp.where(inside, score, -jnp.inf), axis=2)
    shrink = jnp.exp(-maxima)
    carry_on = (labels_q == carry_mark).astype(jnp.float32)
    carry_den = exact_product("thf,hf->ht", query_feat, carry_sum) * carry_on[None, :]
    carry_num = exact_product("thf,hfd->htd", query_feat, carry_state) * carry_on[None, :, None]
    powered = jnp.where(inside, jnp.exp(score - maxima[:, :, None]), 0.0)
    denominator = jnp.sum(powered, axis=2) + shrink * (jnp.sum(kernel, axis=2) + carry_den)
    ratios = shrink / denominator
    probability = powered / denominator[:, :, None]
    weight_low = probability.astype(jnp.bfloat16)
    attended = quick_product("hte,ehd->htd", weight_low, value_ext) + ratios[:, :, None] * (
        exact_product("hte,ehd->htd", kernel, value_ext) + carry_num
    )
    grad_wide = grad_rows.astype(jnp.float32)
    deltas = jnp.sum(jnp.transpose(grad_wide, (1, 0, 2)) * attended, axis=2)
    score_grad, kernel_grad, kernel_scaled = pair_grads(
        probability, kernel, far_sign, ratios, deltas, grad_rows, value_ext
    )
    query_grad = quick_product("hte,ehd->thd", score_grad, key_ext) * scale
    carry_term = (
        exact_product("hfd,thd->thf", carry_state, grad_rows)
        - deltas.T[:, :, None] * carry_sum[None]
    )
    feat_grad = (
        exact_product("hte,ehf->thf", kernel_grad, feat_ext)
        + (carry_on[:, None] * ratios.T)[:, :, None] * carry_term
    )
    return (
        query_grad,
        feat_grad,
        maxima,
        denominator,
        deltas,
        ratios,
        (weight_low, score_grad, kernel_grad, kernel_scaled),
    )


def key_summary(key_feat, value_rows, labels):
    keep = labels == labels[-1]
    state = quick_product(
        "thf,thd->hfd", key_feat * keep.astype(jnp.bfloat16)[:, None, None], value_rows
    )
    total = jnp.sum(key_feat.astype(jnp.float32) * keep.astype(jnp.float32)[:, None, None], axis=0)
    return (state, total, labels[-1])


def query_summary(query_feat, grad_rows, labels, ratios, deltas):
    use = (labels == labels[0]).astype(jnp.float32)[:, None] * ratios.T
    weighted = query_feat.astype(jnp.float32) * use[:, :, None]
    state = exact_product("thf,thd->hfd", weighted, grad_rows)
    total = jnp.sum(weighted * deltas.T[:, :, None], axis=0)
    return (state, total, labels[0])


def combine_pair(earlier, later):
    keep = ((earlier[2] == later[2]) | (later[2] == 0)).astype(jnp.float32)
    state = later[0] + keep.reshape(keep.shape + (1, 1, 1)) * earlier[0]
    total = later[1] + keep.reshape(keep.shape + (1, 1)) * earlier[1]
    mark = jnp.where(later[2] == 0, earlier[2], later[2])
    return (state, total, mark)


def apply_reverse(value_grad, kfeat_grad, key_feat, value_rows, labels, summary):
    state, total, mark = summary
    use = (labels == mark).astype(jnp.float32)[:, None, None]
    value_grad = value_grad + use * exact_product("hfd,thf->thd", state, key_feat)
    kfeat_grad = kfeat_grad + use * (exact_product("hfd,thd->thf", state, value_rows) - total[None])
    return (value_grad, kfeat_grad)


def per_device(queries, keys, values, out_grad, query_feats, key_feats, segment_ids, windows):
    rows = queries.shape[0]
    heads = windows.shape[0]
    head_dim = queries.shape[1] // heads
    feat = query_feats.shape[1] // heads
    tail = rows - WMAX
    query_rows = queries.reshape(rows, heads, head_dim)
    key_rows = keys.reshape(rows, heads, head_dim)
    value_rows = values.reshape(rows, heads, head_dim)
    grad_rows = out_grad.reshape(rows, heads, head_dim)
    query_feat = query_feats.reshape(rows, heads, feat)
    key_feat = key_feats.reshape(rows, heads, feat)
    labels = segment_ids + 1
    edge = jnp.concatenate(
        [
            keys[tail:],
            values[tail:],
            key_feats[tail:],
            jnp.broadcast_to(labels[tail:, None], (WMAX, 128)).astype(keys.dtype),
        ],
        axis=1,
    )
    count = lax.axis_size("seq")
    longest = count * rows // 2
    reach = min(count - 1, (longest + rows - 2) // rows)
    own_ends = jnp.stack([labels[0], labels[-1]])

    def gathered(after):
        if after is None:
            return own_ends
        tied, after = lax.optimization_barrier((own_ends, after))
        return lax.all_gather(tied, "seq")

    carried, mark, halo, ends = carried_in(
        packed(key_summary(key_feat, value_rows, labels)), gathered, "seq", reach, False, edge
    )
    carry = unpacked(carried, mark, heads, feat)
    halo_key = halo[:, : heads * head_dim].reshape(WMAX, heads, head_dim)
    halo_value = halo[:, heads * head_dim : 2 * heads * head_dim].reshape(WMAX, heads, head_dim)
    halo_feat = halo[:, 2 * heads * head_dim : 2 * heads * head_dim + heads * feat].reshape(
        WMAX, heads, feat
    )
    halo_label = halo[:, -1].astype(jnp.int32)
    key_ext = jnp.concatenate([halo_key, key_rows], axis=0)
    value_ext = jnp.concatenate([halo_value, value_rows], axis=0)
    feat_ext = jnp.concatenate([halo_feat, key_feat], axis=0)
    label_ext = jnp.concatenate([halo_label, labels], axis=0)
    query_grad, feat_grad, maxima, denominator, deltas, ratios, pieces = forward_block(
        query_rows,
        query_feat,
        grad_rows,
        key_ext,
        value_ext,
        feat_ext,
        labels,
        label_ext,
        windows,
        carry,
    )
    summed, mark, unused, ends = carried_in(
        packed(query_summary(query_feat, grad_rows, labels, ratios, deltas)),
        ends,
        "seq",
        reach,
        True,
    )
    summary = unpacked(summed, mark, heads, feat)
    weight_low, score_grad, kernel_grad, kernel_scaled = pieces
    key_full, value_full, kfeat_full = key_side(
        query_rows, query_feat, grad_rows, weight_low, score_grad, kernel_grad, kernel_scaled
    )
    rim = jnp.concatenate([key_full[:WMAX], value_full[:WMAX], kfeat_full[:WMAX]], axis=1)
    rim = passed_along(rim.astype(jnp.bfloat16), "seq", -1).astype(jnp.float32)
    back_key, back_value, back_feat = (
        rim[:, :heads],
        rim[:, heads : 2 * heads],
        rim[:, 2 * heads :],
    )
    key_grad = key_full[WMAX:]
    value_grad = value_full[WMAX:]
    kfeat_grad = kfeat_full[WMAX:]
    key_grad = jnp.concatenate([key_grad[:tail], key_grad[tail:] + back_key], axis=0)
    value_grad = jnp.concatenate([value_grad[:tail], value_grad[tail:] + back_value], axis=0)
    kfeat_grad = jnp.concatenate([kfeat_grad[:tail], kfeat_grad[tail:] + back_feat], axis=0)
    value_grad, kfeat_grad = apply_reverse(
        value_grad, kfeat_grad, key_feat, value_rows, labels, summary
    )
    return (
        query_grad.reshape(rows, heads * head_dim).astype(jnp.bfloat16),
        key_grad.reshape(rows, heads * head_dim).astype(jnp.bfloat16),
        value_grad.reshape(rows, heads * head_dim).astype(jnp.bfloat16),
        feat_grad.reshape(rows, heads * feat).astype(jnp.bfloat16),
        kfeat_grad.reshape(rows, heads * feat).astype(jnp.bfloat16),
    )


def solution(mesh):
    in_specs = (
        P(("group", "seq"), None),
        P(("group", "seq"), None),
        P(("group", "seq"), None),
        P(("group", "seq"), None),
        P(("group", "seq"), None),
        P(("group", "seq"), None),
        P(("group", "seq")),
        P("group"),
    )
    out_specs = (
        P(("group", "seq"), None),
        P(("group", "seq"), None),
        P(("group", "seq"), None),
        P(("group", "seq"), None),
        P(("group", "seq"), None),
    )
    return jax.shard_map(
        per_device, mesh=mesh, in_specs=in_specs, out_specs=out_specs, check_vma=False
    )
```

```python
import math

import jax
import jax.numpy as jnp
from jax import lax
from jax.sharding import PartitionSpec as P

WMAX = 64


def passed_along(value, axis, steps):
    count = lax.axis_size(axis)
    leading, last = (max(0, -steps), min(count, count - steps))
    return lax.ppermute(value, axis, [(source, source + steps) for source in range(leading, last)])


def packed(summary):
    state, total = summary[:2]
    heads, feat, width = state.shape
    half = heads // 2
    rows = [state.reshape(2, half * feat, width), total.reshape(2, half, width)]
    return jnp.concatenate(rows, axis=1)


def unpacked(payload, mark, heads, feat):
    width = payload.shape[2]
    half = heads // 2
    state = payload[:, : half * feat].reshape(heads, feat, width)
    total = payload[:, half * feat : half * feat + half].reshape(heads, width)
    return (state, total, mark)


def join_kept(earlier, later, keep):
    return later + keep.astype(jnp.float32) * earlier


def swapped(value, axis):
    count = lax.axis_size(axis)
    pairs = [(device, device ^ 1) for device in range(count)]
    return lax.ppermute(value, axis, pairs)


def carried_in(value, ends, axis, reach, backward, rider=None):
    if callable(ends):
        own = ends(None)
        partner = swapped(own, axis)
        first_keep = own[0 if backward else 1] == partner[0 if backward else 1]
    else:
        first_keep = None
    count = lax.axis_size(axis)
    step = -1 if backward else 1
    device = lax.axis_index(axis)
    parity = device % 2
    spot = count - 1 - device if backward else device
    chip_at = spot // 2

    def mark_at(place):
        inside = (place >= 0) & (place < count)
        real = count - 1 - place if backward else place
        found = ends[jnp.clip(real, 0, count - 1), 0 if backward else 1]
        return jnp.where(inside, found, 0)

    def chip_mark(chip):
        return mark_at(2 * chip + 1)

    def kept(far, near):
        return (far == near) | (near == 0)

    is_first = spot % 2 == 0
    own_half = lax.dynamic_index_in_dim(value, parity, 0, keepdims=False)
    other_half = lax.dynamic_index_in_dim(value, 1 - parity, 0, keepdims=False)
    partner_half = swapped(other_half, axis)
    if rider is not None:
        rider, partner_half = lax.optimization_barrier((rider, partner_half))
        rider = passed_along(rider, axis, step)
    earlier = jnp.where(is_first, own_half, partner_half)
    later = jnp.where(is_first, partner_half, own_half)
    if first_keep is None:
        first_keep = kept(mark_at(2 * chip_at), mark_at(2 * chip_at + 1))
    chip = join_kept(earlier, later, first_keep)
    if callable(ends):
        ends = ends(chip)
    chips = (reach + 1) // 2
    total = passed_along(chip, axis, 2 * step)
    length = 1
    if chips >= 2:
        keep = kept(chip_mark(chip_at - 2), chip_mark(chip_at - 1))
        total = join_kept(passed_along(chip, axis, 4 * step), total, keep)
        length = 2
    while length < chips:
        keep = kept(chip_mark(chip_at - length - 1), chip_mark(chip_at - 1))
        total = join_kept(passed_along(total, axis, 2 * length * step), total, keep)
        length *= 2
    extended = join_kept(total, earlier, kept(chip_mark(chip_at - 1), mark_at(2 * chip_at)))
    mine = jnp.where(is_first, total, extended)
    theirs = swapped(jnp.where(is_first, extended, total), axis)
    whole = jnp.where(parity == 0, jnp.stack([mine, theirs]), jnp.stack([theirs, mine]))
    return (whole, mark_at(spot - 1), rider, ends)


def quick_product(form, left, right):
    return jnp.einsum(form, left, right, preferred_element_type=jnp.float32)


def exact_product(form, left, right):
    return jnp.einsum(
        form,
        left.astype(jnp.float32),
        right.astype(jnp.float32),
        precision=lax.Precision.HIGHEST,
        preferred_element_type=jnp.float32,
    )


def pair_masks(labels_q, labels_k, windows, offset):
    distance = (
        jnp.arange(labels_q.shape[0], dtype=jnp.int32)[:, None]
        + offset
        - jnp.arange(labels_k.shape[0], dtype=jnp.int32)[None, :]
    )
    matched = (labels_q[:, None] == labels_k[None, :]) & (labels_q[:, None] > 0) & (distance >= 0)
    inside = matched[None] & (distance[None] < windows[:, None, None])
    is_local = (jnp.arange(labels_k.shape[0], dtype=jnp.int32) >= offset)[None, None, :]
    far_sign = jnp.where(
        is_local, (matched[None] & ~inside).astype(jnp.float32), -inside.astype(jnp.float32)
    )
    return (inside, far_sign)


def pair_scores(query_rows, query_feat, key_ext, feat_ext, labels_q, labels_k, windows, offset):
    inside, far_sign = pair_masks(labels_q, labels_k, windows, offset)
    scale = 1.0 / math.sqrt(query_rows.shape[2])
    score = quick_product("thd,ehd->hte", query_rows, key_ext) * scale
    kernel = quick_product("thf,ehf->hte", query_feat, feat_ext) * far_sign
    return (inside, far_sign, score, kernel)


def pair_grads(probability, kernel, far_sign, ratios, deltas, grad_rows, value_ext):
    weight_grad = quick_product("thd,ehd->hte", grad_rows, value_ext) - deltas[:, :, None]
    score_grad = (probability * weight_grad).astype(jnp.bfloat16)
    kernel_grad = weight_grad * ratios[:, :, None] * far_sign
    return (score_grad, kernel_grad, kernel * ratios[:, :, None])


def key_side(query_rows, query_feat, grad_rows, weight_low, score_grad, kernel_grad, kernel_scaled):
    scale = 1.0 / math.sqrt(query_rows.shape[2])
    key_grad = quick_product("hte,thd->ehd", score_grad, query_rows) * scale
    value_grad = quick_product("hte,thd->ehd", weight_low, grad_rows) + exact_product(
        "hte,thd->ehd", kernel_scaled, grad_rows
    )
    kfeat_grad = exact_product("hte,thf->ehf", kernel_grad, query_feat)
    return (key_grad, value_grad, kfeat_grad)


def forward_block(
    query_rows,
    query_feat,
    grad_rows,
    key_ext,
    value_ext,
    feat_ext,
    labels_q,
    labels_k,
    windows,
    carry,
):
    carry_state, carry_sum, carry_mark = carry
    offset = key_ext.shape[0] - query_rows.shape[0]
    scale = 1.0 / math.sqrt(query_rows.shape[2])
    inside, far_sign, score, kernel = pair_scores(
        query_rows, query_feat, key_ext, feat_ext, labels_q, labels_k, windows, offset
    )
    maxima = jnp.max(jnp.where(inside, score, -jnp.inf), axis=2)
    shrink = jnp.exp(-maxima)
    carry_on = (labels_q == carry_mark).astype(jnp.float32)
    carry_den = exact_product("thf,hf->ht", query_feat, carry_sum) * carry_on[None, :]
    carry_num = exact_product("thf,hfd->htd", query_feat, carry_state) * carry_on[None, :, None]
    powered = jnp.where(inside, jnp.exp(score - maxima[:, :, None]), 0.0)
    denominator = jnp.sum(powered, axis=2) + shrink * (jnp.sum(kernel, axis=2) + carry_den)
    ratios = shrink / denominator
    probability = powered / denominator[:, :, None]
    weight_low = probability.astype(jnp.bfloat16)
    attended = quick_product("hte,ehd->htd", weight_low, value_ext) + ratios[:, :, None] * (
        exact_product("hte,ehd->htd", kernel, value_ext) + carry_num
    )
    grad_wide = grad_rows.astype(jnp.float32)
    deltas = jnp.sum(jnp.transpose(grad_wide, (1, 0, 2)) * attended, axis=2)
    score_grad, kernel_grad, kernel_scaled = pair_grads(
        probability, kernel, far_sign, ratios, deltas, grad_rows, value_ext
    )
    query_grad = quick_product("hte,ehd->thd", score_grad, key_ext) * scale
    carry_term = (
        exact_product("hfd,thd->thf", carry_state, grad_rows)
        - deltas.T[:, :, None] * carry_sum[None]
    )
    feat_grad = (
        exact_product("hte,ehf->thf", kernel_grad, feat_ext)
        + (carry_on[:, None] * ratios.T)[:, :, None] * carry_term
    )
    return (
        query_grad,
        feat_grad,
        maxima,
        denominator,
        deltas,
        ratios,
        (weight_low, score_grad, kernel_grad, kernel_scaled),
    )


def key_summary(key_feat, value_rows, labels):
    keep = labels == labels[-1]
    state = quick_product(
        "thf,thd->hfd", key_feat * keep.astype(jnp.bfloat16)[:, None, None], value_rows
    )
    rows, heads, feat = key_feat.shape
    terms = key_feat.astype(jnp.float32) * keep.astype(jnp.float32)[:, None, None]
    total = jnp.sum(terms.reshape(rows, 2, heads // 2, feat), axis=0)
    return (state, total, labels[-1])


def query_summary(query_feat, grad_rows, labels, ratios, deltas):
    use = (labels == labels[0]).astype(jnp.float32)[:, None] * ratios.T
    weighted = query_feat.astype(jnp.float32) * use[:, :, None]
    state = exact_product("thf,thd->hfd", weighted, grad_rows)
    rows, heads, feat = weighted.shape
    terms = weighted * deltas.T[:, :, None]
    total = jnp.sum(terms.reshape(rows, 2, heads // 2, feat), axis=0)
    return (state, total, labels[0])


def combine_pair(earlier, later):
    keep = ((earlier[2] == later[2]) | (later[2] == 0)).astype(jnp.float32)
    state = later[0] + keep.reshape(keep.shape + (1, 1, 1)) * earlier[0]
    total = later[1] + keep.reshape(keep.shape + (1, 1)) * earlier[1]
    mark = jnp.where(later[2] == 0, earlier[2], later[2])
    return (state, total, mark)


def apply_reverse(value_grad, kfeat_grad, key_feat, value_rows, labels, summary):
    state, total, mark = summary
    use = (labels == mark).astype(jnp.float32)[:, None, None]
    value_grad = value_grad + use * exact_product("hfd,thf->thd", state, key_feat)
    kfeat_grad = kfeat_grad + use * (exact_product("hfd,thd->thf", state, value_rows) - total[None])
    return (value_grad, kfeat_grad)


def per_device(queries, keys, values, out_grad, query_feats, key_feats, segment_ids, windows):
    rows = queries.shape[0]
    heads = windows.shape[0]
    head_dim = queries.shape[1] // heads
    feat = query_feats.shape[1] // heads
    tail = rows - WMAX
    query_rows = queries.reshape(rows, heads, head_dim)
    key_rows = keys.reshape(rows, heads, head_dim)
    value_rows = values.reshape(rows, heads, head_dim)
    grad_rows = out_grad.reshape(rows, heads, head_dim)
    query_feat = query_feats.reshape(rows, heads, feat)
    key_feat = key_feats.reshape(rows, heads, feat)
    labels = segment_ids + 1
    edge = jnp.concatenate(
        [
            keys[tail:],
            values[tail:],
            key_feats[tail:],
            jnp.broadcast_to(labels[tail:, None], (WMAX, 128)).astype(keys.dtype),
        ],
        axis=1,
    )
    count = lax.axis_size("seq")
    longest = count * rows // 2
    reach = min(count - 1, (longest + rows - 2) // rows)
    own_ends = jnp.stack([labels[0], labels[-1]])

    def gathered(after):
        if after is None:
            return own_ends
        tied, after = lax.optimization_barrier((own_ends, after))
        return lax.all_gather(tied, "seq")

    carried, mark, halo, ends = carried_in(
        packed(key_summary(key_feat, value_rows, labels)), gathered, "seq", reach, False, edge
    )
    carry = unpacked(carried, mark, heads, feat)
    halo_key = halo[:, : heads * head_dim].reshape(WMAX, heads, head_dim)
    halo_value = halo[:, heads * head_dim : 2 * heads * head_dim].reshape(WMAX, heads, head_dim)
    halo_feat = halo[:, 2 * heads * head_dim : 2 * heads * head_dim + heads * feat].reshape(
        WMAX, heads, feat
    )
    halo_label = halo[:, -1].astype(jnp.int32)
    key_ext = jnp.concatenate([halo_key, key_rows], axis=0)
    value_ext = jnp.concatenate([halo_value, value_rows], axis=0)
    feat_ext = jnp.concatenate([halo_feat, key_feat], axis=0)
    label_ext = jnp.concatenate([halo_label, labels], axis=0)
    query_grad, feat_grad, maxima, denominator, deltas, ratios, pieces = forward_block(
        query_rows,
        query_feat,
        grad_rows,
        key_ext,
        value_ext,
        feat_ext,
        labels,
        label_ext,
        windows,
        carry,
    )
    summed, mark, unused, ends = carried_in(
        packed(query_summary(query_feat, grad_rows, labels, ratios, deltas)),
        ends,
        "seq",
        reach,
        True,
    )
    summary = unpacked(summed, mark, heads, feat)
    weight_low, score_grad, kernel_grad, kernel_scaled = pieces
    key_full, value_full, kfeat_full = key_side(
        query_rows, query_feat, grad_rows, weight_low, score_grad, kernel_grad, kernel_scaled
    )
    rim = jnp.concatenate([key_full[:WMAX], value_full[:WMAX], kfeat_full[:WMAX]], axis=1)
    rim = passed_along(rim.astype(jnp.bfloat16), "seq", -1).astype(jnp.float32)
    back_key, back_value, back_feat = (
        rim[:, :heads],
        rim[:, heads : 2 * heads],
        rim[:, 2 * heads :],
    )
    key_grad = key_full[WMAX:]
    value_grad = value_full[WMAX:]
    kfeat_grad = kfeat_full[WMAX:]
    key_grad = jnp.concatenate([key_grad[:tail], key_grad[tail:] + back_key], axis=0)
    value_grad = jnp.concatenate([value_grad[:tail], value_grad[tail:] + back_value], axis=0)
    kfeat_grad = jnp.concatenate([kfeat_grad[:tail], kfeat_grad[tail:] + back_feat], axis=0)
    value_grad, kfeat_grad = apply_reverse(
        value_grad, kfeat_grad, key_feat, value_rows, labels, summary
    )
    return (
        query_grad.reshape(rows, heads * head_dim).astype(jnp.bfloat16),
        key_grad.reshape(rows, heads * head_dim).astype(jnp.bfloat16),
        value_grad.reshape(rows, heads * head_dim).astype(jnp.bfloat16),
        feat_grad.reshape(rows, heads * feat).astype(jnp.bfloat16),
        kfeat_grad.reshape(rows, heads * feat).astype(jnp.bfloat16),
    )


def solution(mesh):
    in_specs = (
        P(("group", "seq"), None),
        P(("group", "seq"), None),
        P(("group", "seq"), None),
        P(("group", "seq"), None),
        P(("group", "seq"), None),
        P(("group", "seq"), None),
        P(("group", "seq")),
        P("group"),
    )
    out_specs = (
        P(("group", "seq"), None),
        P(("group", "seq"), None),
        P(("group", "seq"), None),
        P(("group", "seq"), None),
        P(("group", "seq"), None),
    )
    return jax.shard_map(
        per_device, mesh=mesh, in_specs=in_specs, out_specs=out_specs, check_vma=False
    )
```

```python
import math

import jax
import jax.numpy as jnp
from jax import lax
from jax.sharding import PartitionSpec as P

WMAX = 64


def passed_along(value, axis, steps):
    count = lax.axis_size(axis)
    leading, last = (max(0, -steps), min(count, count - steps))
    return lax.ppermute(value, axis, [(source, source + steps) for source in range(leading, last)])


def packed(summary):
    state, total = summary[:2]
    heads, feat, width = state.shape
    half = heads // 2
    rows = [state.reshape(2, half * feat, width), total.reshape(2, half, width)]
    return jnp.concatenate(rows, axis=1)


def unpacked(payload, mark, heads, feat):
    width = payload.shape[2]
    half = heads // 2
    state = payload[:, : half * feat].reshape(heads, feat, width)
    total = payload[:, half * feat : half * feat + half].reshape(heads, width)
    return (state, total, mark)


def join_kept(earlier, later, keep):
    return later + keep.astype(jnp.float32) * earlier


def swapped(value, axis):
    count = lax.axis_size(axis)
    pairs = [(device, device ^ 1) for device in range(count)]
    return lax.ppermute(value, axis, pairs)


def carried_in(value, ends, axis, reach, backward, rider=None):
    if callable(ends):
        own = ends(None)
        partner = swapped(own, axis)
        first_keep = own[0 if backward else 1] == partner[0 if backward else 1]
    else:
        first_keep = None
    count = lax.axis_size(axis)
    step = -1 if backward else 1
    device = lax.axis_index(axis)
    parity = device % 2
    spot = count - 1 - device if backward else device
    chip_at = spot // 2

    def mark_at(place):
        inside = (place >= 0) & (place < count)
        real = count - 1 - place if backward else place
        found = ends[jnp.clip(real, 0, count - 1), 0 if backward else 1]
        return jnp.where(inside, found, 0)

    def chip_mark(chip):
        return mark_at(2 * chip + 1)

    def kept(far, near):
        return (far == near) | (near == 0)

    is_first = spot % 2 == 0
    own_half = lax.dynamic_index_in_dim(value, parity, 0, keepdims=False)
    other_half = lax.dynamic_index_in_dim(value, 1 - parity, 0, keepdims=False)
    partner_half = swapped(other_half, axis)
    if rider is not None and not backward:
        rider, partner_half = lax.optimization_barrier((rider, partner_half))
        rider = passed_along(rider, axis, step)
    earlier = jnp.where(is_first, own_half, partner_half)
    later = jnp.where(is_first, partner_half, own_half)
    if first_keep is None:
        first_keep = kept(mark_at(2 * chip_at), mark_at(2 * chip_at + 1))
    chip = join_kept(earlier, later, first_keep)
    if callable(ends):
        ends = ends(chip)
    chips = (reach + 1) // 2
    total = passed_along(chip, axis, 2 * step)
    length = 1
    if chips >= 2:
        keep = kept(chip_mark(chip_at - 2), chip_mark(chip_at - 1))
        total = join_kept(passed_along(chip, axis, 4 * step), total, keep)
        length = 2
    while length < chips:
        keep = kept(chip_mark(chip_at - length - 1), chip_mark(chip_at - 1))
        total = join_kept(passed_along(total, axis, 2 * length * step), total, keep)
        length *= 2
    if rider is not None and backward:
        rider, total = lax.optimization_barrier((rider, total))
        rider = passed_along(rider, axis, step)
    extended = join_kept(total, earlier, kept(chip_mark(chip_at - 1), mark_at(2 * chip_at)))
    mine = jnp.where(is_first, total, extended)
    theirs = swapped(jnp.where(is_first, extended, total), axis)
    whole = jnp.where(parity == 0, jnp.stack([mine, theirs]), jnp.stack([theirs, mine]))
    return (whole, mark_at(spot - 1), rider, ends)


def quick_product(form, left, right):
    return jnp.einsum(form, left, right, preferred_element_type=jnp.float32)


def exact_product(form, left, right):
    return jnp.einsum(
        form,
        left.astype(jnp.float32),
        right.astype(jnp.float32),
        precision=lax.Precision.HIGHEST,
        preferred_element_type=jnp.float32,
    )


def pair_masks(labels_q, labels_k, windows, offset):
    distance = (
        jnp.arange(labels_q.shape[0], dtype=jnp.int32)[:, None]
        + offset
        - jnp.arange(labels_k.shape[0], dtype=jnp.int32)[None, :]
    )
    matched = (labels_q[:, None] == labels_k[None, :]) & (labels_q[:, None] > 0) & (distance >= 0)
    inside = matched[None] & (distance[None] < windows[:, None, None])
    is_local = (jnp.arange(labels_k.shape[0], dtype=jnp.int32) >= offset)[None, None, :]
    far_sign = jnp.where(
        is_local, (matched[None] & ~inside).astype(jnp.float32), -inside.astype(jnp.float32)
    )
    return (inside, far_sign)


def pair_scores(query_rows, query_feat, key_ext, feat_ext, labels_q, labels_k, windows, offset):
    inside, far_sign = pair_masks(labels_q, labels_k, windows, offset)
    scale = 1.0 / math.sqrt(query_rows.shape[2])
    score = quick_product("thd,ehd->hte", query_rows, key_ext) * scale
    kernel = quick_product("thf,ehf->hte", query_feat, feat_ext) * far_sign
    return (inside, far_sign, score, kernel)


def pair_grads(probability, kernel, far_sign, ratios, deltas, grad_rows, value_ext):
    weight_grad = quick_product("thd,ehd->hte", grad_rows, value_ext) - deltas[:, :, None]
    score_grad = (probability * weight_grad).astype(jnp.bfloat16)
    kernel_grad = weight_grad * ratios[:, :, None] * far_sign
    return (score_grad, kernel_grad, kernel * ratios[:, :, None])


def key_side(query_rows, query_feat, grad_rows, weight_low, score_grad, kernel_grad, kernel_scaled):
    scale = 1.0 / math.sqrt(query_rows.shape[2])
    key_grad = quick_product("hte,thd->ehd", score_grad, query_rows) * scale
    value_grad = quick_product("hte,thd->ehd", weight_low, grad_rows) + exact_product(
        "hte,thd->ehd", kernel_scaled, grad_rows
    )
    kfeat_grad = exact_product("hte,thf->ehf", kernel_grad, query_feat)
    return (key_grad, value_grad, kfeat_grad)


def forward_block(
    query_rows,
    query_feat,
    grad_rows,
    key_ext,
    value_ext,
    feat_ext,
    labels_q,
    labels_k,
    windows,
    carry,
):
    carry_state, carry_sum, carry_mark = carry
    offset = key_ext.shape[0] - query_rows.shape[0]
    scale = 1.0 / math.sqrt(query_rows.shape[2])
    inside, far_sign, score, kernel = pair_scores(
        query_rows, query_feat, key_ext, feat_ext, labels_q, labels_k, windows, offset
    )
    maxima = jnp.max(jnp.where(inside, score, -jnp.inf), axis=2)
    shrink = jnp.exp(-maxima)
    carry_on = (labels_q == carry_mark).astype(jnp.float32)
    carry_den = exact_product("thf,hf->ht", query_feat, carry_sum) * carry_on[None, :]
    carry_num = exact_product("thf,hfd->htd", query_feat, carry_state) * carry_on[None, :, None]
    powered = jnp.where(inside, jnp.exp(score - maxima[:, :, None]), 0.0)
    denominator = jnp.sum(powered, axis=2) + shrink * (jnp.sum(kernel, axis=2) + carry_den)
    ratios = shrink / denominator
    probability = powered / denominator[:, :, None]
    weight_low = probability.astype(jnp.bfloat16)
    attended = quick_product("hte,ehd->htd", weight_low, value_ext) + ratios[:, :, None] * (
        exact_product("hte,ehd->htd", kernel, value_ext) + carry_num
    )
    grad_wide = grad_rows.astype(jnp.float32)
    deltas = jnp.sum(jnp.transpose(grad_wide, (1, 0, 2)) * attended, axis=2)
    score_grad, kernel_grad, kernel_scaled = pair_grads(
        probability, kernel, far_sign, ratios, deltas, grad_rows, value_ext
    )
    query_grad = quick_product("hte,ehd->thd", score_grad, key_ext) * scale
    carry_term = (
        exact_product("hfd,thd->thf", carry_state, grad_rows)
        - deltas.T[:, :, None] * carry_sum[None]
    )
    feat_grad = (
        exact_product("hte,ehf->thf", kernel_grad, feat_ext)
        + (carry_on[:, None] * ratios.T)[:, :, None] * carry_term
    )
    return (
        query_grad,
        feat_grad,
        maxima,
        denominator,
        deltas,
        ratios,
        (weight_low, score_grad, kernel_grad, kernel_scaled),
    )


def key_summary(key_feat, value_rows, labels):
    keep = labels == labels[-1]
    state = quick_product(
        "thf,thd->hfd", key_feat * keep.astype(jnp.bfloat16)[:, None, None], value_rows
    )
    total = jnp.sum(key_feat.astype(jnp.float32) * keep.astype(jnp.float32)[:, None, None], axis=0)
    return (state, total, labels[-1])


def query_summary(query_feat, grad_rows, labels, ratios, deltas):
    use = (labels == labels[0]).astype(jnp.float32)[:, None] * ratios.T
    weighted = query_feat.astype(jnp.float32) * use[:, :, None]
    state = exact_product("thf,thd->hfd", weighted, grad_rows)
    total = jnp.sum(weighted * deltas.T[:, :, None], axis=0)
    return (state, total, labels[0])


def combine_pair(earlier, later):
    keep = ((earlier[2] == later[2]) | (later[2] == 0)).astype(jnp.float32)
    state = later[0] + keep.reshape(keep.shape + (1, 1, 1)) * earlier[0]
    total = later[1] + keep.reshape(keep.shape + (1, 1)) * earlier[1]
    mark = jnp.where(later[2] == 0, earlier[2], later[2])
    return (state, total, mark)


def apply_reverse(value_grad, kfeat_grad, key_feat, value_rows, labels, summary):
    state, total, mark = summary
    use = (labels == mark).astype(jnp.float32)[:, None, None]
    value_grad = value_grad + use * exact_product("hfd,thf->thd", state, key_feat)
    kfeat_grad = kfeat_grad + use * (exact_product("hfd,thd->thf", state, value_rows) - total[None])
    return (value_grad, kfeat_grad)


def per_device(queries, keys, values, out_grad, query_feats, key_feats, segment_ids, windows):
    rows = queries.shape[0]
    heads = windows.shape[0]
    head_dim = queries.shape[1] // heads
    feat = query_feats.shape[1] // heads
    tail = rows - WMAX
    query_rows = queries.reshape(rows, heads, head_dim)
    key_rows = keys.reshape(rows, heads, head_dim)
    value_rows = values.reshape(rows, heads, head_dim)
    grad_rows = out_grad.reshape(rows, heads, head_dim)
    query_feat = query_feats.reshape(rows, heads, feat)
    key_feat = key_feats.reshape(rows, heads, feat)
    labels = segment_ids + 1
    edge = jnp.concatenate(
        [
            keys[tail:],
            values[tail:],
            key_feats[tail:],
            jnp.broadcast_to(labels[tail:, None], (WMAX, 128)).astype(keys.dtype),
        ],
        axis=1,
    )
    count = lax.axis_size("seq")
    longest = count * rows // 2
    reach = min(count - 1, (longest + rows - 2) // rows)
    own_ends = jnp.stack([labels[0], labels[-1]])

    def gathered(after):
        if after is None:
            return own_ends
        tied, after = lax.optimization_barrier((own_ends, after))
        return lax.all_gather(tied, "seq")

    carried, mark, halo, ends = carried_in(
        packed(key_summary(key_feat, value_rows, labels)), gathered, "seq", reach, False, edge
    )
    carry = unpacked(carried, mark, heads, feat)
    halo_key = halo[:, : heads * head_dim].reshape(WMAX, heads, head_dim)
    halo_value = halo[:, heads * head_dim : 2 * heads * head_dim].reshape(WMAX, heads, head_dim)
    halo_feat = halo[:, 2 * heads * head_dim : 2 * heads * head_dim + heads * feat].reshape(
        WMAX, heads, feat
    )
    halo_label = halo[:, -1].astype(jnp.int32)
    key_ext = jnp.concatenate([halo_key, key_rows], axis=0)
    value_ext = jnp.concatenate([halo_value, value_rows], axis=0)
    feat_ext = jnp.concatenate([halo_feat, key_feat], axis=0)
    label_ext = jnp.concatenate([halo_label, labels], axis=0)
    query_grad, feat_grad, maxima, denominator, deltas, ratios, pieces = forward_block(
        query_rows,
        query_feat,
        grad_rows,
        key_ext,
        value_ext,
        feat_ext,
        labels,
        label_ext,
        windows,
        carry,
    )
    weight_low, score_grad, kernel_grad, kernel_scaled = pieces
    key_full, value_full, kfeat_full = key_side(
        query_rows, query_feat, grad_rows, weight_low, score_grad, kernel_grad, kernel_scaled
    )
    rim = jnp.concatenate([key_full[:WMAX], value_full[:WMAX], kfeat_full[:WMAX]], axis=1)
    summed, mark, rim, ends = carried_in(
        packed(query_summary(query_feat, grad_rows, labels, ratios, deltas)),
        ends,
        "seq",
        reach,
        True,
        rim.astype(jnp.bfloat16),
    )
    rim = rim.astype(jnp.float32)
    summary = unpacked(summed, mark, heads, feat)
    back_key, back_value, back_feat = (
        rim[:, :heads],
        rim[:, heads : 2 * heads],
        rim[:, 2 * heads :],
    )
    key_grad = key_full[WMAX:]
    value_grad = value_full[WMAX:]
    kfeat_grad = kfeat_full[WMAX:]
    key_grad = jnp.concatenate([key_grad[:tail], key_grad[tail:] + back_key], axis=0)
    value_grad = jnp.concatenate([value_grad[:tail], value_grad[tail:] + back_value], axis=0)
    kfeat_grad = jnp.concatenate([kfeat_grad[:tail], kfeat_grad[tail:] + back_feat], axis=0)
    value_grad, kfeat_grad = apply_reverse(
        value_grad, kfeat_grad, key_feat, value_rows, labels, summary
    )
    return (
        query_grad.reshape(rows, heads * head_dim).astype(jnp.bfloat16),
        key_grad.reshape(rows, heads * head_dim).astype(jnp.bfloat16),
        value_grad.reshape(rows, heads * head_dim).astype(jnp.bfloat16),
        feat_grad.reshape(rows, heads * feat).astype(jnp.bfloat16),
        kfeat_grad.reshape(rows, heads * feat).astype(jnp.bfloat16),
    )


def solution(mesh):
    in_specs = (
        P(("group", "seq"), None),
        P(("group", "seq"), None),
        P(("group", "seq"), None),
        P(("group", "seq"), None),
        P(("group", "seq"), None),
        P(("group", "seq"), None),
        P(("group", "seq")),
        P("group"),
    )
    out_specs = (
        P(("group", "seq"), None),
        P(("group", "seq"), None),
        P(("group", "seq"), None),
        P(("group", "seq"), None),
        P(("group", "seq"), None),
    )
    return jax.shard_map(
        per_device, mesh=mesh, in_specs=in_specs, out_specs=out_specs, check_vma=False
    )
```

```python
import math

import jax
import jax.numpy as jnp
from jax import lax
from jax.sharding import PartitionSpec as P

WMAX = 64


def passed_along(value, axis, steps):
    count = lax.axis_size(axis)
    leading, last = (max(0, -steps), min(count, count - steps))
    return lax.ppermute(value, axis, [(source, source + steps) for source in range(leading, last)])


def packed(summary):
    state, total = summary[:2]
    heads, feat, width = state.shape
    half = heads // 2
    rows = [state.reshape(2, half * feat, width), total.reshape(2, half, width)]
    return jnp.concatenate(rows, axis=1)


def unpacked(payload, mark, heads, feat):
    width = payload.shape[2]
    half = heads // 2
    state = payload[:, : half * feat].reshape(heads, feat, width)
    total = payload[:, half * feat : half * feat + half].reshape(heads, width)
    return (state, total, mark)


def join_kept(earlier, later, keep):
    return later + keep.astype(jnp.float32) * earlier


def swapped(value, axis):
    count = lax.axis_size(axis)
    pairs = [(device, device ^ 1) for device in range(count)]
    return lax.ppermute(value, axis, pairs)


def carried_in(value, ends, axis, reach, backward, rider=None):
    if callable(ends):
        own = ends(None)
        partner = swapped(own, axis)
        first_keep = own[0 if backward else 1] == partner[0 if backward else 1]
    else:
        first_keep = None
    count = lax.axis_size(axis)
    step = -1 if backward else 1
    device = lax.axis_index(axis)
    parity = device % 2
    spot = count - 1 - device if backward else device
    chip_at = spot // 2

    def mark_at(place):
        inside = (place >= 0) & (place < count)
        real = count - 1 - place if backward else place
        found = ends[jnp.clip(real, 0, count - 1), 0 if backward else 1]
        return jnp.where(inside, found, 0)

    def chip_mark(chip):
        return mark_at(2 * chip + 1)

    def kept(far, near):
        return (far == near) | (near == 0)

    is_first = spot % 2 == 0
    own_half = lax.dynamic_index_in_dim(value, parity, 0, keepdims=False)
    other_half = lax.dynamic_index_in_dim(value, 1 - parity, 0, keepdims=False)
    partner_half = swapped(other_half, axis)
    if rider is not None:
        rider, partner_half = lax.optimization_barrier((rider, partner_half))
        rider = passed_along(rider, axis, step)
    earlier = jnp.where(is_first, own_half, partner_half)
    later = jnp.where(is_first, partner_half, own_half)
    if first_keep is None:
        first_keep = kept(mark_at(2 * chip_at), mark_at(2 * chip_at + 1))
    chip = join_kept(earlier, later, first_keep)
    if callable(ends):
        ends = ends(chip)
    chips = (reach + 1) // 2
    total = passed_along(chip, axis, 2 * step)
    length = 1
    while length < chips:
        keep = kept(chip_mark(chip_at - length - 1), chip_mark(chip_at - 1))
        total = join_kept(passed_along(total, axis, 2 * length * step), total, keep)
        length *= 2
    extended = join_kept(total, earlier, kept(chip_mark(chip_at - 1), mark_at(2 * chip_at)))
    mine = jnp.where(is_first, total, extended)
    theirs = swapped(jnp.where(is_first, extended, total), axis)
    whole = jnp.where(parity == 0, jnp.stack([mine, theirs]), jnp.stack([theirs, mine]))
    return (whole, mark_at(spot - 1), rider, ends)


def quick_product(form, left, right):
    return jnp.einsum(form, left, right, preferred_element_type=jnp.float32)


def exact_product(form, left, right):
    return jnp.einsum(
        form,
        left.astype(jnp.float32),
        right.astype(jnp.float32),
        precision=lax.Precision.HIGHEST,
        preferred_element_type=jnp.float32,
    )


def pair_masks(labels_q, labels_k, windows, offset):
    distance = (
        jnp.arange(labels_q.shape[0], dtype=jnp.int32)[:, None]
        + offset
        - jnp.arange(labels_k.shape[0], dtype=jnp.int32)[None, :]
    )
    matched = (labels_q[:, None] == labels_k[None, :]) & (labels_q[:, None] > 0) & (distance >= 0)
    inside = matched[None] & (distance[None] < windows[:, None, None])
    is_local = (jnp.arange(labels_k.shape[0], dtype=jnp.int32) >= offset)[None, None, :]
    far_sign = jnp.where(
        is_local, (matched[None] & ~inside).astype(jnp.float32), -inside.astype(jnp.float32)
    )
    return (inside, far_sign)


def pair_scores(query_rows, query_feat, key_ext, feat_ext, labels_q, labels_k, windows, offset):
    inside, far_sign = pair_masks(labels_q, labels_k, windows, offset)
    scale = 1.0 / math.sqrt(query_rows.shape[2])
    score = quick_product("thd,ehd->hte", query_rows, key_ext) * scale
    kernel = quick_product("thf,ehf->hte", query_feat, feat_ext) * far_sign
    return (inside, far_sign, score, kernel)


def pair_grads(probability, kernel, far_sign, ratios, deltas, grad_rows, value_ext):
    weight_grad = quick_product("thd,ehd->hte", grad_rows, value_ext) - deltas[:, :, None]
    score_grad = (probability * weight_grad).astype(jnp.bfloat16)
    kernel_grad = weight_grad * ratios[:, :, None] * far_sign
    return (score_grad, kernel_grad, kernel * ratios[:, :, None])


def key_side(query_rows, query_feat, grad_rows, weight_low, score_grad, kernel_grad, kernel_scaled):
    scale = 1.0 / math.sqrt(query_rows.shape[2])
    key_grad = quick_product("hte,thd->ehd", score_grad, query_rows) * scale
    value_grad = quick_product("hte,thd->ehd", weight_low, grad_rows) + exact_product(
        "hte,thd->ehd", kernel_scaled, grad_rows
    )
    kfeat_grad = exact_product("hte,thf->ehf", kernel_grad, query_feat)
    return (key_grad, value_grad, kfeat_grad)


def forward_block(
    query_rows,
    query_feat,
    grad_rows,
    key_ext,
    value_ext,
    feat_ext,
    labels_q,
    labels_k,
    windows,
    carry,
):
    carry_state, carry_sum, carry_mark = carry
    offset = key_ext.shape[0] - query_rows.shape[0]
    scale = 1.0 / math.sqrt(query_rows.shape[2])
    inside, far_sign, score, kernel = pair_scores(
        query_rows, query_feat, key_ext, feat_ext, labels_q, labels_k, windows, offset
    )
    maxima = jnp.max(jnp.where(inside, score, -jnp.inf), axis=2)
    shrink = jnp.exp(-maxima)
    carry_on = (labels_q == carry_mark).astype(jnp.float32)
    carry_den = exact_product("thf,hf->ht", query_feat, carry_sum) * carry_on[None, :]
    carry_num = exact_product("thf,hfd->htd", query_feat, carry_state) * carry_on[None, :, None]
    powered = jnp.where(inside, jnp.exp(score - maxima[:, :, None]), 0.0)
    denominator = jnp.sum(powered, axis=2) + shrink * (jnp.sum(kernel, axis=2) + carry_den)
    ratios = shrink / denominator
    probability = powered / denominator[:, :, None]
    weight_low = probability.astype(jnp.bfloat16)
    attended = quick_product("hte,ehd->htd", weight_low, value_ext) + ratios[:, :, None] * (
        exact_product("hte,ehd->htd", kernel, value_ext) + carry_num
    )
    grad_wide = grad_rows.astype(jnp.float32)
    deltas = jnp.sum(jnp.transpose(grad_wide, (1, 0, 2)) * attended, axis=2)
    score_grad, kernel_grad, kernel_scaled = pair_grads(
        probability, kernel, far_sign, ratios, deltas, grad_rows, value_ext
    )
    query_grad = quick_product("hte,ehd->thd", score_grad, key_ext) * scale
    carry_term = (
        exact_product("hfd,thd->thf", carry_state, grad_rows)
        - deltas.T[:, :, None] * carry_sum[None]
    )
    feat_grad = (
        exact_product("hte,ehf->thf", kernel_grad, feat_ext)
        + (carry_on[:, None] * ratios.T)[:, :, None] * carry_term
    )
    return (
        query_grad,
        feat_grad,
        maxima,
        denominator,
        deltas,
        ratios,
        (weight_low, score_grad, kernel_grad, kernel_scaled),
    )


def key_summary(key_feat, value_rows, labels):
    keep = labels == labels[-1]
    state = quick_product(
        "thf,thd->hfd", key_feat * keep.astype(jnp.bfloat16)[:, None, None], value_rows
    )
    total = jnp.sum(key_feat.astype(jnp.float32) * keep.astype(jnp.float32)[:, None, None], axis=0)
    return (state, total, labels[-1])


def query_summary(query_feat, grad_rows, labels, ratios, deltas):
    use = (labels == labels[0]).astype(jnp.float32)[:, None] * ratios.T
    weighted = query_feat.astype(jnp.float32) * use[:, :, None]
    state = exact_product("thf,thd->hfd", weighted, grad_rows)
    total = jnp.sum(weighted * deltas.T[:, :, None], axis=0)
    return (state, total, labels[0])


def combine_pair(earlier, later):
    keep = ((earlier[2] == later[2]) | (later[2] == 0)).astype(jnp.float32)
    state = later[0] + keep.reshape(keep.shape + (1, 1, 1)) * earlier[0]
    total = later[1] + keep.reshape(keep.shape + (1, 1)) * earlier[1]
    mark = jnp.where(later[2] == 0, earlier[2], later[2])
    return (state, total, mark)


def apply_reverse(value_grad, kfeat_grad, key_feat, value_rows, labels, summary):
    state, total, mark = summary
    use = (labels == mark).astype(jnp.float32)[:, None, None]
    value_grad = value_grad + use * exact_product("hfd,thf->thd", state, key_feat)
    kfeat_grad = kfeat_grad + use * (exact_product("hfd,thd->thf", state, value_rows) - total[None])
    return (value_grad, kfeat_grad)


def per_device(queries, keys, values, out_grad, query_feats, key_feats, segment_ids, windows):
    rows = queries.shape[0]
    heads = windows.shape[0]
    head_dim = queries.shape[1] // heads
    feat = query_feats.shape[1] // heads
    tail = rows - WMAX
    query_rows = queries.reshape(rows, heads, head_dim)
    key_rows = keys.reshape(rows, heads, head_dim)
    value_rows = values.reshape(rows, heads, head_dim)
    grad_rows = out_grad.reshape(rows, heads, head_dim)
    query_feat = query_feats.reshape(rows, heads, feat)
    key_feat = key_feats.reshape(rows, heads, feat)
    labels = segment_ids + 1
    edge = jnp.concatenate(
        [
            keys[tail:],
            values[tail:],
            key_feats[tail:],
            jnp.broadcast_to(labels[tail:, None], (WMAX, 128)).astype(keys.dtype),
        ],
        axis=1,
    )
    count = lax.axis_size("seq")
    longest = count * rows // 2
    reach = min(count - 1, (longest + rows - 2) // rows)
    own_ends = jnp.stack([labels[0], labels[-1]])

    def gathered(after):
        if after is None:
            return own_ends
        tied, after = lax.optimization_barrier((own_ends, after))
        return lax.all_gather(tied, "seq")

    carried, mark, halo, ends = carried_in(
        packed(key_summary(key_feat, value_rows, labels)), gathered, "seq", reach, False, edge
    )
    carry = unpacked(carried, mark, heads, feat)
    halo_key = halo[:, : heads * head_dim].reshape(WMAX, heads, head_dim)
    halo_value = halo[:, heads * head_dim : 2 * heads * head_dim].reshape(WMAX, heads, head_dim)
    halo_feat = halo[:, 2 * heads * head_dim : 2 * heads * head_dim + heads * feat].reshape(
        WMAX, heads, feat
    )
    halo_label = halo[:, -1].astype(jnp.int32)
    key_ext = jnp.concatenate([halo_key, key_rows], axis=0)
    value_ext = jnp.concatenate([halo_value, value_rows], axis=0)
    feat_ext = jnp.concatenate([halo_feat, key_feat], axis=0)
    label_ext = jnp.concatenate([halo_label, labels], axis=0)
    query_grad, feat_grad, maxima, denominator, deltas, ratios, pieces = forward_block(
        query_rows,
        query_feat,
        grad_rows,
        key_ext,
        value_ext,
        feat_ext,
        labels,
        label_ext,
        windows,
        carry,
    )
    summed, mark, unused, ends = carried_in(
        packed(query_summary(query_feat, grad_rows, labels, ratios, deltas)),
        ends,
        "seq",
        reach,
        True,
    )
    summary = unpacked(summed, mark, heads, feat)
    weight_low, score_grad, kernel_grad, kernel_scaled = pieces
    key_full, value_full, kfeat_full = key_side(
        query_rows, query_feat, grad_rows, weight_low, score_grad, kernel_grad, kernel_scaled
    )
    rim = jnp.concatenate([key_full[:WMAX], value_full[:WMAX], kfeat_full[:WMAX]], axis=1)
    rim = passed_along(rim.astype(jnp.bfloat16), "seq", -1).astype(jnp.float32)
    back_key, back_value, back_feat = (
        rim[:, :heads],
        rim[:, heads : 2 * heads],
        rim[:, 2 * heads :],
    )
    key_grad = key_full[WMAX:]
    value_grad = value_full[WMAX:]
    kfeat_grad = kfeat_full[WMAX:]
    key_grad = jnp.concatenate([key_grad[:tail], key_grad[tail:] + back_key], axis=0)
    value_grad = jnp.concatenate([value_grad[:tail], value_grad[tail:] + back_value], axis=0)
    kfeat_grad = jnp.concatenate([kfeat_grad[:tail], kfeat_grad[tail:] + back_feat], axis=0)
    value_grad, kfeat_grad = apply_reverse(
        value_grad, kfeat_grad, key_feat, value_rows, labels, summary
    )
    return (
        query_grad.reshape(rows, heads * head_dim).astype(jnp.bfloat16),
        key_grad.reshape(rows, heads * head_dim).astype(jnp.bfloat16),
        value_grad.reshape(rows, heads * head_dim).astype(jnp.bfloat16),
        feat_grad.reshape(rows, heads * feat).astype(jnp.bfloat16),
        kfeat_grad.reshape(rows, heads * feat).astype(jnp.bfloat16),
    )


def solution(mesh):
    in_specs = (
        P(("group", "seq"), None),
        P(("group", "seq"), None),
        P(("group", "seq"), None),
        P(("group", "seq"), None),
        P(("group", "seq"), None),
        P(("group", "seq"), None),
        P(("group", "seq")),
        P("group"),
    )
    out_specs = (
        P(("group", "seq"), None),
        P(("group", "seq"), None),
        P(("group", "seq"), None),
        P(("group", "seq"), None),
        P(("group", "seq"), None),
    )
    return jax.shard_map(
        per_device, mesh=mesh, in_specs=in_specs, out_specs=out_specs, check_vma=False
    )
```

```python
import math

import jax
import jax.numpy as jnp
from jax import lax
from jax.sharding import PartitionSpec as P

WMAX = 64


def passed_along(value, axis, steps):
    count = lax.axis_size(axis)
    leading, last = (max(0, -steps), min(count, count - steps))
    return lax.ppermute(value, axis, [(source, source + steps) for source in range(leading, last)])


def packed(summary):
    state, total = summary[:2]
    heads, feat, width = state.shape
    half = heads // 2
    rows = [state.reshape(2, half * feat, width), total.reshape(2, half, width)]
    return jnp.concatenate(rows, axis=1)


def unpacked(payload, mark, heads, feat):
    width = payload.shape[2]
    half = heads // 2
    state = payload[:, : half * feat].reshape(heads, feat, width)
    total = payload[:, half * feat : half * feat + half].reshape(heads, width)
    return (state, total, mark)


def join_kept(earlier, later, keep):
    return later + keep.astype(jnp.float32) * earlier


def swapped(value, axis):
    count = lax.axis_size(axis)
    pairs = [(device, device ^ 1) for device in range(count)]
    return lax.ppermute(value, axis, pairs)


def carried_in(value, ends, axis, reach, backward, rider=None):
    if callable(ends):
        own = ends(None)
        partner = swapped(own, axis)
        first_keep = own[0 if backward else 1] == partner[0 if backward else 1]
    else:
        first_keep = None
    count = lax.axis_size(axis)
    step = -1 if backward else 1
    device = lax.axis_index(axis)
    parity = device % 2
    spot = count - 1 - device if backward else device
    chip_at = spot // 2

    def mark_at(place):
        inside = (place >= 0) & (place < count)
        real = count - 1 - place if backward else place
        found = ends[jnp.clip(real, 0, count - 1), 0 if backward else 1]
        return jnp.where(inside, found, 0)

    def chip_mark(chip):
        return mark_at(2 * chip + 1)

    def kept(far, near):
        return (far == near) | (near == 0)

    is_first = spot % 2 == 0
    own_half = lax.dynamic_index_in_dim(value, parity, 0, keepdims=False)
    other_half = lax.dynamic_index_in_dim(value, 1 - parity, 0, keepdims=False)
    partner_half = swapped(other_half, axis)
    if rider is not None:
        rider, partner_half = lax.optimization_barrier((rider, partner_half))
        rider = passed_along(rider, axis, step)
    earlier = jnp.where(is_first, own_half, partner_half)
    later = jnp.where(is_first, partner_half, own_half)
    if first_keep is None:
        first_keep = kept(mark_at(2 * chip_at), mark_at(2 * chip_at + 1))
    chip = join_kept(earlier, later, first_keep)
    if callable(ends):
        ends = ends(chip)
    chips = (reach + 1) // 2
    total = passed_along(chip, axis, 2 * step)
    length = 1
    if chips >= 2:
        keep = kept(chip_mark(chip_at - 2), chip_mark(chip_at - 1))
        total = join_kept(passed_along(chip, axis, 4 * step), total, keep)
        length = 2
    while length < chips:
        keep = kept(chip_mark(chip_at - length - 1), chip_mark(chip_at - 1))
        total = join_kept(passed_along(total, axis, 2 * length * step), total, keep)
        length *= 2
    extended = join_kept(total, earlier, kept(chip_mark(chip_at - 1), mark_at(2 * chip_at)))
    mine = jnp.where(is_first, total, extended)
    theirs = swapped(jnp.where(is_first, extended, total), axis)
    whole = lax.dynamic_update_index_in_dim(jnp.stack([theirs, theirs]), mine, parity, 0)
    return (whole, mark_at(spot - 1), rider, ends)


def quick_product(form, left, right):
    return jnp.einsum(form, left, right, preferred_element_type=jnp.float32)


def exact_product(form, left, right):
    return jnp.einsum(
        form,
        left.astype(jnp.float32),
        right.astype(jnp.float32),
        precision=lax.Precision.HIGHEST,
        preferred_element_type=jnp.float32,
    )


def pair_masks(labels_q, labels_k, windows, offset):
    distance = (
        jnp.arange(labels_q.shape[0], dtype=jnp.int32)[:, None]
        + offset
        - jnp.arange(labels_k.shape[0], dtype=jnp.int32)[None, :]
    )
    matched = (labels_q[:, None] == labels_k[None, :]) & (labels_q[:, None] > 0) & (distance >= 0)
    inside = matched[None] & (distance[None] < windows[:, None, None])
    is_local = (jnp.arange(labels_k.shape[0], dtype=jnp.int32) >= offset)[None, None, :]
    far_sign = jnp.where(
        is_local, (matched[None] & ~inside).astype(jnp.float32), -inside.astype(jnp.float32)
    )
    return (inside, far_sign)


def pair_scores(query_rows, query_feat, key_ext, feat_ext, labels_q, labels_k, windows, offset):
    inside, far_sign = pair_masks(labels_q, labels_k, windows, offset)
    scale = 1.0 / math.sqrt(query_rows.shape[2])
    score = quick_product("thd,ehd->hte", query_rows, key_ext) * scale
    kernel = quick_product("thf,ehf->hte", query_feat, feat_ext) * far_sign
    return (inside, far_sign, score, kernel)


def pair_grads(probability, kernel, far_sign, ratios, deltas, grad_rows, value_ext):
    weight_grad = quick_product("thd,ehd->hte", grad_rows, value_ext) - deltas[:, :, None]
    score_grad = (probability * weight_grad).astype(jnp.bfloat16)
    kernel_grad = weight_grad * ratios[:, :, None] * far_sign
    return (score_grad, kernel_grad, kernel * ratios[:, :, None])


def key_side(query_rows, query_feat, grad_rows, weight_low, score_grad, kernel_grad, kernel_scaled):
    scale = 1.0 / math.sqrt(query_rows.shape[2])
    key_grad = quick_product("hte,thd->ehd", score_grad, query_rows) * scale
    value_grad = quick_product("hte,thd->ehd", weight_low, grad_rows) + exact_product(
        "hte,thd->ehd", kernel_scaled, grad_rows
    )
    kfeat_grad = exact_product("hte,thf->ehf", kernel_grad, query_feat)
    return (key_grad, value_grad, kfeat_grad)


def forward_block(
    query_rows,
    query_feat,
    grad_rows,
    key_ext,
    value_ext,
    feat_ext,
    labels_q,
    labels_k,
    windows,
    carry,
):
    carry_state, carry_sum, carry_mark = carry
    offset = key_ext.shape[0] - query_rows.shape[0]
    scale = 1.0 / math.sqrt(query_rows.shape[2])
    inside, far_sign, score, kernel = pair_scores(
        query_rows, query_feat, key_ext, feat_ext, labels_q, labels_k, windows, offset
    )
    maxima = jnp.max(jnp.where(inside, score, -jnp.inf), axis=2)
    shrink = jnp.exp(-maxima)
    carry_on = (labels_q == carry_mark).astype(jnp.float32)
    carry_den = exact_product("thf,hf->ht", query_feat, carry_sum) * carry_on[None, :]
    carry_num = exact_product("thf,hfd->htd", query_feat, carry_state) * carry_on[None, :, None]
    powered = jnp.where(inside, jnp.exp(score - maxima[:, :, None]), 0.0)
    denominator = jnp.sum(powered, axis=2) + shrink * (jnp.sum(kernel, axis=2) + carry_den)
    ratios = shrink / denominator
    probability = powered / denominator[:, :, None]
    weight_low = probability.astype(jnp.bfloat16)
    attended = quick_product("hte,ehd->htd", weight_low, value_ext) + ratios[:, :, None] * (
        exact_product("hte,ehd->htd", kernel, value_ext) + carry_num
    )
    grad_wide = grad_rows.astype(jnp.float32)
    deltas = jnp.sum(jnp.transpose(grad_wide, (1, 0, 2)) * attended, axis=2)
    score_grad, kernel_grad, kernel_scaled = pair_grads(
        probability, kernel, far_sign, ratios, deltas, grad_rows, value_ext
    )
    query_grad = quick_product("hte,ehd->thd", score_grad, key_ext) * scale
    carry_term = (
        exact_product("hfd,thd->thf", carry_state, grad_rows)
        - deltas.T[:, :, None] * carry_sum[None]
    )
    feat_grad = (
        exact_product("hte,ehf->thf", kernel_grad, feat_ext)
        + (carry_on[:, None] * ratios.T)[:, :, None] * carry_term
    )
    return (
        query_grad,
        feat_grad,
        maxima,
        denominator,
        deltas,
        ratios,
        (weight_low, score_grad, kernel_grad, kernel_scaled),
    )


def key_summary(key_feat, value_rows, labels):
    keep = labels == labels[-1]
    state = quick_product(
        "thf,thd->hfd", key_feat * keep.astype(jnp.bfloat16)[:, None, None], value_rows
    )
    total = jnp.sum(key_feat.astype(jnp.float32) * keep.astype(jnp.float32)[:, None, None], axis=0)
    return (state, total, labels[-1])


def query_summary(query_feat, grad_rows, labels, ratios, deltas):
    use = (labels == labels[0]).astype(jnp.float32)[:, None] * ratios.T
    weighted = query_feat.astype(jnp.float32) * use[:, :, None]
    state = exact_product("thf,thd->hfd", weighted, grad_rows)
    total = jnp.sum(weighted * deltas.T[:, :, None], axis=0)
    return (state, total, labels[0])


def combine_pair(earlier, later):
    keep = ((earlier[2] == later[2]) | (later[2] == 0)).astype(jnp.float32)
    state = later[0] + keep.reshape(keep.shape + (1, 1, 1)) * earlier[0]
    total = later[1] + keep.reshape(keep.shape + (1, 1)) * earlier[1]
    mark = jnp.where(later[2] == 0, earlier[2], later[2])
    return (state, total, mark)


def apply_reverse(value_grad, kfeat_grad, key_feat, value_rows, labels, summary):
    state, total, mark = summary
    use = (labels == mark).astype(jnp.float32)[:, None, None]
    value_grad = value_grad + use * exact_product("hfd,thf->thd", state, key_feat)
    kfeat_grad = kfeat_grad + use * (exact_product("hfd,thd->thf", state, value_rows) - total[None])
    return (value_grad, kfeat_grad)


def per_device(queries, keys, values, out_grad, query_feats, key_feats, segment_ids, windows):
    rows = queries.shape[0]
    heads = windows.shape[0]
    head_dim = queries.shape[1] // heads
    feat = query_feats.shape[1] // heads
    tail = rows - WMAX
    query_rows = queries.reshape(rows, heads, head_dim)
    key_rows = keys.reshape(rows, heads, head_dim)
    value_rows = values.reshape(rows, heads, head_dim)
    grad_rows = out_grad.reshape(rows, heads, head_dim)
    query_feat = query_feats.reshape(rows, heads, feat)
    key_feat = key_feats.reshape(rows, heads, feat)
    labels = segment_ids + 1
    edge = jnp.concatenate(
        [
            keys[tail:],
            values[tail:],
            key_feats[tail:],
            jnp.broadcast_to(labels[tail:, None], (WMAX, 128)).astype(keys.dtype),
        ],
        axis=1,
    )
    count = lax.axis_size("seq")
    longest = count * rows // 2
    reach = min(count - 1, (longest + rows - 2) // rows)
    own_ends = jnp.stack([labels[0], labels[-1]])

    def gathered(after):
        if after is None:
            return own_ends
        tied, after = lax.optimization_barrier((own_ends, after))
        return lax.all_gather(tied, "seq")

    carried, mark, halo, ends = carried_in(
        packed(key_summary(key_feat, value_rows, labels)), gathered, "seq", reach, False, edge
    )
    carry = unpacked(carried, mark, heads, feat)
    halo_key = halo[:, : heads * head_dim].reshape(WMAX, heads, head_dim)
    halo_value = halo[:, heads * head_dim : 2 * heads * head_dim].reshape(WMAX, heads, head_dim)
    halo_feat = halo[:, 2 * heads * head_dim : 2 * heads * head_dim + heads * feat].reshape(
        WMAX, heads, feat
    )
    halo_label = halo[:, -1].astype(jnp.int32)
    key_ext = jnp.concatenate([halo_key, key_rows], axis=0)
    value_ext = jnp.concatenate([halo_value, value_rows], axis=0)
    feat_ext = jnp.concatenate([halo_feat, key_feat], axis=0)
    label_ext = jnp.concatenate([halo_label, labels], axis=0)
    query_grad, feat_grad, maxima, denominator, deltas, ratios, pieces = forward_block(
        query_rows,
        query_feat,
        grad_rows,
        key_ext,
        value_ext,
        feat_ext,
        labels,
        label_ext,
        windows,
        carry,
    )
    summed, mark, unused, ends = carried_in(
        packed(query_summary(query_feat, grad_rows, labels, ratios, deltas)),
        ends,
        "seq",
        reach,
        True,
    )
    summary = unpacked(summed, mark, heads, feat)
    weight_low, score_grad, kernel_grad, kernel_scaled = pieces
    key_full, value_full, kfeat_full = key_side(
        query_rows, query_feat, grad_rows, weight_low, score_grad, kernel_grad, kernel_scaled
    )
    rim = jnp.concatenate([key_full[:WMAX], value_full[:WMAX], kfeat_full[:WMAX]], axis=1)
    rim = passed_along(rim.astype(jnp.bfloat16), "seq", -1).astype(jnp.float32)
    back_key, back_value, back_feat = (
        rim[:, :heads],
        rim[:, heads : 2 * heads],
        rim[:, 2 * heads :],
    )
    key_grad = key_full[WMAX:]
    value_grad = value_full[WMAX:]
    kfeat_grad = kfeat_full[WMAX:]
    key_grad = jnp.concatenate([key_grad[:tail], key_grad[tail:] + back_key], axis=0)
    value_grad = jnp.concatenate([value_grad[:tail], value_grad[tail:] + back_value], axis=0)
    kfeat_grad = jnp.concatenate([kfeat_grad[:tail], kfeat_grad[tail:] + back_feat], axis=0)
    value_grad, kfeat_grad = apply_reverse(
        value_grad, kfeat_grad, key_feat, value_rows, labels, summary
    )
    return (
        query_grad.reshape(rows, heads * head_dim).astype(jnp.bfloat16),
        key_grad.reshape(rows, heads * head_dim).astype(jnp.bfloat16),
        value_grad.reshape(rows, heads * head_dim).astype(jnp.bfloat16),
        feat_grad.reshape(rows, heads * feat).astype(jnp.bfloat16),
        kfeat_grad.reshape(rows, heads * feat).astype(jnp.bfloat16),
    )


def solution(mesh):
    in_specs = (
        P(("group", "seq"), None),
        P(("group", "seq"), None),
        P(("group", "seq"), None),
        P(("group", "seq"), None),
        P(("group", "seq"), None),
        P(("group", "seq"), None),
        P(("group", "seq")),
        P("group"),
    )
    out_specs = (
        P(("group", "seq"), None),
        P(("group", "seq"), None),
        P(("group", "seq"), None),
        P(("group", "seq"), None),
        P(("group", "seq"), None),
    )
    return jax.shard_map(
        per_device, mesh=mesh, in_specs=in_specs, out_specs=out_specs, check_vma=False
    )
```
